512 devices in a mesh: graph: 32 (over z, core), irreps: 16 (over y, x).
Axes of the slice: x: 4, y: 4, z: 16, core: 2. Of those that a mesh axis runs over, the one named last changes fastest.
Arguments:
- node_feats: bfloat16 [49, 128, 2048], P(None, 'irreps', 'graph'), may hold values from -8 to 8
- norm_gain: float32 [7, 128], P(None, 'irreps'), may hold values from 0.1 to 1.9
- species: int32 [2048], P('graph'), may hold values from 0 to 89
- send_list: int32 [8192], P('graph'), may hold values from 0 to 63
- edge_source: int32 [32768], P('graph'), may hold values from 0 to 319, as said below
- edge_target: int32 [32768], P('graph'), may hold values from 0 to 63
- edge_count: int32 [32], P('graph'), may hold values from 512 to 1024, as said below
- edge_length: float32 [32768], P('graph'), may hold values from 0.8 to 6
- wigner: bfloat16 [235, 32768], P(None, 'graph'), may hold values from -2.5 to 2.5
- radial_in: bfloat16 [512, 128], replicated, may hold values from -0.25 to 0.25
- species_table: bfloat16 [90, 128], replicated, may hold values from -6 to 6
- radial_out: bfloat16 [128, 896], replicated, may hold values from -0.5 to 0.5
- order_zero: bfloat16 [896, 896], replicated, may hold values from -0.1875 to 0.1875
- order_one: bfloat16 [2, 768, 768], replicated, may hold values from -0.15625 to 0.15625
- order_two: bfloat16 [2, 640, 640], replicated, may hold values from -0.15625 to 0.15625
- project_weight: bfloat16 [7, 128, 128], P(None, None, 'irreps'), may hold values from -0.5 to 0.5
Outputs:
- new_feats: bfloat16 [49, 128, 2048], P(None, 'irreps', 'graph')
The draws below stay inside these ranges and needn't reach their ends.
Inputs may be any that keep to these rules, and one draw needn't show every extreme that they name: `edge_source`: an index into the table of its edge's domain. A domain reads no slot of its own send block; from each other domain it reads only the first few slots (between 1 and 8 of them), and it reads slot 7 of some domain. `edge_count`: edge slots at or past a domain's count are padding; some domain has all 1024 live.
All inputs are finite; a program needn't handle non-finite values.
Results may differ from the reference program's by a relative error of at most 0.006.
Values may be sent and summed in bfloat16 or wider, within the bound.
No kernel may reach another device: no remote copies, remote signals or barrier semaphores. Data moves between devices by JAX's collectives and lax.ppermute only.
A program may use at most 128 MiB of HBM per device.

```python
import jax
import jax.numpy as jnp
import numpy as np
from jax import lax

CHANNELS = 128
MAX_DEGREE = 6
MAX_ORDER = 2
RADIAL_BASIS = 512
EDGE_CHANNELS = 128
ELEMENTS = 90
ATOMS_DEV = 64
EDGES_DEV = 1024
PEER_SLOTS = 8
COEFFS = 49
ROTATED = 29
WIGNER_LEN = 235
ALL_ATOMS = 2048
ALL_EDGES = 32768
ALL_SENDS = 8192
N_GRAPH = 32


def draw_node_feats(key, part):
    ramp_top = 3.0
    ramp = ramp_top ** (jnp.arange(CHANNELS, dtype=jnp.float32) / (CHANNELS - 1))
    values = jax.random.normal(key, (COEFFS, CHANNELS, ALL_ATOMS), jnp.float32)
    return jnp.clip(values * ramp[None, :, None] / jnp.sqrt(ramp_top), -8.0, 8.0).astype(jnp.bfloat16)


def draw_edge_source(key, part):
    key_list = [jax.random.fold_in(key, 100 + index) for index in range(6)]
    domains = jnp.arange(N_GRAPH, dtype=jnp.int32)
    live_slots = jax.random.randint(key_list[0], (N_GRAPH, N_GRAPH), 1, PEER_SLOTS + 1)
    shift_full = jax.random.randint(key_list[1], (N_GRAPH,), 0, N_GRAPH - 1)
    full_peer = (domains + 1 + shift_full) % N_GRAPH
    full_peer = jnp.where(domains == 0, N_GRAPH - 1, full_peer)
    live_slots = jnp.where(domains[None, :] == full_peer[:, None], PEER_SLOTS, live_slots)
    edge_ids = jnp.arange(ALL_EDGES, dtype=jnp.int32)
    owner_domain = edge_ids // EDGES_DEV
    local_pick = jax.random.randint(key_list[2], (ALL_EDGES,), 0, 3) == 0
    local_atom = jax.random.randint(key_list[3], (ALL_EDGES,), 0, ATOMS_DEV)
    peer_domain = (owner_domain + 1 + jax.random.randint(key_list[4], (ALL_EDGES,), 0, N_GRAPH - 1)) % N_GRAPH
    slot_index = jax.random.randint(key_list[5], (ALL_EDGES,), 0, 1 << 20) % live_slots[owner_domain, peer_domain]
    remote_index = ATOMS_DEV + peer_domain * PEER_SLOTS + slot_index
    chosen = jnp.where(local_pick, local_atom, remote_index)
    first_edge = edge_ids % EDGES_DEV == 0
    top_index = ATOMS_DEV + full_peer[owner_domain] * PEER_SLOTS + PEER_SLOTS - 1
    return jnp.where(first_edge, top_index, chosen).astype(jnp.int32)


def draw_edge_count(key, part):
    counts_drawn = jax.random.randint(key, (N_GRAPH,), EDGES_DEV // 2, EDGES_DEV + 1)
    busiest = jax.random.randint(jax.random.fold_in(key, 3), (), 0, N_GRAPH)
    return jnp.where(jnp.arange(N_GRAPH, dtype=jnp.int32) == busiest, EDGES_DEV, counts_drawn).astype(jnp.int32)


def with_ends(values, key, smallest, top_value):
    longest = values.shape.index(max(values.shape))
    spots = []
    for shift in (0, 1):
        where = [jax.random.randint(jax.random.fold_in(key, axis), (), 0, length) for axis, length in enumerate(values.shape)]
        where[longest] = (where[longest] + shift) % values.shape[longest]
        spots.append(tuple(where))
    return values.at[spots[0]].set(smallest).at[spots[1]].set(top_value)


def block_scale(key, shape, split, smallest, high):
    def one(dim, blocks):
        steps = jax.random.uniform(jax.random.fold_in(jax.random.fold_in(key, 6), dim), (blocks,), jnp.float32, smallest / len(split), high / len(split))
        return jnp.repeat(jnp.exp(steps), shape[dim] // blocks).reshape((-1,) + (1,) * (len(shape) - dim - 1))

    level = one(*split[0])
    for cut in split[1:]:
        level = level * one(*cut)
    return level


def bell_draw(own_key, dims, width, bound, cuts=(), kind=jnp.bfloat16):
    result = jax.random.normal(own_key, dims, jnp.float32) * width
    if len(cuts) > 0:
        result = block_scale(own_key, dims, cuts, -0.22, 0.18) * result
    return jnp.clip(result, min=-bound, max=bound).astype(kind)


def setup_inputs(seed: int = 0) -> dict:
    splits = jax.random.split(jax.random.key(seed), 17)
    return {
        "node_feats": draw_node_feats(jax.random.fold_in(splits[16], 71), 0),
        "norm_gain": jnp.clip(1.0 + 0.18 * jax.random.normal(splits[1], (MAX_DEGREE + 1, CHANNELS), jnp.float32), 0.1, 1.9),
        "species": with_ends(jax.random.randint(splits[2], (ALL_ATOMS,), 0, ELEMENTS), jax.random.fold_in(splits[2], 1), 0, ELEMENTS - 1).astype(jnp.int32),
        "send_list": with_ends(jax.random.randint(splits[3], (ALL_SENDS,), 0, ATOMS_DEV), jax.random.fold_in(splits[3], 1), 0, ATOMS_DEV - 1).astype(jnp.int32),
        "edge_source": draw_edge_source(jax.random.fold_in(splits[16], 71), 0),
        "edge_target": with_ends(jax.random.randint(splits[5], (ALL_EDGES,), 0, ATOMS_DEV), jax.random.fold_in(splits[5], 1), 0, ATOMS_DEV - 1).astype(jnp.int32),
        "edge_count": draw_edge_count(jax.random.fold_in(splits[16], 71), 0),
        "edge_length": jnp.clip(0.8 + 5.2 * jax.random.uniform(splits[7], (ALL_EDGES,), jnp.float32) ** block_scale(splits[7], (ALL_EDGES,), ((0, 32),), -0.2, 0.2), 0.8, 6.0),
        "wigner": bell_draw(splits[8], (WIGNER_LEN, ALL_EDGES), 0.4, 2.5, ((1, 32),)),
        "radial_in": bell_draw(splits[9], (RADIAL_BASIS, EDGE_CHANNELS), RADIAL_BASIS ** -0.5, 0.25),
        "species_table": bell_draw(splits[10], (ELEMENTS, EDGE_CHANNELS), 1.0, 6.0),
        "radial_out": bell_draw(splits[11], (EDGE_CHANNELS, (MAX_DEGREE + 1) * CHANNELS), EDGE_CHANNELS ** -0.5, 0.5),
        "order_zero": bell_draw(splits[12], ((MAX_DEGREE + 1) * CHANNELS, (MAX_DEGREE + 1) * CHANNELS), ((MAX_DEGREE + 1) * CHANNELS) ** -0.5, 0.1875),
        "order_one": bell_draw(splits[13], (2, MAX_DEGREE * CHANNELS, MAX_DEGREE * CHANNELS), (2 * MAX_DEGREE * CHANNELS) ** -0.5, 0.15625),
        "order_two": bell_draw(splits[14], (2, (MAX_DEGREE - 1) * CHANNELS, (MAX_DEGREE - 1) * CHANNELS), (2 * (MAX_DEGREE - 1) * CHANNELS) ** -0.5, 0.15625),
        "project_weight": bell_draw(splits[15], (MAX_DEGREE + 1, CHANNELS, CHANNELS), CHANNELS ** -0.5, 0.5, ((2, 16),)),
    }


EPSILON = 1e-06
CUTOFF = 6.0

def order_index(degree, harmonic):
    if harmonic == 0:
        return degree
    first_row = MAX_DEGREE + 1
    for level in range(1, abs(harmonic)):
        first_row = first_row + 2 * (MAX_DEGREE + 1 - level)
    if harmonic < 0:
        first_row = first_row + MAX_DEGREE + 1 - abs(harmonic)
    return first_row + degree - abs(harmonic)

def wigner_start(degree):
    running = 0
    for level in range(degree):
        running = running + (2 * min(level, MAX_ORDER) + 1) * (2 * level + 1)
    return running

def left_dot(weight, values):
    return jnp.dot(weight.T, values, preferred_element_type=jnp.float32)

def degree_sums(squares):
    return jnp.stack([lax.optimization_barrier(jnp.sum(squares[degree * degree:(degree + 1) ** 2], axis=0)) for degree in range(MAX_DEGREE + 1)])

def normalize(node_feats, norm_gain, totals):
    levels = MAX_DEGREE + 1
    degree_of = np.repeat(np.arange(levels), 2 * np.arange(levels) + 1)
    entry_counts = (2 * np.arange(levels) + 1) * CHANNELS
    inverse = 1.0 / jnp.sqrt(totals / jnp.asarray(entry_counts, jnp.float32)[:, None] + EPSILON)
    gain_rows = norm_gain[degree_of]
    scale_rows = inverse[degree_of]
    return (node_feats.astype(jnp.float32) * gain_rows[:, :, None] * scale_rows[:, None, :]).astype(jnp.bfloat16)

def rotate(source, wig_rows):
    num_edges = source.shape[2]
    pieces = [None] * ROTATED
    for degree in range(MAX_DEGREE + 1):
        reach_order = min(degree, MAX_ORDER)
        span_cols = 2 * degree + 1
        first_row = wigner_start(degree)
        blocks = wig_rows[first_row:first_row + (2 * reach_order + 1) * span_cols].astype(jnp.float32)
        blocks = blocks.reshape(2 * reach_order + 1, span_cols, num_edges)
        chosen = source[degree * degree:(degree + 1) ** 2].astype(jnp.float32)
        turned = jnp.einsum('kje,jce->kce', blocks, chosen)
        for position in range(2 * reach_order + 1):
            pieces[order_index(degree, position - reach_order)] = turned[position]
    return jnp.stack(pieces).astype(jnp.bfloat16)

def unrotate(gated, wig_rows):
    num_edges = gated.shape[2]
    pieces = []
    for degree in range(MAX_DEGREE + 1):
        reach_order = min(degree, MAX_ORDER)
        span_cols = 2 * degree + 1
        first_row = wigner_start(degree)
        blocks = wig_rows[first_row:first_row + (2 * reach_order + 1) * span_cols].astype(jnp.float32)
        blocks = blocks.reshape(2 * reach_order + 1, span_cols, num_edges)
        chosen = jnp.stack([gated[order_index(degree, position - reach_order)] for position in range(2 * reach_order + 1)]).astype(jnp.float32)
        pieces.append(jnp.einsum('kje,kce->jce', blocks, chosen))
    return jnp.concatenate(pieces, axis=0)

def radial_weights(lengths, kind_ids, radial_in, species_table, radial_out):
    basis_count = radial_in.shape[0]
    spacing = CUTOFF / (basis_count - 1)
    centers = jnp.arange(basis_count, dtype=jnp.float32) * spacing
    basis_rows = jnp.exp(-0.5 * jnp.square((lengths[None, :] - centers[:, None]) / (2.0 * spacing))).astype(jnp.bfloat16)
    onehot = (kind_ids[None, :] == jnp.arange(species_table.shape[0], dtype=jnp.int32)[:, None]).astype(jnp.bfloat16)
    hidden = jax.nn.silu(left_dot(radial_in, basis_rows) + left_dot(species_table, onehot)).astype(jnp.bfloat16)
    return left_dot(radial_out, hidden)

def convolve(rotated, radial, order_zero, order_one, order_two):
    levels = MAX_DEGREE + 1
    channel_count = rotated.shape[1]
    num_edges = rotated.shape[2]
    lowest = (rotated[:levels].astype(jnp.float32).reshape(levels * channel_count, num_edges) * radial).astype(jnp.bfloat16)
    outputs = [left_dot(order_zero, lowest).reshape(levels, channel_count, num_edges)]
    first_row = levels
    for harmonic, weight in ((1, order_one), (2, order_two)):
        span_rows = levels - harmonic
        plus_rows = rotated[first_row:first_row + span_rows].reshape(span_rows * channel_count, num_edges)
        minus_rows = rotated[first_row + span_rows:first_row + 2 * span_rows].reshape(span_rows * channel_count, num_edges)
        joined = jnp.concatenate([plus_rows, minus_rows], axis=1)
        real_part = left_dot(weight[0], joined)
        cross_part = left_dot(weight[1], joined)
        outputs.append((real_part[:, :num_edges] - cross_part[:, num_edges:]).reshape(span_rows, channel_count, num_edges))
        outputs.append((cross_part[:, :num_edges] + real_part[:, num_edges:]).reshape(span_rows, channel_count, num_edges))
        first_row = first_row + 2 * span_rows
    mixed = jnp.concatenate(outputs, axis=0)
    scalar = mixed[0]
    return jnp.concatenate([jax.nn.silu(scalar)[None], mixed[1:] * jax.nn.sigmoid(scalar)[None]], axis=0).astype(jnp.bfloat16)

def reference(node_feats, norm_gain, species, send_list, edge_source, edge_target, edge_count, edge_length, wigner, radial_in, species_table, radial_out, order_zero, order_one, order_two, project_weight):
    levels = MAX_DEGREE + 1
    squares = lax.optimization_barrier(jnp.sum(jnp.square(node_feats.astype(jnp.float32)), axis=1))
    totals = degree_sums(squares)
    normed = normalize(node_feats, norm_gain, totals)
    senders = send_list.reshape(N_GRAPH, N_GRAPH, PEER_SLOTS)
    domains = jnp.arange(N_GRAPH, dtype=jnp.int32)
    remote = jnp.transpose(senders, (1, 0, 2)) + (domains * ATOMS_DEV)[None, :, None]
    local = domains[:, None] * ATOMS_DEV + jnp.arange(ATOMS_DEV, dtype=jnp.int32)[None, :]
    lookup = jnp.concatenate([local, remote.reshape(N_GRAPH, N_GRAPH * PEER_SLOTS)], axis=1).astype(jnp.int32)
    per_domain = (lookup, edge_source.reshape(N_GRAPH, EDGES_DEV), edge_target.reshape(N_GRAPH, EDGES_DEV), edge_count, edge_length.reshape(N_GRAPH, EDGES_DEV), jnp.moveaxis(wigner.reshape(WIGNER_LEN, N_GRAPH, EDGES_DEV), 1, 0), species.reshape(N_GRAPH, ATOMS_DEV))

    def one_domain(items):
        lookup_row, sources, targets, count_one, lengths, wig_rows, kinds_domain = items
        gathered = normed[:, :, lookup_row[sources]]
        rotated = rotate(gathered, wig_rows)
        radial = radial_weights(lengths, kinds_domain[targets], radial_in, species_table, radial_out)
        gated = convolve(rotated, radial, order_zero, order_one, order_two)
        messages = unrotate(gated, wig_rows)
        edge_weight = jnp.where(jnp.arange(EDGES_DEV, dtype=jnp.int32) < count_one, 0.25, 0.0).astype(jnp.float32)
        summed = jnp.zeros((COEFFS, CHANNELS, ATOMS_DEV), jnp.float32).at[:, :, targets].add(messages * edge_weight[None, None, :])
        return summed.astype(jnp.bfloat16)
    combined = lax.map(one_domain, per_domain)
    combined = jnp.transpose(combined, (1, 2, 0, 3)).reshape(COEFFS, CHANNELS, ALL_ATOMS)
    updates = []
    for degree in range(levels):
        updates.append(jnp.einsum('io,jia->joa', project_weight[degree].astype(jnp.float32), combined[degree * degree:(degree + 1) ** 2].astype(jnp.float32)))
    projected = jnp.concatenate(updates, axis=0)
    return (node_feats.astype(jnp.float32) + projected).astype(jnp.bfloat16)
```

```python
import jax
import jax.numpy as jnp
import numpy as np
from jax import lax
from jax.sharding import PartitionSpec as P

CHANNELS = 128
MAX_DEGREE = 6
MAX_ORDER = 2
ROTATED = 29


EPSILON = 1e-06
CUTOFF = 6.0


def order_index(degree, harmonic):
    if harmonic == 0:
        return degree
    first_row = MAX_DEGREE + 1
    for level in range(1, abs(harmonic)):
        first_row = first_row + 2 * (MAX_DEGREE + 1 - level)
    if harmonic < 0:
        first_row = first_row + MAX_DEGREE + 1 - abs(harmonic)
    return first_row + degree - abs(harmonic)


def wigner_start(degree):
    running = 0
    for level in range(degree):
        running = running + (2 * min(level, MAX_ORDER) + 1) * (2 * level + 1)
    return running


def left_dot(weight, values):
    return lax.dot_general(
        weight, values, (((0,), (0,)), ((), ())), preferred_element_type=jnp.float32
    )


def degree_sums(squares):
    return jnp.stack(
        [
            jnp.sum(squares[degree * degree : (degree + 1) ** 2], axis=0)
            for degree in range(MAX_DEGREE + 1)
        ]
    )


def normalize(node_feats, norm_gain, totals):
    levels = MAX_DEGREE + 1
    degree_of = np.repeat(np.arange(levels), 2 * np.arange(levels) + 1)
    entry_counts = (2 * np.arange(levels) + 1) * CHANNELS
    inverse = 1.0 / jnp.sqrt(totals / jnp.asarray(entry_counts, jnp.float32)[:, None] + EPSILON)
    gain_rows = norm_gain[degree_of]
    scale_rows = inverse[degree_of]
    return (node_feats.astype(jnp.float32) * gain_rows[:, :, None] * scale_rows[:, None, :]).astype(
        jnp.bfloat16
    )


def normalize_rows(values, gain_full, totals):
    levels = MAX_DEGREE + 1
    degree_of = np.repeat(np.arange(levels), 2 * np.arange(levels) + 1)
    entry_counts = (2 * np.arange(levels) + 1) * CHANNELS
    inverse = 1.0 / jnp.sqrt(totals / jnp.asarray(entry_counts, jnp.float32)[:, None] + EPSILON)
    gain_rows = gain_full[degree_of]
    scale_rows = inverse[degree_of]
    return (values * gain_rows[:, :, None] * scale_rows[:, None, :]).astype(jnp.bfloat16)


def rotate(source, wig_rows):
    pieces = [None] * ROTATED
    for degree in range(MAX_DEGREE + 1):
        reach_order = min(degree, MAX_ORDER)
        span_cols = 2 * degree + 1
        first_row = wigner_start(degree)
        for position in range(2 * reach_order + 1):
            total = None
            for column in range(span_cols):
                term = wig_rows[first_row + position * span_cols + column][None, :] * source[degree * degree + column]
                total = term if total is None else total + term
            pieces[order_index(degree, position - reach_order)] = total
    return jnp.stack(pieces).astype(jnp.bfloat16)


def unrotate(gated, wig_rows):
    pieces = []
    for degree in range(MAX_DEGREE + 1):
        reach_order = min(degree, MAX_ORDER)
        span_cols = 2 * degree + 1
        first_row = wigner_start(degree)
        for column in range(span_cols):
            total = None
            for position in range(2 * reach_order + 1):
                term = wig_rows[first_row + position * span_cols + column][None, :] * gated[
                    order_index(degree, position - reach_order)
                ]
                total = term if total is None else total + term
            pieces.append(total)
    return jnp.stack(pieces)


def radial_weights(lengths, kind_ids, radial_in, species_table, radial_out):
    basis_count = radial_in.shape[0]
    spacing = CUTOFF / (basis_count - 1)
    centers = jnp.arange(basis_count, dtype=jnp.float32) * spacing
    basis_rows = jnp.exp(
        -0.5 * jnp.square((lengths[None, :] - centers[:, None]) / (2.0 * spacing))
    ).astype(jnp.bfloat16)
    onehot = (
        kind_ids[None, :] == jnp.arange(species_table.shape[0], dtype=jnp.int32)[:, None]
    ).astype(jnp.bfloat16)
    hidden = jax.nn.silu(left_dot(radial_in, basis_rows) + left_dot(species_table, onehot)).astype(
        jnp.bfloat16
    )
    return left_dot(radial_out, hidden)


def convolve(rotated, radial, order_zero, order_one, order_two):
    levels = MAX_DEGREE + 1
    channel_count = rotated.shape[1]
    num_edges = rotated.shape[2]
    lowest = (
        rotated[:levels].astype(jnp.float32).reshape(levels * channel_count, num_edges) * radial
    ).astype(jnp.bfloat16)
    outputs = [left_dot(order_zero, lowest).reshape(levels, channel_count, num_edges)]
    first_row = levels
    for harmonic, weight in ((1, order_one), (2, order_two)):
        span_rows = levels - harmonic
        plus_rows = rotated[first_row : first_row + span_rows].reshape(
            span_rows * channel_count, num_edges
        )
        minus_rows = rotated[first_row + span_rows : first_row + 2 * span_rows].reshape(
            span_rows * channel_count, num_edges
        )
        joined = jnp.concatenate([plus_rows, minus_rows], axis=1)
        real_part = left_dot(weight[0], joined)
        cross_part = left_dot(weight[1], joined)
        outputs.append(
            (real_part[:, :num_edges] - cross_part[:, num_edges:]).reshape(
                span_rows, channel_count, num_edges
            )
        )
        outputs.append(
            (cross_part[:, :num_edges] + real_part[:, num_edges:]).reshape(
                span_rows, channel_count, num_edges
            )
        )
        first_row = first_row + 2 * span_rows
    mixed = jnp.concatenate(outputs, axis=0)
    scalar = mixed[0]
    return jnp.concatenate(
        [jax.nn.silu(scalar)[None], mixed[1:] * jax.nn.sigmoid(scalar)[None]], axis=0
    ).astype(jnp.bfloat16)


def split_dot(values, weight):
    upper_part = values.astype(jnp.bfloat16)
    lower_part = (values - upper_part.astype(jnp.float32)).astype(jnp.bfloat16)
    return jnp.dot(upper_part, weight, preferred_element_type=jnp.float32) + jnp.dot(
        lower_part, weight, preferred_element_type=jnp.float32
    )


def body(
    node_feats,
    norm_gain,
    species,
    send_list,
    edge_source,
    edge_target,
    edge_count,
    edge_length,
    wigner,
    radial_in,
    species_table,
    radial_out,
    order_zero,
    order_one,
    order_two,
    project_weight,
):
    levels = MAX_DEGREE + 1
    owners = lax.axis_size("irreps")
    quarter = lax.axis_index("irreps")
    coeffs, span_chan, atom_count = node_feats.shape
    per_owner = edge_source.shape[0] // owners
    first_edge = quarter * per_owner

    outgoing = node_feats[:, :, send_list]
    arrived = lax.all_to_all(outgoing, "graph", split_axis=2, concat_axis=2, tiled=True)

    packed = jnp.concatenate(
        [norm_gain, project_weight.astype(jnp.float32).reshape(levels, -1)], axis=1
    )
    spread = lax.all_to_all(
        jnp.broadcast_to(packed[None], (owners,) + packed.shape), "irreps", 0, 0, tiled=True
    )
    gain_full = jnp.transpose(spread[:, :, :span_chan], (1, 0, 2)).reshape(levels, owners * span_chan)
    weight_full = jnp.transpose(
        spread[:, :, span_chan:].reshape(owners, levels, CHANNELS, span_chan), (1, 2, 0, 3)
    ).reshape(levels, CHANNELS, owners * span_chan)

    lookup = jnp.concatenate([node_feats, arrived], axis=2)
    source = lax.all_to_all(
        lookup[:, :, edge_source], "irreps", split_axis=2, concat_axis=1, tiled=True
    )
    source = source.astype(jnp.float32)
    squares = jnp.sum(jnp.square(source), axis=1)
    totals = degree_sums(squares)
    normed = normalize_rows(source, gain_full, totals)

    wig_mine = lax.dynamic_slice_in_dim(wigner, first_edge, per_owner, 1).astype(jnp.float32)
    rotated = rotate(normed.astype(jnp.float32), wig_mine)
    targets_mine = lax.dynamic_slice_in_dim(edge_target, first_edge, per_owner)
    lengths_mine = lax.dynamic_slice_in_dim(edge_length, first_edge, per_owner)
    radial = radial_weights(
        lengths_mine, species[targets_mine], radial_in, species_table, radial_out
    )
    gated = convolve(rotated, radial, order_zero, order_one, order_two)
    messages = unrotate(gated.astype(jnp.float32), wig_mine)
    edge_weight = jnp.where(
        first_edge + jnp.arange(per_owner, dtype=jnp.int32) < edge_count[0], 0.25, 0.0
    ).astype(jnp.float32)
    onehot = jnp.where(
        targets_mine[:, None] == jnp.arange(atom_count, dtype=jnp.int32)[None, :],
        edge_weight[:, None],
        0.0,
    ).astype(jnp.bfloat16)
    summed = split_dot(messages.reshape(-1, per_owner), onehot).reshape(coeffs, CHANNELS, atom_count)
    upper_part = summed.astype(jnp.bfloat16)
    lower_part = (summed - upper_part.astype(jnp.float32)).astype(jnp.bfloat16)
    updates = []
    for degree in range(levels):
        rows = slice(degree * degree, (degree + 1) ** 2)
        weight = weight_full[degree].astype(jnp.bfloat16)
        updates.append(
            jnp.einsum("io,jia->oja", weight, upper_part[rows], preferred_element_type=jnp.float32)
            + jnp.einsum("io,jia->oja", weight, lower_part[rows], preferred_element_type=jnp.float32)
        )
    projected = jnp.concatenate(updates, axis=1)
    returned = lax.all_to_all(
        projected.reshape(owners, span_chan, coeffs, atom_count), "irreps", 0, 0, tiled=True
    )
    total = jnp.transpose(jnp.sum(returned, axis=0), (1, 0, 2))
    return (node_feats.astype(jnp.float32) + total).astype(jnp.bfloat16)


def solution(mesh):
    return jax.shard_map(
        body,
        mesh=mesh,
        in_specs=(
            P(None, "irreps", "graph"),
            P(None, "irreps"),
            P("graph"),
            P("graph"),
            P("graph"),
            P("graph"),
            P("graph"),
            P("graph"),
            P(None, "graph"),
            P(),
            P(),
            P(),
            P(),
            P(),
            P(),
            P(None, None, "irreps"),
        ),
        out_specs=P(None, "irreps", "graph"),
        check_vma=False,
    )
```

```python
import jax
import jax.numpy as jnp
import numpy as np
from jax import lax
from jax.sharding import PartitionSpec as P
from jax.experimental import pallas as pl
from jax.experimental.pallas import tpu as pltpu

CHANNELS = 128
MAX_DEGREE = 6
MAX_ORDER = 2
ROTATED = 29


EPSILON = 1e-06
CUTOFF = 6.0


def order_index(degree, harmonic):
    if harmonic == 0:
        return degree
    first_row = MAX_DEGREE + 1
    for level in range(1, abs(harmonic)):
        first_row = first_row + 2 * (MAX_DEGREE + 1 - level)
    if harmonic < 0:
        first_row = first_row + MAX_DEGREE + 1 - abs(harmonic)
    return first_row + degree - abs(harmonic)


def wigner_start(degree):
    running = 0
    for level in range(degree):
        running = running + (2 * min(level, MAX_ORDER) + 1) * (2 * level + 1)
    return running


def left_dot(weight, values):
    return lax.dot_general(
        weight, values, (((0,), (0,)), ((), ())), preferred_element_type=jnp.float32
    )


def degree_sums(squares):
    return jnp.stack(
        [
            jnp.sum(squares[degree * degree : (degree + 1) ** 2], axis=0)
            for degree in range(MAX_DEGREE + 1)
        ]
    )


def normalize(node_feats, norm_gain, totals):
    levels = MAX_DEGREE + 1
    degree_of = np.repeat(np.arange(levels), 2 * np.arange(levels) + 1)
    entry_counts = (2 * np.arange(levels) + 1) * CHANNELS
    inverse = 1.0 / jnp.sqrt(totals / jnp.asarray(entry_counts, jnp.float32)[:, None] + EPSILON)
    gain_rows = norm_gain[degree_of]
    scale_rows = inverse[degree_of]
    return (node_feats.astype(jnp.float32) * gain_rows[:, :, None] * scale_rows[:, None, :]).astype(
        jnp.bfloat16
    )


def normalize_rows(values, gain_full, totals):
    levels = MAX_DEGREE + 1
    degree_of = np.repeat(np.arange(levels), 2 * np.arange(levels) + 1)
    entry_counts = (2 * np.arange(levels) + 1) * CHANNELS
    inverse = 1.0 / jnp.sqrt(totals / jnp.asarray(entry_counts, jnp.float32)[:, None] + EPSILON)
    gain_rows = gain_full[degree_of]
    scale_rows = inverse[degree_of]
    return (values * gain_rows[:, :, None] * scale_rows[:, None, :]).astype(jnp.bfloat16)


def rotate(source, wig_rows):
    pieces = [None] * ROTATED
    for degree in range(MAX_DEGREE + 1):
        reach_order = min(degree, MAX_ORDER)
        span_cols = 2 * degree + 1
        first_row = wigner_start(degree)
        for position in range(2 * reach_order + 1):
            total = None
            for column in range(span_cols):
                term = wig_rows[first_row + position * span_cols + column][None, :] * source[degree * degree + column]
                total = term if total is None else total + term
            pieces[order_index(degree, position - reach_order)] = total
    return jnp.stack(pieces).astype(jnp.bfloat16)


def unrotate(gated, wig_rows):
    pieces = []
    for degree in range(MAX_DEGREE + 1):
        reach_order = min(degree, MAX_ORDER)
        span_cols = 2 * degree + 1
        first_row = wigner_start(degree)
        for column in range(span_cols):
            total = None
            for position in range(2 * reach_order + 1):
                term = wig_rows[first_row + position * span_cols + column][None, :] * gated[
                    order_index(degree, position - reach_order)
                ]
                total = term if total is None else total + term
            pieces.append(total)
    return jnp.stack(pieces)


def radial_weights(lengths, kind_ids, radial_in, species_table, radial_out):
    basis_count = radial_in.shape[0]
    spacing = CUTOFF / (basis_count - 1)
    centers = jnp.arange(basis_count, dtype=jnp.float32) * spacing
    basis_rows = jnp.exp(
        -0.5 * jnp.square((lengths[None, :] - centers[:, None]) / (2.0 * spacing))
    ).astype(jnp.bfloat16)
    onehot = (
        kind_ids[None, :] == jnp.arange(species_table.shape[0], dtype=jnp.int32)[:, None]
    ).astype(jnp.bfloat16)
    hidden = jax.nn.silu(left_dot(radial_in, basis_rows) + left_dot(species_table, onehot)).astype(
        jnp.bfloat16
    )
    return left_dot(radial_out, hidden)


def convolve(rotated, radial, order_zero, order_one, order_two):
    levels = MAX_DEGREE + 1
    channel_count = rotated.shape[1]
    num_edges = rotated.shape[2]
    lowest = (
        rotated[:levels].astype(jnp.float32).reshape(levels * channel_count, num_edges) * radial
    ).astype(jnp.bfloat16)
    outputs = [left_dot(order_zero, lowest).reshape(levels, channel_count, num_edges)]
    first_row = levels
    for harmonic, weight in ((1, order_one), (2, order_two)):
        span_rows = levels - harmonic
        plus_rows = rotated[first_row : first_row + span_rows].reshape(
            span_rows * channel_count, num_edges
        )
        minus_rows = rotated[first_row + span_rows : first_row + 2 * span_rows].reshape(
            span_rows * channel_count, num_edges
        )
        joined = jnp.concatenate([plus_rows, minus_rows], axis=1)
        real_part = left_dot(weight[0], joined)
        cross_part = left_dot(weight[1], joined)
        outputs.append(
            (real_part[:, :num_edges] - cross_part[:, num_edges:]).reshape(
                span_rows, channel_count, num_edges
            )
        )
        outputs.append(
            (cross_part[:, :num_edges] + real_part[:, num_edges:]).reshape(
                span_rows, channel_count, num_edges
            )
        )
        first_row = first_row + 2 * span_rows
    mixed = jnp.concatenate(outputs, axis=0)
    scalar = mixed[0]
    return jnp.concatenate(
        [jax.nn.silu(scalar)[None], mixed[1:] * jax.nn.sigmoid(scalar)[None]], axis=0
    ).astype(jnp.bfloat16)


def conv_kernel(
    src_ref, gain_ref, wig_ref, length_ref, kind_ref, basis_in_ref, kind_table_ref, radial_out_ref,
    zero_ref, one_ref, two_ref, onehot_ref, proj_ref, out_ref,
):
    levels = MAX_DEGREE + 1
    channel_count = src_ref.shape[1]
    num_edges = src_ref.shape[2]
    basis_count = basis_in_ref.shape[1]
    wig = wig_ref[...].astype(jnp.float32)
    gain = gain_ref[...]

    rows = [src_ref[j].astype(jnp.float32) for j in range(src_ref.shape[0])]
    normed = [None] * len(rows)
    for degree in range(levels):
        span = range(degree * degree, (degree + 1) ** 2)
        total = None
        for j in span:
            part = jnp.sum(rows[j] * rows[j], axis=0, keepdims=True)
            total = part if total is None else total + part
        inverse = 1.0 / jnp.sqrt(total / float((2 * degree + 1) * CHANNELS) + EPSILON)
        scale = gain[:, degree : degree + 1]
        for j in span:
            normed[j] = (rows[j] * scale * inverse).astype(jnp.bfloat16).astype(jnp.float32)

    rotated = [None] * ROTATED
    for degree in range(levels):
        reach_order = min(degree, MAX_ORDER)
        span_cols = 2 * degree + 1
        first_row = wigner_start(degree)
        for position in range(2 * reach_order + 1):
            total = None
            for column in range(span_cols):
                row = first_row + position * span_cols + column
                term = wig[row : row + 1, :] * normed[degree * degree + column]
                total = term if total is None else total + term
            rotated[order_index(degree, position - reach_order)] = total.astype(jnp.bfloat16)

    spacing = CUTOFF / (basis_count - 1)
    centers = lax.broadcasted_iota(jnp.int32, (basis_count, num_edges), 0).astype(jnp.float32) * spacing
    basis_rows = jnp.exp(
        -0.5 * jnp.square((length_ref[...] - centers) / (2.0 * spacing))
    ).astype(jnp.bfloat16)
    hidden = jnp.dot(basis_in_ref[...], basis_rows, preferred_element_type=jnp.float32) + jnp.dot(
        kind_table_ref[...], kind_ref[...], preferred_element_type=jnp.float32
    )
    hidden = (hidden * jax.nn.sigmoid(hidden)).astype(jnp.bfloat16)
    radial = jnp.dot(radial_out_ref[...], hidden, preferred_element_type=jnp.float32)

    lowest = jnp.concatenate(
        [
            (rotated[degree].astype(jnp.float32) * radial[degree * channel_count : (degree + 1) * channel_count]).astype(
                jnp.bfloat16
            )
            for degree in range(levels)
        ],
        axis=0,
    )
    mixed0 = jnp.dot(zero_ref[...], lowest, preferred_element_type=jnp.float32)
    mixed = [mixed0[degree * channel_count : (degree + 1) * channel_count] for degree in range(levels)]
    first_row = levels
    for harmonic, weight_ref in ((1, one_ref), (2, two_ref)):
        span_rows = levels - harmonic
        plus_rows = jnp.concatenate(rotated[first_row : first_row + span_rows], axis=0)
        minus_rows = jnp.concatenate(rotated[first_row + span_rows : first_row + 2 * span_rows], axis=0)
        real_plus = jnp.dot(weight_ref[0], plus_rows, preferred_element_type=jnp.float32)
        real_minus = jnp.dot(weight_ref[0], minus_rows, preferred_element_type=jnp.float32)
        cross_plus = jnp.dot(weight_ref[1], plus_rows, preferred_element_type=jnp.float32)
        cross_minus = jnp.dot(weight_ref[1], minus_rows, preferred_element_type=jnp.float32)
        new_plus = real_plus - cross_minus
        new_minus = cross_plus + real_minus
        mixed += [new_plus[k * channel_count : (k + 1) * channel_count] for k in range(span_rows)]
        mixed += [new_minus[k * channel_count : (k + 1) * channel_count] for k in range(span_rows)]
        first_row = first_row + 2 * span_rows

    scalar = mixed[0]
    gate = jax.nn.sigmoid(scalar)
    gated = [(scalar * gate).astype(jnp.bfloat16).astype(jnp.float32)] + [
        (piece * gate).astype(jnp.bfloat16).astype(jnp.float32) for piece in mixed[1:]
    ]

    messages = []
    for degree in range(levels):
        reach_order = min(degree, MAX_ORDER)
        span_cols = 2 * degree + 1
        first_row = wigner_start(degree)
        for column in range(span_cols):
            total = None
            for position in range(2 * reach_order + 1):
                row = first_row + position * span_cols + column
                term = wig[row : row + 1, :] * gated[order_index(degree, position - reach_order)]
                total = term if total is None else total + term
            messages.append(total)
    stacked = jnp.concatenate(messages, axis=0)
    upper_part = stacked.astype(jnp.bfloat16)
    lower_part = (stacked - upper_part.astype(jnp.float32)).astype(jnp.bfloat16)
    onehot = onehot_ref[...]
    summed = jnp.dot(upper_part, onehot, preferred_element_type=jnp.float32) + jnp.dot(
        lower_part, onehot, preferred_element_type=jnp.float32
    )
    for degree in range(levels):
        weight = proj_ref[degree]
        for j in range(degree * degree, (degree + 1) ** 2):
            piece = summed[j * channel_count : (j + 1) * channel_count]
            high = piece.astype(jnp.bfloat16)
            low = (piece - high.astype(jnp.float32)).astype(jnp.bfloat16)
            out_ref[j] = jnp.dot(weight, high, preferred_element_type=jnp.float32) + jnp.dot(
                weight, low, preferred_element_type=jnp.float32
            )


def convolve_edges(source, gain_cols, wig_mine, lengths, kind_onehot, radial_in, species_table, radial_out,
                   order_zero, order_one, order_two, onehot, proj_t):
    coeffs, channel_count, num_edges = source.shape
    atom_count = onehot.shape[1]
    operands = (
        source,
        gain_cols,
        wig_mine,
        lengths[None, :],
        kind_onehot,
        radial_in.T,
        species_table.T,
        radial_out.T,
        order_zero.T,
        jnp.transpose(order_one, (0, 2, 1)),
        jnp.transpose(order_two, (0, 2, 1)),
        onehot,
        proj_t,
    )
    flops = 2 * num_edges * (order_zero.size + 2 * order_one.size + 2 * order_two.size + radial_out.size + radial_in.size)
    return pl.pallas_call(
        conv_kernel,
        out_shape=jax.ShapeDtypeStruct((coeffs, channel_count, atom_count), jnp.float32),
        in_specs=[pl.BlockSpec(memory_space=pltpu.VMEM)] * len(operands),
        out_specs=pl.BlockSpec(memory_space=pltpu.VMEM),
        cost_estimate=pl.CostEstimate(
            flops=flops,
            transcendentals=num_edges * (radial_in.shape[0] + 2 * channel_count),
            bytes_accessed=sum(int(x.size) * x.dtype.itemsize for x in operands) + coeffs * channel_count * atom_count * 4,
        ),
    )(*operands)


def split_dot(values, weight):
    upper_part = values.astype(jnp.bfloat16)
    lower_part = (values - upper_part.astype(jnp.float32)).astype(jnp.bfloat16)
    return jnp.dot(upper_part, weight, preferred_element_type=jnp.float32) + jnp.dot(
        lower_part, weight, preferred_element_type=jnp.float32
    )


def body(
    node_feats,
    norm_gain,
    species,
    send_list,
    edge_source,
    edge_target,
    edge_count,
    edge_length,
    wigner,
    radial_in,
    species_table,
    radial_out,
    order_zero,
    order_one,
    order_two,
    project_weight,
):
    levels = MAX_DEGREE + 1
    owners = lax.axis_size("irreps")
    quarter = lax.axis_index("irreps")
    coeffs, span_chan, atom_count = node_feats.shape
    per_owner = edge_source.shape[0] // owners
    first_edge = quarter * per_owner

    outgoing = node_feats[:, :, send_list]
    arrived = lax.all_to_all(outgoing, "graph", split_axis=2, concat_axis=2, tiled=True)

    packed = jnp.concatenate(
        [norm_gain, project_weight.astype(jnp.float32).reshape(levels, -1)], axis=1
    )
    spread = lax.all_to_all(
        jnp.broadcast_to(packed[None], (owners,) + packed.shape), "irreps", 0, 0, tiled=True
    )
    gain_full = jnp.transpose(spread[:, :, :span_chan], (1, 0, 2)).reshape(levels, owners * span_chan)
    weight_full = jnp.transpose(
        spread[:, :, span_chan:].reshape(owners, levels, CHANNELS, span_chan), (1, 2, 0, 3)
    ).reshape(levels, CHANNELS, owners * span_chan)

    lookup = jnp.concatenate([node_feats, arrived], axis=2)
    source = lax.all_to_all(
        lookup[:, :, edge_source], "irreps", split_axis=2, concat_axis=1, tiled=True
    )
    wig_mine = lax.dynamic_slice_in_dim(wigner, first_edge, per_owner, 1)
    targets_mine = lax.dynamic_slice_in_dim(edge_target, first_edge, per_owner)
    lengths_mine = lax.dynamic_slice_in_dim(edge_length, first_edge, per_owner)
    kinds = species[targets_mine]
    kind_onehot = (
        kinds[None, :] == jnp.arange(species_table.shape[0], dtype=jnp.int32)[:, None]
    ).astype(jnp.bfloat16)
    edge_weight = jnp.where(
        first_edge + jnp.arange(per_owner, dtype=jnp.int32) < edge_count[0], 0.25, 0.0
    ).astype(jnp.float32)
    onehot = jnp.where(
        targets_mine[:, None] == jnp.arange(atom_count, dtype=jnp.int32)[None, :],
        edge_weight[:, None],
        0.0,
    ).astype(jnp.bfloat16)
    proj_t = jnp.transpose(weight_full, (0, 2, 1)).astype(jnp.bfloat16)
    projected = convolve_edges(
        source, gain_full.T, wig_mine, lengths_mine, kind_onehot, radial_in, species_table, radial_out,
        order_zero, order_one, order_two, onehot, proj_t,
    )
    projected = jnp.transpose(projected, (1, 0, 2))
    returned = lax.all_to_all(
        projected.reshape(owners, span_chan, coeffs, atom_count), "irreps", 0, 0, tiled=True
    )
    total = jnp.transpose(jnp.sum(returned, axis=0), (1, 0, 2))
    return (node_feats.astype(jnp.float32) + total).astype(jnp.bfloat16)


def solution(mesh):
    return jax.shard_map(
        body,
        mesh=mesh,
        in_specs=(
            P(None, "irreps", "graph"),
            P(None, "irreps"),
            P("graph"),
            P("graph"),
            P("graph"),
            P("graph"),
            P("graph"),
            P("graph"),
            P(None, "graph"),
            P(),
            P(),
            P(),
            P(),
            P(),
            P(),
            P(None, None, "irreps"),
        ),
        out_specs=P(None, "irreps", "graph"),
        check_vma=False,
    )
```

```python
import jax
import jax.numpy as jnp
import numpy as np
from jax import lax
from jax.sharding import PartitionSpec as P
from jax.experimental import pallas as pl
from jax.experimental.pallas import tpu as pltpu

CHANNELS = 128
MAX_DEGREE = 6
MAX_ORDER = 2
ROTATED = 29
COEFFS = 49


EPSILON = 1e-06
CUTOFF = 6.0


def order_index(degree, harmonic):
    if harmonic == 0:
        return degree
    first_row = MAX_DEGREE + 1
    for level in range(1, abs(harmonic)):
        first_row = first_row + 2 * (MAX_DEGREE + 1 - level)
    if harmonic < 0:
        first_row = first_row + MAX_DEGREE + 1 - abs(harmonic)
    return first_row + degree - abs(harmonic)


def wigner_start(degree):
    running = 0
    for level in range(degree):
        running = running + (2 * min(level, MAX_ORDER) + 1) * (2 * level + 1)
    return running


def left_dot(weight, values):
    return lax.dot_general(
        weight, values, (((0,), (0,)), ((), ())), preferred_element_type=jnp.float32
    )


def degree_sums(squares):
    return jnp.stack(
        [
            jnp.sum(squares[degree * degree : (degree + 1) ** 2], axis=0)
            for degree in range(MAX_DEGREE + 1)
        ]
    )


def normalize(node_feats, norm_gain, totals):
    levels = MAX_DEGREE + 1
    degree_of = np.repeat(np.arange(levels), 2 * np.arange(levels) + 1)
    entry_counts = (2 * np.arange(levels) + 1) * CHANNELS
    inverse = 1.0 / jnp.sqrt(totals / jnp.asarray(entry_counts, jnp.float32)[:, None] + EPSILON)
    gain_rows = norm_gain[degree_of]
    scale_rows = inverse[degree_of]
    return (node_feats.astype(jnp.float32) * gain_rows[:, :, None] * scale_rows[:, None, :]).astype(
        jnp.bfloat16
    )


def normalize_rows(values, gain_full, totals):
    levels = MAX_DEGREE + 1
    degree_of = np.repeat(np.arange(levels), 2 * np.arange(levels) + 1)
    entry_counts = (2 * np.arange(levels) + 1) * CHANNELS
    inverse = 1.0 / jnp.sqrt(totals / jnp.asarray(entry_counts, jnp.float32)[:, None] + EPSILON)
    gain_rows = gain_full[degree_of]
    scale_rows = inverse[degree_of]
    return (values * gain_rows[:, :, None] * scale_rows[:, None, :]).astype(jnp.bfloat16)


def rotate(source, wig_rows):
    pieces = [None] * ROTATED
    for degree in range(MAX_DEGREE + 1):
        reach_order = min(degree, MAX_ORDER)
        span_cols = 2 * degree + 1
        first_row = wigner_start(degree)
        for position in range(2 * reach_order + 1):
            total = None
            for column in range(span_cols):
                term = wig_rows[first_row + position * span_cols + column][None, :] * source[degree * degree + column]
                total = term if total is None else total + term
            pieces[order_index(degree, position - reach_order)] = total
    return jnp.stack(pieces).astype(jnp.bfloat16)


def unrotate(gated, wig_rows):
    pieces = []
    for degree in range(MAX_DEGREE + 1):
        reach_order = min(degree, MAX_ORDER)
        span_cols = 2 * degree + 1
        first_row = wigner_start(degree)
        for column in range(span_cols):
            total = None
            for position in range(2 * reach_order + 1):
                term = wig_rows[first_row + position * span_cols + column][None, :] * gated[
                    order_index(degree, position - reach_order)
                ]
                total = term if total is None else total + term
            pieces.append(total)
    return jnp.stack(pieces)


def radial_weights(lengths, kind_ids, radial_in, species_table, radial_out):
    basis_count = radial_in.shape[0]
    spacing = CUTOFF / (basis_count - 1)
    centers = jnp.arange(basis_count, dtype=jnp.float32) * spacing
    basis_rows = jnp.exp(
        -0.5 * jnp.square((lengths[None, :] - centers[:, None]) / (2.0 * spacing))
    ).astype(jnp.bfloat16)
    onehot = (
        kind_ids[None, :] == jnp.arange(species_table.shape[0], dtype=jnp.int32)[:, None]
    ).astype(jnp.bfloat16)
    hidden = jax.nn.silu(left_dot(radial_in, basis_rows) + left_dot(species_table, onehot)).astype(
        jnp.bfloat16
    )
    return left_dot(radial_out, hidden)


def convolve(rotated, radial, order_zero, order_one, order_two):
    levels = MAX_DEGREE + 1
    channel_count = rotated.shape[1]
    num_edges = rotated.shape[2]
    lowest = (
        rotated[:levels].astype(jnp.float32).reshape(levels * channel_count, num_edges) * radial
    ).astype(jnp.bfloat16)
    outputs = [left_dot(order_zero, lowest).reshape(levels, channel_count, num_edges)]
    first_row = levels
    for harmonic, weight in ((1, order_one), (2, order_two)):
        span_rows = levels - harmonic
        plus_rows = rotated[first_row : first_row + span_rows].reshape(
            span_rows * channel_count, num_edges
        )
        minus_rows = rotated[first_row + span_rows : first_row + 2 * span_rows].reshape(
            span_rows * channel_count, num_edges
        )
        joined = jnp.concatenate([plus_rows, minus_rows], axis=1)
        real_part = left_dot(weight[0], joined)
        cross_part = left_dot(weight[1], joined)
        outputs.append(
            (real_part[:, :num_edges] - cross_part[:, num_edges:]).reshape(
                span_rows, channel_count, num_edges
            )
        )
        outputs.append(
            (cross_part[:, :num_edges] + real_part[:, num_edges:]).reshape(
                span_rows, channel_count, num_edges
            )
        )
        first_row = first_row + 2 * span_rows
    mixed = jnp.concatenate(outputs, axis=0)
    scalar = mixed[0]
    return jnp.concatenate(
        [jax.nn.silu(scalar)[None], mixed[1:] * jax.nn.sigmoid(scalar)[None]], axis=0
    ).astype(jnp.bfloat16)


def conv_kernel(
    src_ref, gain_ref, wig_ref, length_ref, kind_ref, basis_in_ref, kind_table_ref, radial_out_ref,
    zero_ref, one_ref, two_ref, onehot_ref, proj_ref, out_ref,
):
    levels = MAX_DEGREE + 1
    channel_count = CHANNELS
    num_edges = src_ref.shape[1]
    basis_count = basis_in_ref.shape[1]
    wig = wig_ref[...].astype(jnp.float32)
    gain = gain_ref[...]

    turned = [src_ref[r].astype(jnp.float32).T for r in range(src_ref.shape[0])]
    span_chan = CHANNELS // len(turned)
    rows = [
        jnp.concatenate([block[j * span_chan : (j + 1) * span_chan] for block in turned], axis=0)
        for j in range(COEFFS)
    ]
    normed = [None] * len(rows)
    for degree in range(levels):
        span = range(degree * degree, (degree + 1) ** 2)
        total = None
        for j in span:
            part = jnp.sum(rows[j] * rows[j], axis=0, keepdims=True)
            total = part if total is None else total + part
        inverse = 1.0 / jnp.sqrt(total / float((2 * degree + 1) * CHANNELS) + EPSILON)
        scale = gain[:, degree : degree + 1]
        for j in span:
            normed[j] = (rows[j] * scale * inverse).astype(jnp.bfloat16).astype(jnp.float32)

    rotated = [None] * ROTATED
    for degree in range(levels):
        reach_order = min(degree, MAX_ORDER)
        span_cols = 2 * degree + 1
        first_row = wigner_start(degree)
        for position in range(2 * reach_order + 1):
            total = None
            for column in range(span_cols):
                row = first_row + position * span_cols + column
                term = wig[row : row + 1, :] * normed[degree * degree + column]
                total = term if total is None else total + term
            rotated[order_index(degree, position - reach_order)] = total.astype(jnp.bfloat16)

    spacing = CUTOFF / (basis_count - 1)
    centers = lax.broadcasted_iota(jnp.int32, (basis_count, num_edges), 0).astype(jnp.float32) * spacing
    basis_rows = jnp.exp(
        -0.5 * jnp.square((length_ref[...] - centers) / (2.0 * spacing))
    ).astype(jnp.bfloat16)
    hidden = jnp.dot(basis_in_ref[...], basis_rows, preferred_element_type=jnp.float32) + jnp.dot(
        kind_table_ref[...], kind_ref[...], preferred_element_type=jnp.float32
    )
    hidden = (hidden * jax.nn.sigmoid(hidden)).astype(jnp.bfloat16)
    radial = jnp.dot(radial_out_ref[...], hidden, preferred_element_type=jnp.float32)

    lowest = jnp.concatenate(
        [
            (rotated[degree].astype(jnp.float32) * radial[degree * channel_count : (degree + 1) * channel_count]).astype(
                jnp.bfloat16
            )
            for degree in range(levels)
        ],
        axis=0,
    )
    mixed0 = jnp.dot(zero_ref[...], lowest, preferred_element_type=jnp.float32)
    mixed = [mixed0[degree * channel_count : (degree + 1) * channel_count] for degree in range(levels)]
    first_row = levels
    for harmonic, weight_ref in ((1, one_ref), (2, two_ref)):
        span_rows = levels - harmonic
        plus_rows = jnp.concatenate(rotated[first_row : first_row + span_rows], axis=0)
        minus_rows = jnp.concatenate(rotated[first_row + span_rows : first_row + 2 * span_rows], axis=0)
        real_plus = jnp.dot(weight_ref[0], plus_rows, preferred_element_type=jnp.float32)
        real_minus = jnp.dot(weight_ref[0], minus_rows, preferred_element_type=jnp.float32)
        cross_plus = jnp.dot(weight_ref[1], plus_rows, preferred_element_type=jnp.float32)
        cross_minus = jnp.dot(weight_ref[1], minus_rows, preferred_element_type=jnp.float32)
        new_plus = real_plus - cross_minus
        new_minus = cross_plus + real_minus
        mixed += [new_plus[k * channel_count : (k + 1) * channel_count] for k in range(span_rows)]
        mixed += [new_minus[k * channel_count : (k + 1) * channel_count] for k in range(span_rows)]
        first_row = first_row + 2 * span_rows

    scalar = mixed[0]
    gate = jax.nn.sigmoid(scalar)
    gated = [(scalar * gate).astype(jnp.bfloat16).astype(jnp.float32)] + [
        (piece * gate).astype(jnp.bfloat16).astype(jnp.float32) for piece in mixed[1:]
    ]

    messages = []
    for degree in range(levels):
        reach_order = min(degree, MAX_ORDER)
        span_cols = 2 * degree + 1
        first_row = wigner_start(degree)
        for column in range(span_cols):
            total = None
            for position in range(2 * reach_order + 1):
                row = first_row + position * span_cols + column
                term = wig[row : row + 1, :] * gated[order_index(degree, position - reach_order)]
                total = term if total is None else total + term
            messages.append(total)
    stacked = jnp.concatenate(messages, axis=0)
    upper_part = stacked.astype(jnp.bfloat16)
    lower_part = (stacked - upper_part.astype(jnp.float32)).astype(jnp.bfloat16)
    onehot = onehot_ref[...]
    summed = jnp.dot(upper_part, onehot, preferred_element_type=jnp.float32) + jnp.dot(
        lower_part, onehot, preferred_element_type=jnp.float32
    )
    for degree in range(levels):
        weight = proj_ref[degree]
        for j in range(degree * degree, (degree + 1) ** 2):
            piece = summed[j * channel_count : (j + 1) * channel_count]
            high = piece.astype(jnp.bfloat16)
            low = (piece - high.astype(jnp.float32)).astype(jnp.bfloat16)
            out_ref[j] = jnp.dot(weight, high, preferred_element_type=jnp.float32) + jnp.dot(
                weight, low, preferred_element_type=jnp.float32
            )


def convolve_edges(source, gain_cols, wig_mine, lengths, kind_onehot, radial_in, species_table, radial_out,
                   order_zero, order_one, order_two, onehot, proj_t):
    coeffs, channel_count = COEFFS, CHANNELS
    num_edges = source.shape[1]
    atom_count = onehot.shape[1]
    operands = (
        source,
        gain_cols,
        wig_mine,
        lengths[None, :],
        kind_onehot,
        radial_in.T,
        species_table.T,
        radial_out.T,
        order_zero.T,
        jnp.transpose(order_one, (0, 2, 1)),
        jnp.transpose(order_two, (0, 2, 1)),
        onehot,
        proj_t,
    )
    flops = 2 * num_edges * (order_zero.size + 2 * order_one.size + 2 * order_two.size + radial_out.size + radial_in.size)
    return pl.pallas_call(
        conv_kernel,
        out_shape=jax.ShapeDtypeStruct((coeffs, channel_count, atom_count), jnp.float32),
        in_specs=[pl.BlockSpec(memory_space=pltpu.VMEM)] * len(operands),
        out_specs=pl.BlockSpec(memory_space=pltpu.VMEM),
        cost_estimate=pl.CostEstimate(
            flops=flops,
            transcendentals=num_edges * (radial_in.shape[0] + 2 * channel_count),
            bytes_accessed=sum(int(x.size) * x.dtype.itemsize for x in operands) + coeffs * channel_count * atom_count * 4,
        ),
    )(*operands)


def split_dot(values, weight):
    upper_part = values.astype(jnp.bfloat16)
    lower_part = (values - upper_part.astype(jnp.float32)).astype(jnp.bfloat16)
    return jnp.dot(upper_part, weight, preferred_element_type=jnp.float32) + jnp.dot(
        lower_part, weight, preferred_element_type=jnp.float32
    )


def body(
    node_feats,
    norm_gain,
    species,
    send_list,
    edge_source,
    edge_target,
    edge_count,
    edge_length,
    wigner,
    radial_in,
    species_table,
    radial_out,
    order_zero,
    order_one,
    order_two,
    project_weight,
):
    levels = MAX_DEGREE + 1
    owners = lax.axis_size("irreps")
    quarter = lax.axis_index("irreps")
    coeffs, span_chan, atom_count = node_feats.shape
    per_owner = edge_source.shape[0] // owners
    first_edge = quarter * per_owner

    row_width = 128 * pl.cdiv(coeffs * span_chan, 128)
    node_rows = jnp.pad(
        node_feats.reshape(coeffs * span_chan, atom_count).T, ((0, 0), (0, row_width - coeffs * span_chan))
    )
    arrived = lax.all_to_all(node_rows[send_list], "graph", 0, 0, tiled=True)

    packed = jnp.concatenate(
        [norm_gain, project_weight.astype(jnp.float32).reshape(levels, -1)], axis=1
    )
    spread = lax.all_to_all(
        jnp.broadcast_to(packed[None], (owners,) + packed.shape), "irreps", 0, 0, tiled=True
    )
    gain_full = jnp.transpose(spread[:, :, :span_chan], (1, 0, 2)).reshape(levels, owners * span_chan)
    weight_full = jnp.transpose(
        spread[:, :, span_chan:].reshape(owners, levels, CHANNELS, span_chan), (1, 2, 0, 3)
    ).reshape(levels, CHANNELS, owners * span_chan)

    lookup = jnp.concatenate([node_rows, arrived], axis=0)
    source = lax.all_to_all(
        lookup[edge_source].reshape(owners, per_owner, row_width), "irreps", 0, 0, tiled=True
    )
    wig_mine = lax.dynamic_slice_in_dim(wigner, first_edge, per_owner, 1)
    targets_mine = lax.dynamic_slice_in_dim(edge_target, first_edge, per_owner)
    lengths_mine = lax.dynamic_slice_in_dim(edge_length, first_edge, per_owner)
    kinds = species[targets_mine]
    kind_onehot = (
        kinds[None, :] == jnp.arange(species_table.shape[0], dtype=jnp.int32)[:, None]
    ).astype(jnp.bfloat16)
    edge_weight = jnp.where(
        first_edge + jnp.arange(per_owner, dtype=jnp.int32) < edge_count[0], 0.25, 0.0
    ).astype(jnp.float32)
    onehot = jnp.where(
        targets_mine[:, None] == jnp.arange(atom_count, dtype=jnp.int32)[None, :],
        edge_weight[:, None],
        0.0,
    ).astype(jnp.bfloat16)
    proj_t = jnp.transpose(weight_full, (0, 2, 1)).astype(jnp.bfloat16)
    projected = convolve_edges(
        source, gain_full.T, wig_mine, lengths_mine, kind_onehot, radial_in, species_table, radial_out,
        order_zero, order_one, order_two, onehot, proj_t,
    )
    projected = jnp.transpose(projected, (1, 0, 2))
    returned = lax.all_to_all(
        projected.reshape(owners, span_chan, coeffs, atom_count).astype(jnp.bfloat16), "irreps", 0, 0, tiled=True
    )
    total = jnp.transpose(jnp.sum(returned.astype(jnp.float32), axis=0), (1, 0, 2))
    return (node_feats.astype(jnp.float32) + total).astype(jnp.bfloat16)


def solution(mesh):
    return jax.shard_map(
        body,
        mesh=mesh,
        in_specs=(
            P(None, "irreps", "graph"),
            P(None, "irreps"),
            P("graph"),
            P("graph"),
            P("graph"),
            P("graph"),
            P("graph"),
            P("graph"),
            P(None, "graph"),
            P(),
            P(),
            P(),
            P(),
            P(),
            P(),
            P(None, None, "irreps"),
        ),
        out_specs=P(None, "irreps", "graph"),
        check_vma=False,
    )
```

```python
import jax
import jax.numpy as jnp
import numpy as np
from jax import lax
from jax.sharding import PartitionSpec as P
from jax.experimental import pallas as pl
from jax.experimental.pallas import tpu as pltpu

CHANNELS = 128
MAX_DEGREE = 6
MAX_ORDER = 2
ROTATED = 29
COEFFS = 49


EPSILON = 1e-06
CUTOFF = 6.0


def order_index(degree, harmonic):
    if harmonic == 0:
        return degree
    first_row = MAX_DEGREE + 1
    for level in range(1, abs(harmonic)):
        first_row = first_row + 2 * (MAX_DEGREE + 1 - level)
    if harmonic < 0:
        first_row = first_row + MAX_DEGREE + 1 - abs(harmonic)
    return first_row + degree - abs(harmonic)


def wigner_start(degree):
    running = 0
    for level in range(degree):
        running = running + (2 * min(level, MAX_ORDER) + 1) * (2 * level + 1)
    return running


def left_dot(weight, values):
    return lax.dot_general(
        weight, values, (((0,), (0,)), ((), ())), preferred_element_type=jnp.float32
    )


def degree_sums(squares):
    return jnp.stack(
        [
            jnp.sum(squares[degree * degree : (degree + 1) ** 2], axis=0)
            for degree in range(MAX_DEGREE + 1)
        ]
    )


def normalize(node_feats, norm_gain, totals):
    levels = MAX_DEGREE + 1
    degree_of = np.repeat(np.arange(levels), 2 * np.arange(levels) + 1)
    entry_counts = (2 * np.arange(levels) + 1) * CHANNELS
    inverse = 1.0 / jnp.sqrt(totals / jnp.asarray(entry_counts, jnp.float32)[:, None] + EPSILON)
    gain_rows = norm_gain[degree_of]
    scale_rows = inverse[degree_of]
    return (node_feats.astype(jnp.float32) * gain_rows[:, :, None] * scale_rows[:, None, :]).astype(
        jnp.bfloat16
    )


def normalize_rows(values, gain_full, totals):
    levels = MAX_DEGREE + 1
    degree_of = np.repeat(np.arange(levels), 2 * np.arange(levels) + 1)
    entry_counts = (2 * np.arange(levels) + 1) * CHANNELS
    inverse = 1.0 / jnp.sqrt(totals / jnp.asarray(entry_counts, jnp.float32)[:, None] + EPSILON)
    gain_rows = gain_full[degree_of]
    scale_rows = inverse[degree_of]
    return (values * gain_rows[:, :, None] * scale_rows[:, None, :]).astype(jnp.bfloat16)


def rotate(source, wig_rows):
    pieces = [None] * ROTATED
    for degree in range(MAX_DEGREE + 1):
        reach_order = min(degree, MAX_ORDER)
        span_cols = 2 * degree + 1
        first_row = wigner_start(degree)
        for position in range(2 * reach_order + 1):
            total = None
            for column in range(span_cols):
                term = wig_rows[first_row + position * span_cols + column][None, :] * source[degree * degree + column]
                total = term if total is None else total + term
            pieces[order_index(degree, position - reach_order)] = total
    return jnp.stack(pieces).astype(jnp.bfloat16)


def unrotate(gated, wig_rows):
    pieces = []
    for degree in range(MAX_DEGREE + 1):
        reach_order = min(degree, MAX_ORDER)
        span_cols = 2 * degree + 1
        first_row = wigner_start(degree)
        for column in range(span_cols):
            total = None
            for position in range(2 * reach_order + 1):
                term = wig_rows[first_row + position * span_cols + column][None, :] * gated[
                    order_index(degree, position - reach_order)
                ]
                total = term if total is None else total + term
            pieces.append(total)
    return jnp.stack(pieces)


def radial_weights(lengths, kind_ids, radial_in, species_table, radial_out):
    basis_count = radial_in.shape[0]
    spacing = CUTOFF / (basis_count - 1)
    centers = jnp.arange(basis_count, dtype=jnp.float32) * spacing
    basis_rows = jnp.exp(
        -0.5 * jnp.square((lengths[None, :] - centers[:, None]) / (2.0 * spacing))
    ).astype(jnp.bfloat16)
    onehot = (
        kind_ids[None, :] == jnp.arange(species_table.shape[0], dtype=jnp.int32)[:, None]
    ).astype(jnp.bfloat16)
    hidden = jax.nn.silu(left_dot(radial_in, basis_rows) + left_dot(species_table, onehot)).astype(
        jnp.bfloat16
    )
    return left_dot(radial_out, hidden)


def convolve(rotated, radial, order_zero, order_one, order_two):
    levels = MAX_DEGREE + 1
    channel_count = rotated.shape[1]
    num_edges = rotated.shape[2]
    lowest = (
        rotated[:levels].astype(jnp.float32).reshape(levels * channel_count, num_edges) * radial
    ).astype(jnp.bfloat16)
    outputs = [left_dot(order_zero, lowest).reshape(levels, channel_count, num_edges)]
    first_row = levels
    for harmonic, weight in ((1, order_one), (2, order_two)):
        span_rows = levels - harmonic
        plus_rows = rotated[first_row : first_row + span_rows].reshape(
            span_rows * channel_count, num_edges
        )
        minus_rows = rotated[first_row + span_rows : first_row + 2 * span_rows].reshape(
            span_rows * channel_count, num_edges
        )
        joined = jnp.concatenate([plus_rows, minus_rows], axis=1)
        real_part = left_dot(weight[0], joined)
        cross_part = left_dot(weight[1], joined)
        outputs.append(
            (real_part[:, :num_edges] - cross_part[:, num_edges:]).reshape(
                span_rows, channel_count, num_edges
            )
        )
        outputs.append(
            (cross_part[:, :num_edges] + real_part[:, num_edges:]).reshape(
                span_rows, channel_count, num_edges
            )
        )
        first_row = first_row + 2 * span_rows
    mixed = jnp.concatenate(outputs, axis=0)
    scalar = mixed[0]
    return jnp.concatenate(
        [jax.nn.silu(scalar)[None], mixed[1:] * jax.nn.sigmoid(scalar)[None]], axis=0
    ).astype(jnp.bfloat16)


def conv_kernel(
    src_ref, gain_ref, wig_ref, length_ref, kind_ref, basis_in_ref, kind_table_ref, radial_out_ref,
    zero_ref, one_ref, two_ref, onehot_ref, proj_ref, out_ref,
):
    levels = MAX_DEGREE + 1
    channel_count = CHANNELS
    num_edges = src_ref.shape[1]
    basis_count = basis_in_ref.shape[1]
    wig = wig_ref[...].astype(jnp.float32)
    gain = gain_ref[...]

    turned = [src_ref[r].astype(jnp.float32).T for r in range(src_ref.shape[0])]
    span_chan = CHANNELS // len(turned)
    rows = [
        jnp.concatenate([block[j * span_chan : (j + 1) * span_chan] for block in turned], axis=0)
        for j in range(COEFFS)
    ]
    normed = [None] * len(rows)
    for degree in range(levels):
        span = range(degree * degree, (degree + 1) ** 2)
        total = None
        for j in span:
            part = jnp.sum(rows[j] * rows[j], axis=0, keepdims=True)
            total = part if total is None else total + part
        inverse = 1.0 / jnp.sqrt(total / float((2 * degree + 1) * CHANNELS) + EPSILON)
        scale = gain[:, degree : degree + 1]
        for j in span:
            normed[j] = (rows[j] * scale * inverse).astype(jnp.bfloat16).astype(jnp.float32)

    rotated = [None] * ROTATED
    for degree in range(levels):
        reach_order = min(degree, MAX_ORDER)
        span_cols = 2 * degree + 1
        first_row = wigner_start(degree)
        for position in range(2 * reach_order + 1):
            total = None
            for column in range(span_cols):
                row = first_row + position * span_cols + column
                term = wig[row : row + 1, :] * normed[degree * degree + column]
                total = term if total is None else total + term
            rotated[order_index(degree, position - reach_order)] = total.astype(jnp.bfloat16)

    spacing = CUTOFF / (basis_count - 1)
    centers = lax.broadcasted_iota(jnp.int32, (basis_count, num_edges), 0).astype(jnp.float32) * spacing
    basis_rows = jnp.exp(
        -0.5 * jnp.square((length_ref[...] - centers) / (2.0 * spacing))
    ).astype(jnp.bfloat16)
    hidden = jnp.dot(basis_in_ref[...], basis_rows, preferred_element_type=jnp.float32) + jnp.dot(
        kind_table_ref[...], kind_ref[...], preferred_element_type=jnp.float32
    )
    hidden = (hidden * jax.nn.sigmoid(hidden)).astype(jnp.bfloat16)
    radial = jnp.dot(radial_out_ref[...], hidden, preferred_element_type=jnp.float32)

    lowest = jnp.concatenate(
        [
            (rotated[degree].astype(jnp.float32) * radial[degree * channel_count : (degree + 1) * channel_count]).astype(
                jnp.bfloat16
            )
            for degree in range(levels)
        ],
        axis=0,
    )
    mixed0 = jnp.dot(zero_ref[...], lowest, preferred_element_type=jnp.float32)
    mixed = [mixed0[degree * channel_count : (degree + 1) * channel_count] for degree in range(levels)]
    first_row = levels
    for harmonic, weight_ref in ((1, one_ref), (2, two_ref)):
        span_rows = levels - harmonic
        plus_rows = jnp.concatenate(rotated[first_row : first_row + span_rows], axis=0)
        minus_rows = jnp.concatenate(rotated[first_row + span_rows : first_row + 2 * span_rows], axis=0)
        real_plus = jnp.dot(weight_ref[0], plus_rows, preferred_element_type=jnp.float32)
        real_minus = jnp.dot(weight_ref[0], minus_rows, preferred_element_type=jnp.float32)
        cross_plus = jnp.dot(weight_ref[1], plus_rows, preferred_element_type=jnp.float32)
        cross_minus = jnp.dot(weight_ref[1], minus_rows, preferred_element_type=jnp.float32)
        new_plus = real_plus - cross_minus
        new_minus = cross_plus + real_minus
        mixed += [new_plus[k * channel_count : (k + 1) * channel_count] for k in range(span_rows)]
        mixed += [new_minus[k * channel_count : (k + 1) * channel_count] for k in range(span_rows)]
        first_row = first_row + 2 * span_rows

    scalar = mixed[0]
    gate = jax.nn.sigmoid(scalar)
    gated = [(scalar * gate).astype(jnp.bfloat16).astype(jnp.float32)] + [
        (piece * gate).astype(jnp.bfloat16).astype(jnp.float32) for piece in mixed[1:]
    ]

    messages = []
    for degree in range(levels):
        reach_order = min(degree, MAX_ORDER)
        span_cols = 2 * degree + 1
        first_row = wigner_start(degree)
        for column in range(span_cols):
            total = None
            for position in range(2 * reach_order + 1):
                row = first_row + position * span_cols + column
                term = wig[row : row + 1, :] * gated[order_index(degree, position - reach_order)]
                total = term if total is None else total + term
            messages.append(total)
    stacked = jnp.concatenate(messages, axis=0)
    upper_part = stacked.astype(jnp.bfloat16)
    lower_part = (stacked - upper_part.astype(jnp.float32)).astype(jnp.bfloat16)
    onehot = onehot_ref[...]
    summed = jnp.dot(upper_part, onehot, preferred_element_type=jnp.float32) + jnp.dot(
        lower_part, onehot, preferred_element_type=jnp.float32
    )
    for degree in range(levels):
        weight = proj_ref[degree]
        for j in range(degree * degree, (degree + 1) ** 2):
            piece = summed[j * channel_count : (j + 1) * channel_count]
            high = piece.astype(jnp.bfloat16)
            low = (piece - high.astype(jnp.float32)).astype(jnp.bfloat16)
            out_ref[j] = jnp.dot(weight, high, preferred_element_type=jnp.float32) + jnp.dot(
                weight, low, preferred_element_type=jnp.float32
            )


def convolve_edges(source, gain_cols, wig_mine, lengths, kind_onehot, radial_in, species_table, radial_out,
                   order_zero, order_one, order_two, onehot, proj_t):
    coeffs, channel_count = COEFFS, CHANNELS
    num_edges = source.shape[1]
    atom_count = onehot.shape[1]
    operands = (
        source,
        gain_cols,
        wig_mine,
        lengths[None, :],
        kind_onehot,
        radial_in.T,
        species_table.T,
        radial_out.T,
        order_zero.T,
        jnp.transpose(order_one, (0, 2, 1)),
        jnp.transpose(order_two, (0, 2, 1)),
        onehot,
        proj_t,
    )
    flops = 2 * num_edges * (order_zero.size + 2 * order_one.size + 2 * order_two.size + radial_out.size + radial_in.size)
    return pl.pallas_call(
        conv_kernel,
        out_shape=jax.ShapeDtypeStruct((coeffs, channel_count, atom_count), jnp.float32),
        in_specs=[pl.BlockSpec(memory_space=pltpu.VMEM)] * len(operands),
        out_specs=pl.BlockSpec(memory_space=pltpu.VMEM),
        cost_estimate=pl.CostEstimate(
            flops=flops,
            transcendentals=num_edges * (radial_in.shape[0] + 2 * channel_count),
            bytes_accessed=sum(int(x.size) * x.dtype.itemsize for x in operands) + coeffs * channel_count * atom_count * 4,
        ),
    )(*operands)


def split_dot(values, weight):
    upper_part = values.astype(jnp.bfloat16)
    lower_part = (values - upper_part.astype(jnp.float32)).astype(jnp.bfloat16)
    return jnp.dot(upper_part, weight, preferred_element_type=jnp.float32) + jnp.dot(
        lower_part, weight, preferred_element_type=jnp.float32
    )


def body(
    node_feats,
    norm_gain,
    species,
    send_list,
    edge_source,
    edge_target,
    edge_count,
    edge_length,
    wigner,
    radial_in,
    species_table,
    radial_out,
    order_zero,
    order_one,
    order_two,
    project_weight,
):
    levels = MAX_DEGREE + 1
    owners = lax.axis_size("irreps")
    quarter = lax.axis_index("irreps")
    coeffs, span_chan, atom_count = node_feats.shape
    per_owner = edge_source.shape[0] // owners
    first_edge = quarter * per_owner

    row_used = coeffs * span_chan
    row_width = 128 * pl.cdiv(row_used, 128)
    node_rows = node_feats.reshape(row_used, atom_count).T
    arrived = lax.all_to_all(node_rows[send_list], "graph", 0, 0, tiled=True)

    gain_high = norm_gain.astype(jnp.bfloat16)
    gain_rest = norm_gain - gain_high.astype(jnp.float32)
    gain_mid = gain_rest.astype(jnp.bfloat16)
    gain_low = (gain_rest - gain_mid.astype(jnp.float32)).astype(jnp.bfloat16)
    extra = jnp.concatenate(
        [project_weight.reshape(-1), gain_high.reshape(-1), gain_mid.reshape(-1), gain_low.reshape(-1)]
    )
    extra_len = extra.shape[0]
    spare = per_owner * (row_width - row_used)
    extra = jnp.pad(extra, (0, spare - extra_len)).reshape(per_owner, row_width - row_used)

    lookup = jnp.concatenate([node_rows, arrived], axis=0)
    outgoing = jnp.concatenate(
        [
            lookup[edge_source].reshape(owners, per_owner, row_used),
            jnp.broadcast_to(extra[None], (owners,) + extra.shape),
        ],
        axis=2,
    )
    source = lax.all_to_all(outgoing, "irreps", 0, 0, tiled=True)
    carried = source[:, :, row_used:].reshape(owners, -1)[:, :extra_len]
    weight_len = project_weight.size
    proj_t = jnp.transpose(
        carried[:, :weight_len].reshape(owners, levels, CHANNELS, span_chan), (1, 0, 3, 2)
    ).reshape(levels, owners * span_chan, CHANNELS)
    gain_parts = carried[:, weight_len:].astype(jnp.float32).reshape(owners, 3, levels, span_chan)
    gain_sum = gain_parts[:, 0] + gain_parts[:, 1] + gain_parts[:, 2]
    gain_cols = jnp.transpose(gain_sum, (0, 2, 1)).reshape(owners * span_chan, levels)

    wig_mine = lax.dynamic_slice_in_dim(wigner, first_edge, per_owner, 1)
    targets_mine = lax.dynamic_slice_in_dim(edge_target, first_edge, per_owner)
    lengths_mine = lax.dynamic_slice_in_dim(edge_length, first_edge, per_owner)
    kinds = species[targets_mine]
    kind_onehot = (
        kinds[None, :] == jnp.arange(species_table.shape[0], dtype=jnp.int32)[:, None]
    ).astype(jnp.bfloat16)
    edge_weight = jnp.where(
        first_edge + jnp.arange(per_owner, dtype=jnp.int32) < edge_count[0], 0.25, 0.0
    ).astype(jnp.float32)
    onehot = jnp.where(
        targets_mine[:, None] == jnp.arange(atom_count, dtype=jnp.int32)[None, :],
        edge_weight[:, None],
        0.0,
    ).astype(jnp.bfloat16)
    projected = convolve_edges(
        source, gain_cols, wig_mine, lengths_mine, kind_onehot, radial_in, species_table, radial_out,
        order_zero, order_one, order_two, onehot, proj_t,
    )
    projected = jnp.transpose(projected, (1, 0, 2))
    returned = lax.all_to_all(
        projected.reshape(owners, span_chan, coeffs, atom_count).astype(jnp.bfloat16), "irreps", 0, 0, tiled=True
    )
    total = jnp.transpose(jnp.sum(returned.astype(jnp.float32), axis=0), (1, 0, 2))
    return (node_feats.astype(jnp.float32) + total).astype(jnp.bfloat16)


def solution(mesh):
    return jax.shard_map(
        body,
        mesh=mesh,
        in_specs=(
            P(None, "irreps", "graph"),
            P(None, "irreps"),
            P("graph"),
            P("graph"),
            P("graph"),
            P("graph"),
            P("graph"),
            P("graph"),
            P(None, "graph"),
            P(),
            P(),
            P(),
            P(),
            P(),
            P(),
            P(None, None, "irreps"),
        ),
        out_specs=P(None, "irreps", "graph"),
        check_vma=False,
    )
```

```python
import jax
import jax.numpy as jnp
import numpy as np
from jax import lax
from jax.sharding import PartitionSpec as P
from jax.experimental import pallas as pl
from jax.experimental.pallas import tpu as pltpu

CHANNELS = 128
MAX_DEGREE = 6
MAX_ORDER = 2
ROTATED = 29
COEFFS = 49


EPSILON = 1e-06
CUTOFF = 6.0


def order_index(degree, harmonic):
    if harmonic == 0:
        return degree
    first_row = MAX_DEGREE + 1
    for level in range(1, abs(harmonic)):
        first_row = first_row + 2 * (MAX_DEGREE + 1 - level)
    if harmonic < 0:
        first_row = first_row + MAX_DEGREE + 1 - abs(harmonic)
    return first_row + degree - abs(harmonic)


def wigner_start(degree):
    running = 0
    for level in range(degree):
        running = running + (2 * min(level, MAX_ORDER) + 1) * (2 * level + 1)
    return running


def left_dot(weight, values):
    return lax.dot_general(
        weight, values, (((0,), (0,)), ((), ())), preferred_element_type=jnp.float32
    )


def degree_sums(squares):
    return jnp.stack(
        [
            jnp.sum(squares[degree * degree : (degree + 1) ** 2], axis=0)
            for degree in range(MAX_DEGREE + 1)
        ]
    )


def normalize(node_feats, norm_gain, totals):
    levels = MAX_DEGREE + 1
    degree_of = np.repeat(np.arange(levels), 2 * np.arange(levels) + 1)
    entry_counts = (2 * np.arange(levels) + 1) * CHANNELS
    inverse = 1.0 / jnp.sqrt(totals / jnp.asarray(entry_counts, jnp.float32)[:, None] + EPSILON)
    gain_rows = norm_gain[degree_of]
    scale_rows = inverse[degree_of]
    return (node_feats.astype(jnp.float32) * gain_rows[:, :, None] * scale_rows[:, None, :]).astype(
        jnp.bfloat16
    )


def normalize_rows(values, gain_full, totals):
    levels = MAX_DEGREE + 1
    degree_of = np.repeat(np.arange(levels), 2 * np.arange(levels) + 1)
    entry_counts = (2 * np.arange(levels) + 1) * CHANNELS
    inverse = 1.0 / jnp.sqrt(totals / jnp.asarray(entry_counts, jnp.float32)[:, None] + EPSILON)
    gain_rows = gain_full[degree_of]
    scale_rows = inverse[degree_of]
    return (values * gain_rows[:, :, None] * scale_rows[:, None, :]).astype(jnp.bfloat16)


def rotate(source, wig_rows):
    pieces = [None] * ROTATED
    for degree in range(MAX_DEGREE + 1):
        reach_order = min(degree, MAX_ORDER)
        span_cols = 2 * degree + 1
        first_row = wigner_start(degree)
        for position in range(2 * reach_order + 1):
            total = None
            for column in range(span_cols):
                term = wig_rows[first_row + position * span_cols + column][None, :] * source[degree * degree + column]
                total = term if total is None else total + term
            pieces[order_index(degree, position - reach_order)] = total
    return jnp.stack(pieces).astype(jnp.bfloat16)


def unrotate(gated, wig_rows):
    pieces = []
    for degree in range(MAX_DEGREE + 1):
        reach_order = min(degree, MAX_ORDER)
        span_cols = 2 * degree + 1
        first_row = wigner_start(degree)
        for column in range(span_cols):
            total = None
            for position in range(2 * reach_order + 1):
                term = wig_rows[first_row + position * span_cols + column][None, :] * gated[
                    order_index(degree, position - reach_order)
                ]
                total = term if total is None else total + term
            pieces.append(total)
    return jnp.stack(pieces)


def radial_weights(lengths, kind_ids, radial_in, species_table, radial_out):
    basis_count = radial_in.shape[0]
    spacing = CUTOFF / (basis_count - 1)
    centers = jnp.arange(basis_count, dtype=jnp.float32) * spacing
    basis_rows = jnp.exp(
        -0.5 * jnp.square((lengths[None, :] - centers[:, None]) / (2.0 * spacing))
    ).astype(jnp.bfloat16)
    onehot = (
        kind_ids[None, :] == jnp.arange(species_table.shape[0], dtype=jnp.int32)[:, None]
    ).astype(jnp.bfloat16)
    hidden = jax.nn.silu(left_dot(radial_in, basis_rows) + left_dot(species_table, onehot)).astype(
        jnp.bfloat16
    )
    return left_dot(radial_out, hidden)


def convolve(rotated, radial, order_zero, order_one, order_two):
    levels = MAX_DEGREE + 1
    channel_count = rotated.shape[1]
    num_edges = rotated.shape[2]
    lowest = (
        rotated[:levels].astype(jnp.float32).reshape(levels * channel_count, num_edges) * radial
    ).astype(jnp.bfloat16)
    outputs = [left_dot(order_zero, lowest).reshape(levels, channel_count, num_edges)]
    first_row = levels
    for harmonic, weight in ((1, order_one), (2, order_two)):
        span_rows = levels - harmonic
        plus_rows = rotated[first_row : first_row + span_rows].reshape(
            span_rows * channel_count, num_edges
        )
        minus_rows = rotated[first_row + span_rows : first_row + 2 * span_rows].reshape(
            span_rows * channel_count, num_edges
        )
        joined = jnp.concatenate([plus_rows, minus_rows], axis=1)
        real_part = left_dot(weight[0], joined)
        cross_part = left_dot(weight[1], joined)
        outputs.append(
            (real_part[:, :num_edges] - cross_part[:, num_edges:]).reshape(
                span_rows, channel_count, num_edges
            )
        )
        outputs.append(
            (cross_part[:, :num_edges] + real_part[:, num_edges:]).reshape(
                span_rows, channel_count, num_edges
            )
        )
        first_row = first_row + 2 * span_rows
    mixed = jnp.concatenate(outputs, axis=0)
    scalar = mixed[0]
    return jnp.concatenate(
        [jax.nn.silu(scalar)[None], mixed[1:] * jax.nn.sigmoid(scalar)[None]], axis=0
    ).astype(jnp.bfloat16)


def conv_kernel(
    src_ref, wig_ref, length_ref, kind_ref, basis_in_ref, kind_table_ref, radial_out_ref,
    zero_ref, one_ref, two_ref, onehot_ref, out_ref,
):
    levels = MAX_DEGREE + 1
    channel_count = CHANNELS
    num_edges = onehot_ref.shape[0]
    basis_count = basis_in_ref.shape[1]
    wig = wig_ref[...].astype(jnp.float32)
    owners = src_ref.shape[0]
    span_chan = CHANNELS // owners
    pick = (
        lax.broadcasted_iota(jnp.int32, (CHANNELS, span_chan), 0) % span_chan
        == lax.broadcasted_iota(jnp.int32, (CHANNELS, span_chan), 1)
    ) & (lax.broadcasted_iota(jnp.int32, (CHANNELS, span_chan), 0) < 3 * span_chan)
    pick = pick.astype(jnp.bfloat16)
    gain = jnp.concatenate(
        [
            jnp.dot(
                src_ref[r, num_edges + span_chan : num_edges + 2 * span_chan, 3 * CHANNELS : 4 * CHANNELS],
                pick,
                preferred_element_type=jnp.float32,
            )
            for r in range(owners)
        ],
        axis=0,
    )
    projection = [
        jnp.concatenate(
            [
                src_ref[
                    r,
                    num_edges + (degree // 4) * span_chan : num_edges + (degree // 4 + 1) * span_chan,
                    (degree % 4) * CHANNELS : (degree % 4 + 1) * CHANNELS,
                ].astype(jnp.float32)
                for r in range(owners)
            ],
            axis=0,
        ).astype(jnp.bfloat16)
        for degree in range(levels)
    ]

    turned = [src_ref[r, 0:num_edges].astype(jnp.float32).T for r in range(owners)]
    rows = [
        jnp.concatenate([block[j * span_chan : (j + 1) * span_chan] for block in turned], axis=0)
        for j in range(COEFFS)
    ]
    normed = [None] * len(rows)
    for degree in range(levels):
        span = range(degree * degree, (degree + 1) ** 2)
        total = None
        for j in span:
            part = jnp.sum(rows[j] * rows[j], axis=0, keepdims=True)
            total = part if total is None else total + part
        inverse = 1.0 / jnp.sqrt(total / float((2 * degree + 1) * CHANNELS) + EPSILON)
        scale = gain[:, degree : degree + 1]
        for j in span:
            normed[j] = (rows[j] * scale * inverse).astype(jnp.bfloat16).astype(jnp.float32)

    rotated = [None] * ROTATED
    for degree in range(levels):
        reach_order = min(degree, MAX_ORDER)
        span_cols = 2 * degree + 1
        first_row = wigner_start(degree)
        for position in range(2 * reach_order + 1):
            total = None
            for column in range(span_cols):
                row = first_row + position * span_cols + column
                term = wig[row : row + 1, :] * normed[degree * degree + column]
                total = term if total is None else total + term
            rotated[order_index(degree, position - reach_order)] = total.astype(jnp.bfloat16)

    spacing = CUTOFF / (basis_count - 1)
    centers = lax.broadcasted_iota(jnp.int32, (basis_count, num_edges), 0).astype(jnp.float32) * spacing
    basis_rows = jnp.exp(
        -0.5 * jnp.square((length_ref[...] - centers) / (2.0 * spacing))
    ).astype(jnp.bfloat16)
    hidden = jnp.dot(basis_in_ref[...], basis_rows, preferred_element_type=jnp.float32) + jnp.dot(
        kind_table_ref[...], kind_ref[...], preferred_element_type=jnp.float32
    )
    hidden = (hidden * jax.nn.sigmoid(hidden)).astype(jnp.bfloat16)
    radial = jnp.dot(radial_out_ref[...], hidden, preferred_element_type=jnp.float32)

    lowest = jnp.concatenate(
        [
            (rotated[degree].astype(jnp.float32) * radial[degree * channel_count : (degree + 1) * channel_count]).astype(
                jnp.bfloat16
            )
            for degree in range(levels)
        ],
        axis=0,
    )
    mixed0 = jnp.dot(zero_ref[...], lowest, preferred_element_type=jnp.float32)
    mixed = [mixed0[degree * channel_count : (degree + 1) * channel_count] for degree in range(levels)]
    first_row = levels
    for harmonic, weight_ref in ((1, one_ref), (2, two_ref)):
        span_rows = levels - harmonic
        plus_rows = jnp.concatenate(rotated[first_row : first_row + span_rows], axis=0)
        minus_rows = jnp.concatenate(rotated[first_row + span_rows : first_row + 2 * span_rows], axis=0)
        real_plus = jnp.dot(weight_ref[0], plus_rows, preferred_element_type=jnp.float32)
        real_minus = jnp.dot(weight_ref[0], minus_rows, preferred_element_type=jnp.float32)
        cross_plus = jnp.dot(weight_ref[1], plus_rows, preferred_element_type=jnp.float32)
        cross_minus = jnp.dot(weight_ref[1], minus_rows, preferred_element_type=jnp.float32)
        new_plus = real_plus - cross_minus
        new_minus = cross_plus + real_minus
        mixed += [new_plus[k * channel_count : (k + 1) * channel_count] for k in range(span_rows)]
        mixed += [new_minus[k * channel_count : (k + 1) * channel_count] for k in range(span_rows)]
        first_row = first_row + 2 * span_rows

    scalar = mixed[0]
    gate = jax.nn.sigmoid(scalar)
    gated = [(scalar * gate).astype(jnp.bfloat16).astype(jnp.float32)] + [
        (piece * gate).astype(jnp.bfloat16).astype(jnp.float32) for piece in mixed[1:]
    ]

    messages = []
    for degree in range(levels):
        reach_order = min(degree, MAX_ORDER)
        span_cols = 2 * degree + 1
        first_row = wigner_start(degree)
        for column in range(span_cols):
            total = None
            for position in range(2 * reach_order + 1):
                row = first_row + position * span_cols + column
                term = wig[row : row + 1, :] * gated[order_index(degree, position - reach_order)]
                total = term if total is None else total + term
            messages.append(total)
    stacked = jnp.concatenate(messages, axis=0)
    upper_part = stacked.astype(jnp.bfloat16)
    lower_part = (stacked - upper_part.astype(jnp.float32)).astype(jnp.bfloat16)
    onehot = onehot_ref[...]
    summed = jnp.dot(upper_part, onehot, preferred_element_type=jnp.float32) + jnp.dot(
        lower_part, onehot, preferred_element_type=jnp.float32
    )
    for degree in range(levels):
        weight = projection[degree]
        for j in range(degree * degree, (degree + 1) ** 2):
            piece = summed[j * channel_count : (j + 1) * channel_count]
            high = piece.astype(jnp.bfloat16)
            low = (piece - high.astype(jnp.float32)).astype(jnp.bfloat16)
            out_ref[j] = jnp.dot(weight, high, preferred_element_type=jnp.float32) + jnp.dot(
                weight, low, preferred_element_type=jnp.float32
            )


def convolve_edges(source, wig_mine, lengths, kind_onehot, radial_in, species_table, radial_out,
                   order_zero, order_one, order_two, onehot, per_owner):
    coeffs, channel_count = COEFFS, CHANNELS
    num_edges = per_owner
    atom_count = onehot.shape[1]
    operands = (
        source,
        wig_mine,
        lengths[None, :],
        kind_onehot,
        radial_in.T,
        species_table.T,
        radial_out.T,
        order_zero.T,
        jnp.transpose(order_one, (0, 2, 1)),
        jnp.transpose(order_two, (0, 2, 1)),
        onehot,
    )
    flops = 2 * num_edges * (order_zero.size + 2 * order_one.size + 2 * order_two.size + radial_out.size + radial_in.size)
    return pl.pallas_call(
        conv_kernel,
        out_shape=jax.ShapeDtypeStruct((coeffs, channel_count, atom_count), jnp.float32),
        in_specs=[pl.BlockSpec(memory_space=pltpu.VMEM)] * len(operands),
        out_specs=pl.BlockSpec(memory_space=pltpu.VMEM),
        cost_estimate=pl.CostEstimate(
            flops=flops,
            transcendentals=num_edges * (radial_in.shape[0] + 2 * channel_count),
            bytes_accessed=sum(int(x.size) * x.dtype.itemsize for x in operands) + coeffs * channel_count * atom_count * 4,
        ),
    )(*operands)


def split_dot(values, weight):
    upper_part = values.astype(jnp.bfloat16)
    lower_part = (values - upper_part.astype(jnp.float32)).astype(jnp.bfloat16)
    return jnp.dot(upper_part, weight, preferred_element_type=jnp.float32) + jnp.dot(
        lower_part, weight, preferred_element_type=jnp.float32
    )


def body(
    node_feats,
    norm_gain,
    species,
    send_list,
    edge_source,
    edge_target,
    edge_count,
    edge_length,
    wigner,
    radial_in,
    species_table,
    radial_out,
    order_zero,
    order_one,
    order_two,
    project_weight,
):
    levels = MAX_DEGREE + 1
    owners = lax.axis_size("irreps")
    quarter = lax.axis_index("irreps")
    coeffs, span_chan, atom_count = node_feats.shape
    per_owner = edge_source.shape[0] // owners
    first_edge = quarter * per_owner

    row_used = coeffs * span_chan
    row_width = 128 * pl.cdiv(row_used, 128)
    node_rows = node_feats.reshape(row_used, atom_count).T
    arrived = lax.all_to_all(node_rows[send_list], "graph", 0, 0, tiled=True)

    gain_high = lax.reduce_precision(norm_gain, exponent_bits=8, mantissa_bits=7)
    gain_rest = norm_gain - gain_high
    gain_mid = lax.reduce_precision(gain_rest, exponent_bits=8, mantissa_bits=7)
    gain_low = gain_rest - gain_mid
    gain_block = jnp.transpose(jnp.stack([gain_high, gain_mid, gain_low]), (2, 0, 1))
    gain_block = jnp.pad(gain_block, ((0, 0), (0, 0), (0, 1))).reshape(span_chan, 3 * (levels + 1))
    gain_block = jnp.pad(gain_block, ((0, 0), (0, CHANNELS - gain_block.shape[1]))).astype(jnp.bfloat16)
    weight_block = jnp.concatenate(
        [jnp.transpose(project_weight, (2, 0, 1)), gain_block[:, None, :]], axis=1
    )
    extra = jnp.transpose(weight_block.reshape(span_chan, 2, 4, CHANNELS), (1, 0, 2, 3)).reshape(
        2 * span_chan, 4 * CHANNELS
    )

    lookup = jnp.concatenate([node_rows, arrived], axis=0)
    gathered = jnp.pad(
        lookup[edge_source].reshape(owners, per_owner, row_used), ((0, 0), (0, 0), (0, row_width - row_used))
    )
    outgoing = jnp.concatenate([gathered, jnp.broadcast_to(extra[None], (owners,) + extra.shape)], axis=1)
    source = lax.all_to_all(outgoing, "irreps", 0, 0, tiled=True)

    wig_mine = lax.dynamic_slice_in_dim(wigner, first_edge, per_owner, 1)
    targets_mine = lax.dynamic_slice_in_dim(edge_target, first_edge, per_owner)
    lengths_mine = lax.dynamic_slice_in_dim(edge_length, first_edge, per_owner)
    kinds = species[targets_mine]
    kind_onehot = (
        kinds[None, :] == jnp.arange(species_table.shape[0], dtype=jnp.int32)[:, None]
    ).astype(jnp.bfloat16)
    edge_weight = jnp.where(
        first_edge + jnp.arange(per_owner, dtype=jnp.int32) < edge_count[0], 0.25, 0.0
    ).astype(jnp.float32)
    onehot = jnp.where(
        targets_mine[:, None] == jnp.arange(atom_count, dtype=jnp.int32)[None, :],
        edge_weight[:, None],
        0.0,
    ).astype(jnp.bfloat16)
    projected = convolve_edges(
        source, wig_mine, lengths_mine, kind_onehot, radial_in, species_table, radial_out,
        order_zero, order_one, order_two, onehot, per_owner,
    )
    projected = jnp.transpose(projected, (1, 0, 2))
    returned = lax.all_to_all(
        projected.reshape(owners, span_chan, coeffs, atom_count).astype(jnp.bfloat16), "irreps", 0, 0, tiled=True
    )
    total = jnp.transpose(jnp.sum(returned.astype(jnp.float32), axis=0), (1, 0, 2))
    return (node_feats.astype(jnp.float32) + total).astype(jnp.bfloat16)


def solution(mesh):
    return jax.shard_map(
        body,
        mesh=mesh,
        in_specs=(
            P(None, "irreps", "graph"),
            P(None, "irreps"),
            P("graph"),
            P("graph"),
            P("graph"),
            P("graph"),
            P("graph"),
            P("graph"),
            P(None, "graph"),
            P(),
            P(),
            P(),
            P(),
            P(),
            P(),
            P(None, None, "irreps"),
        ),
        out_specs=P(None, "irreps", "graph"),
        check_vma=False,
    )
```

```python
import jax
import jax.numpy as jnp
import numpy as np
from jax import lax
from jax.sharding import PartitionSpec as P
from jax.experimental import pallas as pl
from jax.experimental.pallas import tpu as pltpu

CHANNELS = 128
MAX_DEGREE = 6
MAX_ORDER = 2
ROTATED = 29
COEFFS = 49


EPSILON = 1e-06
CUTOFF = 6.0


def order_index(degree, harmonic):
    if harmonic == 0:
        return degree
    first_row = MAX_DEGREE + 1
    for level in range(1, abs(harmonic)):
        first_row = first_row + 2 * (MAX_DEGREE + 1 - level)
    if harmonic < 0:
        first_row = first_row + MAX_DEGREE + 1 - abs(harmonic)
    return first_row + degree - abs(harmonic)


def wigner_start(degree):
    running = 0
    for level in range(degree):
        running = running + (2 * min(level, MAX_ORDER) + 1) * (2 * level + 1)
    return running


def left_dot(weight, values):
    return lax.dot_general(
        weight, values, (((0,), (0,)), ((), ())), preferred_element_type=jnp.float32
    )


def degree_sums(squares):
    return jnp.stack(
        [
            jnp.sum(squares[degree * degree : (degree + 1) ** 2], axis=0)
            for degree in range(MAX_DEGREE + 1)
        ]
    )


def normalize(node_feats, norm_gain, totals):
    levels = MAX_DEGREE + 1
    degree_of = np.repeat(np.arange(levels), 2 * np.arange(levels) + 1)
    entry_counts = (2 * np.arange(levels) + 1) * CHANNELS
    inverse = 1.0 / jnp.sqrt(totals / jnp.asarray(entry_counts, jnp.float32)[:, None] + EPSILON)
    gain_rows = norm_gain[degree_of]
    scale_rows = inverse[degree_of]
    return (node_feats.astype(jnp.float32) * gain_rows[:, :, None] * scale_rows[:, None, :]).astype(
        jnp.bfloat16
    )


def normalize_rows(values, gain_full, totals):
    levels = MAX_DEGREE + 1
    degree_of = np.repeat(np.arange(levels), 2 * np.arange(levels) + 1)
    entry_counts = (2 * np.arange(levels) + 1) * CHANNELS
    inverse = 1.0 / jnp.sqrt(totals / jnp.asarray(entry_counts, jnp.float32)[:, None] + EPSILON)
    gain_rows = gain_full[degree_of]
    scale_rows = inverse[degree_of]
    return (values * gain_rows[:, :, None] * scale_rows[:, None, :]).astype(jnp.bfloat16)


def rotate(source, wig_rows):
    pieces = [None] * ROTATED
    for degree in range(MAX_DEGREE + 1):
        reach_order = min(degree, MAX_ORDER)
        span_cols = 2 * degree + 1
        first_row = wigner_start(degree)
        for position in range(2 * reach_order + 1):
            total = None
            for column in range(span_cols):
                term = wig_rows[first_row + position * span_cols + column][None, :] * source[degree * degree + column]
                total = term if total is None else total + term
            pieces[order_index(degree, position - reach_order)] = total
    return jnp.stack(pieces).astype(jnp.bfloat16)


def unrotate(gated, wig_rows):
    pieces = []
    for degree in range(MAX_DEGREE + 1):
        reach_order = min(degree, MAX_ORDER)
        span_cols = 2 * degree + 1
        first_row = wigner_start(degree)
        for column in range(span_cols):
            total = None
            for position in range(2 * reach_order + 1):
                term = wig_rows[first_row + position * span_cols + column][None, :] * gated[
                    order_index(degree, position - reach_order)
                ]
                total = term if total is None else total + term
            pieces.append(total)
    return jnp.stack(pieces)


def radial_weights(lengths, kind_ids, radial_in, species_table, radial_out):
    basis_count = radial_in.shape[0]
    spacing = CUTOFF / (basis_count - 1)
    centers = jnp.arange(basis_count, dtype=jnp.float32) * spacing
    basis_rows = jnp.exp(
        -0.5 * jnp.square((lengths[None, :] - centers[:, None]) / (2.0 * spacing))
    ).astype(jnp.bfloat16)
    onehot = (
        kind_ids[None, :] == jnp.arange(species_table.shape[0], dtype=jnp.int32)[:, None]
    ).astype(jnp.bfloat16)
    hidden = jax.nn.silu(left_dot(radial_in, basis_rows) + left_dot(species_table, onehot)).astype(
        jnp.bfloat16
    )
    return left_dot(radial_out, hidden)


def convolve(rotated, radial, order_zero, order_one, order_two):
    levels = MAX_DEGREE + 1
    channel_count = rotated.shape[1]
    num_edges = rotated.shape[2]
    lowest = (
        rotated[:levels].astype(jnp.float32).reshape(levels * channel_count, num_edges) * radial
    ).astype(jnp.bfloat16)
    outputs = [left_dot(order_zero, lowest).reshape(levels, channel_count, num_edges)]
    first_row = levels
    for harmonic, weight in ((1, order_one), (2, order_two)):
        span_rows = levels - harmonic
        plus_rows = rotated[first_row : first_row + span_rows].reshape(
            span_rows * channel_count, num_edges
        )
        minus_rows = rotated[first_row + span_rows : first_row + 2 * span_rows].reshape(
            span_rows * channel_count, num_edges
        )
        joined = jnp.concatenate([plus_rows, minus_rows], axis=1)
        real_part = left_dot(weight[0], joined)
        cross_part = left_dot(weight[1], joined)
        outputs.append(
            (real_part[:, :num_edges] - cross_part[:, num_edges:]).reshape(
                span_rows, channel_count, num_edges
            )
        )
        outputs.append(
            (cross_part[:, :num_edges] + real_part[:, num_edges:]).reshape(
                span_rows, channel_count, num_edges
            )
        )
        first_row = first_row + 2 * span_rows
    mixed = jnp.concatenate(outputs, axis=0)
    scalar = mixed[0]
    return jnp.concatenate(
        [jax.nn.silu(scalar)[None], mixed[1:] * jax.nn.sigmoid(scalar)[None]], axis=0
    ).astype(jnp.bfloat16)


def conv_kernel(
    src_ref, wig_ref, length_ref, kind_ref, basis_in_ref, kind_table_ref, radial_out_ref,
    zero_ref, one_ref, two_ref, onehot_ref, out_ref,
):
    levels = MAX_DEGREE + 1
    channel_count = CHANNELS
    num_edges = onehot_ref.shape[0]
    basis_count = basis_in_ref.shape[1]
    wig = wig_ref[...].astype(jnp.float32)
    owners = src_ref.shape[0]
    span_chan = CHANNELS // owners
    pick = (
        lax.broadcasted_iota(jnp.int32, (CHANNELS, span_chan), 0) % span_chan
        == lax.broadcasted_iota(jnp.int32, (CHANNELS, span_chan), 1)
    ) & (lax.broadcasted_iota(jnp.int32, (CHANNELS, span_chan), 0) < 3 * span_chan)
    pick = pick.astype(jnp.bfloat16)
    gain = jnp.concatenate(
        [
            jnp.dot(
                src_ref[r, num_edges + span_chan : num_edges + 2 * span_chan, 3 * CHANNELS : 4 * CHANNELS],
                pick,
                preferred_element_type=jnp.float32,
            )
            for r in range(owners)
        ],
        axis=0,
    )
    projection = [
        jnp.concatenate(
            [
                src_ref[
                    r,
                    num_edges + (degree // 4) * span_chan : num_edges + (degree // 4 + 1) * span_chan,
                    (degree % 4) * CHANNELS : (degree % 4 + 1) * CHANNELS,
                ].astype(jnp.float32)
                for r in range(owners)
            ],
            axis=0,
        ).astype(jnp.bfloat16)
        for degree in range(levels)
    ]

    turned = [src_ref[r, 0:num_edges].astype(jnp.float32).T for r in range(owners)]
    rows = [
        jnp.concatenate([block[j * span_chan : (j + 1) * span_chan] for block in turned], axis=0)
        for j in range(COEFFS)
    ]
    normed = [None] * len(rows)
    for degree in range(levels):
        span = range(degree * degree, (degree + 1) ** 2)
        total = None
        for j in span:
            part = jnp.sum(rows[j] * rows[j], axis=0, keepdims=True)
            total = part if total is None else total + part
        inverse = 1.0 / jnp.sqrt(total / float((2 * degree + 1) * CHANNELS) + EPSILON)
        scale = gain[:, degree : degree + 1]
        for j in span:
            normed[j] = (rows[j] * scale * inverse).astype(jnp.bfloat16).astype(jnp.float32)

    rotated = [None] * ROTATED
    for degree in range(levels):
        reach_order = min(degree, MAX_ORDER)
        span_cols = 2 * degree + 1
        first_row = wigner_start(degree)
        for position in range(2 * reach_order + 1):
            total = None
            for column in range(span_cols):
                row = first_row + position * span_cols + column
                term = wig[row : row + 1, :] * normed[degree * degree + column]
                total = term if total is None else total + term
            rotated[order_index(degree, position - reach_order)] = total.astype(jnp.bfloat16)

    spacing = CUTOFF / (basis_count - 1)
    centers = lax.broadcasted_iota(jnp.int32, (basis_count, num_edges), 0).astype(jnp.float32) * spacing
    basis_rows = jnp.exp(
        -0.5 * jnp.square((length_ref[...] - centers) / (2.0 * spacing))
    ).astype(jnp.bfloat16)
    hidden = jnp.dot(basis_in_ref[...], basis_rows, preferred_element_type=jnp.float32) + jnp.dot(
        kind_table_ref[...], kind_ref[...], preferred_element_type=jnp.float32
    )
    hidden = (hidden * jax.nn.sigmoid(hidden)).astype(jnp.bfloat16)
    radial = jnp.dot(radial_out_ref[...], hidden, preferred_element_type=jnp.float32)

    lowest = jnp.concatenate(
        [
            (rotated[degree].astype(jnp.float32) * radial[degree * channel_count : (degree + 1) * channel_count]).astype(
                jnp.bfloat16
            )
            for degree in range(levels)
        ],
        axis=0,
    )
    mixed0 = jnp.dot(zero_ref[...], lowest, preferred_element_type=jnp.float32)
    mixed = [mixed0[degree * channel_count : (degree + 1) * channel_count] for degree in range(levels)]
    first_row = levels
    for harmonic, weight_ref in ((1, one_ref), (2, two_ref)):
        span_rows = levels - harmonic
        plus_rows = jnp.concatenate(rotated[first_row : first_row + span_rows], axis=0)
        minus_rows = jnp.concatenate(rotated[first_row + span_rows : first_row + 2 * span_rows], axis=0)
        real_plus = jnp.dot(weight_ref[0], plus_rows, preferred_element_type=jnp.float32)
        real_minus = jnp.dot(weight_ref[0], minus_rows, preferred_element_type=jnp.float32)
        cross_plus = jnp.dot(weight_ref[1], plus_rows, preferred_element_type=jnp.float32)
        cross_minus = jnp.dot(weight_ref[1], minus_rows, preferred_element_type=jnp.float32)
        new_plus = real_plus - cross_minus
        new_minus = cross_plus + real_minus
        mixed += [new_plus[k * channel_count : (k + 1) * channel_count] for k in range(span_rows)]
        mixed += [new_minus[k * channel_count : (k + 1) * channel_count] for k in range(span_rows)]
        first_row = first_row + 2 * span_rows

    scalar = mixed[0]
    gate = jax.nn.sigmoid(scalar)
    gated = [(scalar * gate).astype(jnp.bfloat16).astype(jnp.float32)] + [
        (piece * gate).astype(jnp.bfloat16).astype(jnp.float32) for piece in mixed[1:]
    ]

    messages = []
    for degree in range(levels):
        reach_order = min(degree, MAX_ORDER)
        span_cols = 2 * degree + 1
        first_row = wigner_start(degree)
        for column in range(span_cols):
            total = None
            for position in range(2 * reach_order + 1):
                row = first_row + position * span_cols + column
                term = wig[row : row + 1, :] * gated[order_index(degree, position - reach_order)]
                total = term if total is None else total + term
            messages.append(total)
    stacked = jnp.concatenate(messages, axis=0)
    upper_part = stacked.astype(jnp.bfloat16)
    lower_part = (stacked - upper_part.astype(jnp.float32)).astype(jnp.bfloat16)
    onehot = onehot_ref[...]
    summed = jnp.dot(upper_part, onehot, preferred_element_type=jnp.float32) + jnp.dot(
        lower_part, onehot, preferred_element_type=jnp.float32
    )
    for degree in range(levels):
        weight = projection[degree]
        for j in range(degree * degree, (degree + 1) ** 2):
            piece = summed[j * channel_count : (j + 1) * channel_count]
            high = piece.astype(jnp.bfloat16)
            low = (piece - high.astype(jnp.float32)).astype(jnp.bfloat16)
            out_ref[j] = jnp.dot(weight, high, preferred_element_type=jnp.float32) + jnp.dot(
                weight, low, preferred_element_type=jnp.float32
            )


def convolve_edges(source, wig_mine, lengths, kind_onehot, radial_in, species_table, radial_out,
                   order_zero, order_one, order_two, onehot, per_owner):
    coeffs, channel_count = COEFFS, CHANNELS
    num_edges = per_owner
    atom_count = onehot.shape[1]
    operands = (
        source,
        wig_mine,
        lengths[None, :],
        kind_onehot,
        radial_in.T,
        species_table.T,
        radial_out.T,
        order_zero.T,
        jnp.transpose(order_one, (0, 2, 1)),
        jnp.transpose(order_two, (0, 2, 1)),
        onehot,
    )
    flops = 2 * num_edges * (order_zero.size + 2 * order_one.size + 2 * order_two.size + radial_out.size + radial_in.size)
    return pl.pallas_call(
        conv_kernel,
        out_shape=jax.ShapeDtypeStruct((coeffs, channel_count, atom_count), jnp.float32),
        in_specs=[pl.BlockSpec(memory_space=pltpu.VMEM)] * len(operands),
        out_specs=pl.BlockSpec(memory_space=pltpu.VMEM),
        cost_estimate=pl.CostEstimate(
            flops=flops,
            transcendentals=num_edges * (radial_in.shape[0] + 2 * channel_count),
            bytes_accessed=sum(int(x.size) * x.dtype.itemsize for x in operands) + coeffs * channel_count * atom_count * 4,
        ),
    )(*operands)


def split_dot(values, weight):
    upper_part = values.astype(jnp.bfloat16)
    lower_part = (values - upper_part.astype(jnp.float32)).astype(jnp.bfloat16)
    return jnp.dot(upper_part, weight, preferred_element_type=jnp.float32) + jnp.dot(
        lower_part, weight, preferred_element_type=jnp.float32
    )


def body(
    node_feats,
    norm_gain,
    species,
    send_list,
    edge_source,
    edge_target,
    edge_count,
    edge_length,
    wigner,
    radial_in,
    species_table,
    radial_out,
    order_zero,
    order_one,
    order_two,
    project_weight,
):
    levels = MAX_DEGREE + 1
    owners = lax.axis_size("irreps")
    quarter = lax.axis_index("irreps")
    coeffs, span_chan, atom_count = node_feats.shape
    per_owner = edge_source.shape[0] // owners
    first_edge = quarter * per_owner

    row_used = coeffs * span_chan
    row_width = 128 * pl.cdiv(row_used, 128)
    node_rows = node_feats.reshape(row_used, atom_count).T
    arrived = lax.all_to_all(node_rows[send_list], "graph", 0, 0, tiled=True)

    gain_high = lax.reduce_precision(norm_gain, exponent_bits=8, mantissa_bits=7)
    gain_rest = norm_gain - gain_high
    gain_mid = lax.reduce_precision(gain_rest, exponent_bits=8, mantissa_bits=7)
    gain_low = gain_rest - gain_mid
    gain_block = jnp.transpose(jnp.stack([gain_high, gain_mid, gain_low]), (2, 0, 1))
    gain_block = jnp.pad(gain_block, ((0, 0), (0, 0), (0, 1))).reshape(span_chan, 3 * (levels + 1))
    gain_block = jnp.pad(gain_block, ((0, 0), (0, CHANNELS - gain_block.shape[1]))).astype(jnp.bfloat16)
    weight_block = jnp.concatenate(
        [jnp.transpose(project_weight, (2, 0, 1)), gain_block[:, None, :]], axis=1
    )
    extra = jnp.transpose(weight_block.reshape(span_chan, 2, 4, CHANNELS), (1, 0, 2, 3)).reshape(
        2 * span_chan, 4 * CHANNELS
    )

    lookup = jnp.concatenate([node_rows, arrived], axis=0)
    gathered = jnp.pad(
        lookup[edge_source].reshape(owners, per_owner, row_used), ((0, 0), (0, 0), (0, row_width - row_used))
    )
    outgoing = jnp.concatenate([gathered, jnp.broadcast_to(extra[None], (owners,) + extra.shape)], axis=1)
    source = lax.all_to_all(outgoing, "irreps", 0, 0, tiled=True)

    wig_mine = lax.dynamic_slice_in_dim(wigner, first_edge, per_owner, 1)
    targets_mine = lax.dynamic_slice_in_dim(edge_target, first_edge, per_owner)
    lengths_mine = lax.dynamic_slice_in_dim(edge_length, first_edge, per_owner)
    kinds = species[targets_mine]
    kind_onehot = (
        kinds[None, :] == jnp.arange(species_table.shape[0], dtype=jnp.int32)[:, None]
    ).astype(jnp.bfloat16)
    edge_weight = jnp.where(
        first_edge + jnp.arange(per_owner, dtype=jnp.int32) < edge_count[0], 0.25, 0.0
    ).astype(jnp.float32)
    onehot = jnp.where(
        targets_mine[:, None] == jnp.arange(atom_count, dtype=jnp.int32)[None, :],
        edge_weight[:, None],
        0.0,
    ).astype(jnp.bfloat16)
    projected = convolve_edges(
        source, wig_mine, lengths_mine, kind_onehot, radial_in, species_table, radial_out,
        order_zero, order_one, order_two, onehot, per_owner,
    )
    projected = jnp.transpose(projected, (1, 0, 2))
    total = jnp.transpose(
        lax.psum_scatter(projected.reshape(owners * span_chan, coeffs, atom_count), "irreps", scatter_dimension=0, tiled=True),
        (1, 0, 2),
    )
    return (node_feats.astype(jnp.float32) + total).astype(jnp.bfloat16)


def solution(mesh):
    return jax.shard_map(
        body,
        mesh=mesh,
        in_specs=(
            P(None, "irreps", "graph"),
            P(None, "irreps"),
            P("graph"),
            P("graph"),
            P("graph"),
            P("graph"),
            P("graph"),
            P("graph"),
            P(None, "graph"),
            P(),
            P(),
            P(),
            P(),
            P(),
            P(),
            P(None, None, "irreps"),
        ),
        out_specs=P(None, "irreps", "graph"),
        check_vma=False,
    )
```

```python
import jax
import jax.numpy as jnp
import numpy as np
from jax import lax
from jax.sharding import PartitionSpec as P
from jax.experimental import pallas as pl
from jax.experimental.pallas import tpu as pltpu

CHANNELS = 128
MAX_DEGREE = 6
MAX_ORDER = 2
ROTATED = 29
COEFFS = 49


EPSILON = 1e-06
CUTOFF = 6.0


def order_index(degree, harmonic):
    if harmonic == 0:
        return degree
    first_row = MAX_DEGREE + 1
    for level in range(1, abs(harmonic)):
        first_row = first_row + 2 * (MAX_DEGREE + 1 - level)
    if harmonic < 0:
        first_row = first_row + MAX_DEGREE + 1 - abs(harmonic)
    return first_row + degree - abs(harmonic)


def wigner_start(degree):
    running = 0
    for level in range(degree):
        running = running + (2 * min(level, MAX_ORDER) + 1) * (2 * level + 1)
    return running


def left_dot(weight, values):
    return lax.dot_general(
        weight, values, (((0,), (0,)), ((), ())), preferred_element_type=jnp.float32
    )


def degree_sums(squares):
    return jnp.stack(
        [
            jnp.sum(squares[degree * degree : (degree + 1) ** 2], axis=0)
            for degree in range(MAX_DEGREE + 1)
        ]
    )


def normalize(node_feats, norm_gain, totals):
    levels = MAX_DEGREE + 1
    degree_of = np.repeat(np.arange(levels), 2 * np.arange(levels) + 1)
    entry_counts = (2 * np.arange(levels) + 1) * CHANNELS
    inverse = 1.0 / jnp.sqrt(totals / jnp.asarray(entry_counts, jnp.float32)[:, None] + EPSILON)
    gain_rows = norm_gain[degree_of]
    scale_rows = inverse[degree_of]
    return (node_feats.astype(jnp.float32) * gain_rows[:, :, None] * scale_rows[:, None, :]).astype(
        jnp.bfloat16
    )


def normalize_rows(values, gain_full, totals):
    levels = MAX_DEGREE + 1
    degree_of = np.repeat(np.arange(levels), 2 * np.arange(levels) + 1)
    entry_counts = (2 * np.arange(levels) + 1) * CHANNELS
    inverse = 1.0 / jnp.sqrt(totals / jnp.asarray(entry_counts, jnp.float32)[:, None] + EPSILON)
    gain_rows = gain_full[degree_of]
    scale_rows = inverse[degree_of]
    return (values * gain_rows[:, :, None] * scale_rows[:, None, :]).astype(jnp.bfloat16)


def rotate(source, wig_rows):
    pieces = [None] * ROTATED
    for degree in range(MAX_DEGREE + 1):
        reach_order = min(degree, MAX_ORDER)
        span_cols = 2 * degree + 1
        first_row = wigner_start(degree)
        for position in range(2 * reach_order + 1):
            total = None
            for column in range(span_cols):
                term = wig_rows[first_row + position * span_cols + column][None, :] * source[degree * degree + column]
                total = term if total is None else total + term
            pieces[order_index(degree, position - reach_order)] = total
    return jnp.stack(pieces).astype(jnp.bfloat16)


def unrotate(gated, wig_rows):
    pieces = []
    for degree in range(MAX_DEGREE + 1):
        reach_order = min(degree, MAX_ORDER)
        span_cols = 2 * degree + 1
        first_row = wigner_start(degree)
        for column in range(span_cols):
            total = None
            for position in range(2 * reach_order + 1):
                term = wig_rows[first_row + position * span_cols + column][None, :] * gated[
                    order_index(degree, position - reach_order)
                ]
                total = term if total is None else total + term
            pieces.append(total)
    return jnp.stack(pieces)


def radial_weights(lengths, kind_ids, radial_in, species_table, radial_out):
    basis_count = radial_in.shape[0]
    spacing = CUTOFF / (basis_count - 1)
    centers = jnp.arange(basis_count, dtype=jnp.float32) * spacing
    basis_rows = jnp.exp(
        -0.5 * jnp.square((lengths[None, :] - centers[:, None]) / (2.0 * spacing))
    ).astype(jnp.bfloat16)
    onehot = (
        kind_ids[None, :] == jnp.arange(species_table.shape[0], dtype=jnp.int32)[:, None]
    ).astype(jnp.bfloat16)
    hidden = jax.nn.silu(left_dot(radial_in, basis_rows) + left_dot(species_table, onehot)).astype(
        jnp.bfloat16
    )
    return left_dot(radial_out, hidden)


def convolve(rotated, radial, order_zero, order_one, order_two):
    levels = MAX_DEGREE + 1
    channel_count = rotated.shape[1]
    num_edges = rotated.shape[2]
    lowest = (
        rotated[:levels].astype(jnp.float32).reshape(levels * channel_count, num_edges) * radial
    ).astype(jnp.bfloat16)
    outputs = [left_dot(order_zero, lowest).reshape(levels, channel_count, num_edges)]
    first_row = levels
    for harmonic, weight in ((1, order_one), (2, order_two)):
        span_rows = levels - harmonic
        plus_rows = rotated[first_row : first_row + span_rows].reshape(
            span_rows * channel_count, num_edges
        )
        minus_rows = rotated[first_row + span_rows : first_row + 2 * span_rows].reshape(
            span_rows * channel_count, num_edges
        )
        joined = jnp.concatenate([plus_rows, minus_rows], axis=1)
        real_part = left_dot(weight[0], joined)
        cross_part = left_dot(weight[1], joined)
        outputs.append(
            (real_part[:, :num_edges] - cross_part[:, num_edges:]).reshape(
                span_rows, channel_count, num_edges
            )
        )
        outputs.append(
            (cross_part[:, :num_edges] + real_part[:, num_edges:]).reshape(
                span_rows, channel_count, num_edges
            )
        )
        first_row = first_row + 2 * span_rows
    mixed = jnp.concatenate(outputs, axis=0)
    scalar = mixed[0]
    return jnp.concatenate(
        [jax.nn.silu(scalar)[None], mixed[1:] * jax.nn.sigmoid(scalar)[None]], axis=0
    ).astype(jnp.bfloat16)


def conv_kernel(
    src_ref, wig_ref, length_ref, kind_ref, basis_in_ref, kind_table_ref, radial_out_ref,
    zero_ref, one_ref, two_ref, onehot_ref, out_ref,
):
    levels = MAX_DEGREE + 1
    channel_count = CHANNELS
    num_edges = onehot_ref.shape[0]
    basis_count = basis_in_ref.shape[1]
    wig = wig_ref[...].astype(jnp.float32)
    owners = src_ref.shape[0]
    span_chan = CHANNELS // owners
    pick = (
        lax.broadcasted_iota(jnp.int32, (CHANNELS, span_chan), 0) % span_chan
        == lax.broadcasted_iota(jnp.int32, (CHANNELS, span_chan), 1)
    ) & (lax.broadcasted_iota(jnp.int32, (CHANNELS, span_chan), 0) < 3 * span_chan)
    pick = pick.astype(jnp.bfloat16)
    gain = jnp.concatenate(
        [
            jnp.dot(
                src_ref[r, num_edges + span_chan : num_edges + 2 * span_chan, 3 * CHANNELS : 4 * CHANNELS],
                pick,
                preferred_element_type=jnp.float32,
            )
            for r in range(owners)
        ],
        axis=0,
    )
    projection = [
        jnp.concatenate(
            [
                src_ref[
                    r,
                    num_edges + (degree // 4) * span_chan : num_edges + (degree // 4 + 1) * span_chan,
                    (degree % 4) * CHANNELS : (degree % 4 + 1) * CHANNELS,
                ].astype(jnp.float32)
                for r in range(owners)
            ],
            axis=0,
        ).astype(jnp.bfloat16)
        for degree in range(levels)
    ]

    turned = [src_ref[r, 0:num_edges].astype(jnp.float32).T for r in range(owners)]
    rows = [
        jnp.concatenate([block[j * span_chan : (j + 1) * span_chan] for block in turned], axis=0)
        for j in range(COEFFS)
    ]
    normed = [None] * len(rows)
    for degree in range(levels):
        span = range(degree * degree, (degree + 1) ** 2)
        total = None
        for j in span:
            part = jnp.sum(rows[j] * rows[j], axis=0, keepdims=True)
            total = part if total is None else total + part
        inverse = 1.0 / jnp.sqrt(total / float((2 * degree + 1) * CHANNELS) + EPSILON)
        scale = gain[:, degree : degree + 1]
        for j in span:
            normed[j] = (rows[j] * scale * inverse).astype(jnp.bfloat16).astype(jnp.float32)

    rotated = [None] * ROTATED
    for degree in range(levels):
        reach_order = min(degree, MAX_ORDER)
        span_cols = 2 * degree + 1
        first_row = wigner_start(degree)
        for position in range(2 * reach_order + 1):
            total = None
            for column in range(span_cols):
                row = first_row + position * span_cols + column
                term = wig[row : row + 1, :] * normed[degree * degree + column]
                total = term if total is None else total + term
            rotated[order_index(degree, position - reach_order)] = total.astype(jnp.bfloat16)

    spacing = CUTOFF / (basis_count - 1)
    centers = lax.broadcasted_iota(jnp.int32, (basis_count, num_edges), 0).astype(jnp.float32) * spacing
    basis_rows = jnp.exp(
        -0.5 * jnp.square((length_ref[...] - centers) / (2.0 * spacing))
    ).astype(jnp.bfloat16)
    hidden = jnp.dot(basis_in_ref[...], basis_rows, preferred_element_type=jnp.float32) + jnp.dot(
        kind_table_ref[...], kind_ref[...], preferred_element_type=jnp.float32
    )
    hidden = (hidden * jax.nn.sigmoid(hidden)).astype(jnp.bfloat16)
    radial = jnp.dot(radial_out_ref[...], hidden, preferred_element_type=jnp.float32)

    lowest = jnp.concatenate(
        [
            (rotated[degree].astype(jnp.float32) * radial[degree * channel_count : (degree + 1) * channel_count]).astype(
                jnp.bfloat16
            )
            for degree in range(levels)
        ],
        axis=0,
    )
    mixed0 = jnp.dot(zero_ref[...], lowest, preferred_element_type=jnp.float32)
    mixed = [mixed0[degree * channel_count : (degree + 1) * channel_count] for degree in range(levels)]
    first_row = levels
    for harmonic, weight_ref in ((1, one_ref), (2, two_ref)):
        span_rows = levels - harmonic
        plus_rows = jnp.concatenate(rotated[first_row : first_row + span_rows], axis=0)
        minus_rows = jnp.concatenate(rotated[first_row + span_rows : first_row + 2 * span_rows], axis=0)
        real_plus = jnp.dot(weight_ref[0], plus_rows, preferred_element_type=jnp.float32)
        real_minus = jnp.dot(weight_ref[0], minus_rows, preferred_element_type=jnp.float32)
        cross_plus = jnp.dot(weight_ref[1], plus_rows, preferred_element_type=jnp.float32)
        cross_minus = jnp.dot(weight_ref[1], minus_rows, preferred_element_type=jnp.float32)
        new_plus = real_plus - cross_minus
        new_minus = cross_plus + real_minus
        mixed += [new_plus[k * channel_count : (k + 1) * channel_count] for k in range(span_rows)]
        mixed += [new_minus[k * channel_count : (k + 1) * channel_count] for k in range(span_rows)]
        first_row = first_row + 2 * span_rows

    scalar = mixed[0]
    gate = jax.nn.sigmoid(scalar)
    gated = [(scalar * gate).astype(jnp.bfloat16).astype(jnp.float32)] + [
        (piece * gate).astype(jnp.bfloat16).astype(jnp.float32) for piece in mixed[1:]
    ]

    messages = []
    for degree in range(levels):
        reach_order = min(degree, MAX_ORDER)
        span_cols = 2 * degree + 1
        first_row = wigner_start(degree)
        for column in range(span_cols):
            total = None
            for position in range(2 * reach_order + 1):
                row = first_row + position * span_cols + column
                term = wig[row : row + 1, :] * gated[order_index(degree, position - reach_order)]
                total = term if total is None else total + term
            messages.append(total)
    stacked = jnp.concatenate(messages, axis=0)
    upper_part = stacked.astype(jnp.bfloat16)
    lower_part = (stacked - upper_part.astype(jnp.float32)).astype(jnp.bfloat16)
    onehot = onehot_ref[...]
    summed = jnp.dot(upper_part, onehot, preferred_element_type=jnp.float32) + jnp.dot(
        lower_part, onehot, preferred_element_type=jnp.float32
    )
    half = span_chan // 2
    pieces = [[] for _ in range(owners)]
    for degree in range(levels):
        weight = projection[degree]
        for j in range(degree * degree, (degree + 1) ** 2):
            piece = summed[j * channel_count : (j + 1) * channel_count]
            high = piece.astype(jnp.bfloat16)
            low = (piece - high.astype(jnp.float32)).astype(jnp.bfloat16)
            result = jnp.dot(weight, high, preferred_element_type=jnp.float32) + jnp.dot(
                weight, low, preferred_element_type=jnp.float32
            )
            for r in range(owners):
                block = result[r * span_chan : (r + 1) * span_chan]
                pieces[r].append(jnp.concatenate([block[:half], block[half:]], axis=1))
    fill = out_ref.shape[1] - COEFFS * half
    for r in range(owners):
        out_ref[r] = jnp.concatenate(
            pieces[r] + [jnp.zeros((fill, out_ref.shape[2]), jnp.float32)], axis=0
        ).astype(out_ref.dtype)


def convolve_edges(source, wig_mine, lengths, kind_onehot, radial_in, species_table, radial_out,
                   order_zero, order_one, order_two, onehot, per_owner):
    coeffs, channel_count = COEFFS, CHANNELS
    num_edges = per_owner
    atom_count = onehot.shape[1]
    owners = source.shape[0]
    out_rows = 16 * pl.cdiv(coeffs * (channel_count // owners) // 2, 16)
    operands = (
        source,
        wig_mine,
        lengths[None, :],
        kind_onehot,
        radial_in.T,
        species_table.T,
        radial_out.T,
        order_zero.T,
        jnp.transpose(order_one, (0, 2, 1)),
        jnp.transpose(order_two, (0, 2, 1)),
        onehot,
    )
    flops = 2 * num_edges * (order_zero.size + 2 * order_one.size + 2 * order_two.size + radial_out.size + radial_in.size)
    return pl.pallas_call(
        conv_kernel,
        out_shape=jax.ShapeDtypeStruct((owners, out_rows, 2 * atom_count), jnp.bfloat16),
        in_specs=[pl.BlockSpec(memory_space=pltpu.VMEM)] * len(operands),
        out_specs=pl.BlockSpec(memory_space=pltpu.VMEM),
        cost_estimate=pl.CostEstimate(
            flops=flops,
            transcendentals=num_edges * (radial_in.shape[0] + 2 * channel_count),
            bytes_accessed=sum(int(x.size) * x.dtype.itemsize for x in operands) + owners * out_rows * atom_count * 4,
        ),
    )(*operands)


def split_dot(values, weight):
    upper_part = values.astype(jnp.bfloat16)
    lower_part = (values - upper_part.astype(jnp.float32)).astype(jnp.bfloat16)
    return jnp.dot(upper_part, weight, preferred_element_type=jnp.float32) + jnp.dot(
        lower_part, weight, preferred_element_type=jnp.float32
    )


def body(
    node_feats,
    norm_gain,
    species,
    send_list,
    edge_source,
    edge_target,
    edge_count,
    edge_length,
    wigner,
    radial_in,
    species_table,
    radial_out,
    order_zero,
    order_one,
    order_two,
    project_weight,
):
    levels = MAX_DEGREE + 1
    owners = lax.axis_size("irreps")
    quarter = lax.axis_index("irreps")
    coeffs, span_chan, atom_count = node_feats.shape
    per_owner = edge_source.shape[0] // owners
    first_edge = quarter * per_owner

    row_used = coeffs * span_chan
    row_width = 128 * pl.cdiv(row_used, 128)
    node_rows = node_feats.reshape(row_used, atom_count).T
    arrived = lax.all_to_all(node_rows[send_list], "graph", 0, 0, tiled=True)

    gain_high = lax.reduce_precision(norm_gain, exponent_bits=8, mantissa_bits=7)
    gain_rest = norm_gain - gain_high
    gain_mid = lax.reduce_precision(gain_rest, exponent_bits=8, mantissa_bits=7)
    gain_low = gain_rest - gain_mid
    gain_block = jnp.transpose(jnp.stack([gain_high, gain_mid, gain_low]), (2, 0, 1))
    gain_block = jnp.pad(gain_block, ((0, 0), (0, 0), (0, 1))).reshape(span_chan, 3 * (levels + 1))
    gain_block = jnp.pad(gain_block, ((0, 0), (0, CHANNELS - gain_block.shape[1]))).astype(jnp.bfloat16)
    pair_order = np.concatenate([np.arange(0, span_chan, 2), np.arange(1, span_chan, 2)])
    weight_block = jnp.concatenate(
        [jnp.transpose(project_weight[:, :, pair_order], (2, 0, 1)), gain_block[:, None, :]], axis=1
    )
    extra = jnp.transpose(weight_block.reshape(span_chan, 2, 4, CHANNELS), (1, 0, 2, 3)).reshape(
        2 * span_chan, 4 * CHANNELS
    )

    lookup = jnp.concatenate([node_rows, arrived], axis=0)
    gathered = jnp.pad(
        lookup[edge_source].reshape(owners, per_owner, row_used), ((0, 0), (0, 0), (0, row_width - row_used))
    )
    outgoing = jnp.concatenate([gathered, jnp.broadcast_to(extra[None], (owners,) + extra.shape)], axis=1)
    source = lax.all_to_all(outgoing, "irreps", 0, 0, tiled=True)

    wig_mine = lax.dynamic_slice_in_dim(wigner, first_edge, per_owner, 1)
    targets_mine = lax.dynamic_slice_in_dim(edge_target, first_edge, per_owner)
    lengths_mine = lax.dynamic_slice_in_dim(edge_length, first_edge, per_owner)
    kinds = species[targets_mine]
    kind_onehot = (
        kinds[None, :] == jnp.arange(species_table.shape[0], dtype=jnp.int32)[:, None]
    ).astype(jnp.bfloat16)
    edge_weight = jnp.where(
        first_edge + jnp.arange(per_owner, dtype=jnp.int32) < edge_count[0], 0.25, 0.0
    ).astype(jnp.float32)
    onehot = jnp.where(
        targets_mine[:, None] == jnp.arange(atom_count, dtype=jnp.int32)[None, :],
        edge_weight[:, None],
        0.0,
    ).astype(jnp.bfloat16)
    projected = convolve_edges(
        source, wig_mine, lengths_mine, kind_onehot, radial_in, species_table, radial_out,
        order_zero, order_one, order_two, onehot, per_owner,
    )
    returned = lax.all_to_all(projected, "irreps", 0, 0, tiled=True)
    total = jnp.sum(returned.astype(jnp.float32), axis=0)[: coeffs * span_chan // 2]
    total = total.reshape(coeffs, span_chan // 2, 2, atom_count).reshape(coeffs, span_chan, atom_count)
    return (node_feats.astype(jnp.float32) + total).astype(jnp.bfloat16)


def solution(mesh):
    return jax.shard_map(
        body,
        mesh=mesh,
        in_specs=(
            P(None, "irreps", "graph"),
            P(None, "irreps"),
            P("graph"),
            P("graph"),
            P("graph"),
            P("graph"),
            P("graph"),
            P("graph"),
            P(None, "graph"),
            P(),
            P(),
            P(),
            P(),
            P(),
            P(),
            P(None, None, "irreps"),
        ),
        out_specs=P(None, "irreps", "graph"),
        check_vma=False,
    )
```

```python
import jax
import jax.numpy as jnp
import numpy as np
from jax import lax
from jax.sharding import PartitionSpec as P
from jax.experimental import pallas as pl
from jax.experimental.pallas import tpu as pltpu

CHANNELS = 128
MAX_DEGREE = 6
MAX_ORDER = 2
ROTATED = 29
COEFFS = 49


EPSILON = 1e-06
CUTOFF = 6.0


def order_index(degree, harmonic):
    if harmonic == 0:
        return degree
    first_row = MAX_DEGREE + 1
    for level in range(1, abs(harmonic)):
        first_row = first_row + 2 * (MAX_DEGREE + 1 - level)
    if harmonic < 0:
        first_row = first_row + MAX_DEGREE + 1 - abs(harmonic)
    return first_row + degree - abs(harmonic)


def wigner_start(degree):
    running = 0
    for level in range(degree):
        running = running + (2 * min(level, MAX_ORDER) + 1) * (2 * level + 1)
    return running


def left_dot(weight, values):
    return lax.dot_general(
        weight, values, (((0,), (0,)), ((), ())), preferred_element_type=jnp.float32
    )


def degree_sums(squares):
    return jnp.stack(
        [
            jnp.sum(squares[degree * degree : (degree + 1) ** 2], axis=0)
            for degree in range(MAX_DEGREE + 1)
        ]
    )


def normalize(node_feats, norm_gain, totals):
    levels = MAX_DEGREE + 1
    degree_of = np.repeat(np.arange(levels), 2 * np.arange(levels) + 1)
    entry_counts = (2 * np.arange(levels) + 1) * CHANNELS
    inverse = 1.0 / jnp.sqrt(totals / jnp.asarray(entry_counts, jnp.float32)[:, None] + EPSILON)
    gain_rows = norm_gain[degree_of]
    scale_rows = inverse[degree_of]
    return (node_feats.astype(jnp.float32) * gain_rows[:, :, None] * scale_rows[:, None, :]).astype(
        jnp.bfloat16
    )


def normalize_rows(values, gain_full, totals):
    levels = MAX_DEGREE + 1
    degree_of = np.repeat(np.arange(levels), 2 * np.arange(levels) + 1)
    entry_counts = (2 * np.arange(levels) + 1) * CHANNELS
    inverse = 1.0 / jnp.sqrt(totals / jnp.asarray(entry_counts, jnp.float32)[:, None] + EPSILON)
    gain_rows = gain_full[degree_of]
    scale_rows = inverse[degree_of]
    return (values * gain_rows[:, :, None] * scale_rows[:, None, :]).astype(jnp.bfloat16)


def rotate(source, wig_rows):
    pieces = [None] * ROTATED
    for degree in range(MAX_DEGREE + 1):
        reach_order = min(degree, MAX_ORDER)
        span_cols = 2 * degree + 1
        first_row = wigner_start(degree)
        for position in range(2 * reach_order + 1):
            total = None
            for column in range(span_cols):
                term = wig_rows[first_row + position * span_cols + column][None, :] * source[degree * degree + column]
                total = term if total is None else total + term
            pieces[order_index(degree, position - reach_order)] = total
    return jnp.stack(pieces).astype(jnp.bfloat16)


def unrotate(gated, wig_rows):
    pieces = []
    for degree in range(MAX_DEGREE + 1):
        reach_order = min(degree, MAX_ORDER)
        span_cols = 2 * degree + 1
        first_row = wigner_start(degree)
        for column in range(span_cols):
            total = None
            for position in range(2 * reach_order + 1):
                term = wig_rows[first_row + position * span_cols + column][None, :] * gated[
                    order_index(degree, position - reach_order)
                ]
                total = term if total is None else total + term
            pieces.append(total)
    return jnp.stack(pieces)


def radial_weights(lengths, kind_ids, radial_in, species_table, radial_out):
    basis_count = radial_in.shape[0]
    spacing = CUTOFF / (basis_count - 1)
    centers = jnp.arange(basis_count, dtype=jnp.float32) * spacing
    basis_rows = jnp.exp(
        -0.5 * jnp.square((lengths[None, :] - centers[:, None]) / (2.0 * spacing))
    ).astype(jnp.bfloat16)
    onehot = (
        kind_ids[None, :] == jnp.arange(species_table.shape[0], dtype=jnp.int32)[:, None]
    ).astype(jnp.bfloat16)
    hidden = jax.nn.silu(left_dot(radial_in, basis_rows) + left_dot(species_table, onehot)).astype(
        jnp.bfloat16
    )
    return left_dot(radial_out, hidden)


def convolve(rotated, radial, order_zero, order_one, order_two):
    levels = MAX_DEGREE + 1
    channel_count = rotated.shape[1]
    num_edges = rotated.shape[2]
    lowest = (
        rotated[:levels].astype(jnp.float32).reshape(levels * channel_count, num_edges) * radial
    ).astype(jnp.bfloat16)
    outputs = [left_dot(order_zero, lowest).reshape(levels, channel_count, num_edges)]
    first_row = levels
    for harmonic, weight in ((1, order_one), (2, order_two)):
        span_rows = levels - harmonic
        plus_rows = rotated[first_row : first_row + span_rows].reshape(
            span_rows * channel_count, num_edges
        )
        minus_rows = rotated[first_row + span_rows : first_row + 2 * span_rows].reshape(
            span_rows * channel_count, num_edges
        )
        joined = jnp.concatenate([plus_rows, minus_rows], axis=1)
        real_part = left_dot(weight[0], joined)
        cross_part = left_dot(weight[1], joined)
        outputs.append(
            (real_part[:, :num_edges] - cross_part[:, num_edges:]).reshape(
                span_rows, channel_count, num_edges
            )
        )
        outputs.append(
            (cross_part[:, :num_edges] + real_part[:, num_edges:]).reshape(
                span_rows, channel_count, num_edges
            )
        )
        first_row = first_row + 2 * span_rows
    mixed = jnp.concatenate(outputs, axis=0)
    scalar = mixed[0]
    return jnp.concatenate(
        [jax.nn.silu(scalar)[None], mixed[1:] * jax.nn.sigmoid(scalar)[None]], axis=0
    ).astype(jnp.bfloat16)


def conv_kernel(
    src_ref, wig_ref, length_ref, kind_ref, basis_in_ref, kind_table_ref, radial_out_ref,
    zero_ref, one_ref, two_ref, onehot_ref, out_ref,
):
    levels = MAX_DEGREE + 1
    channel_count = CHANNELS
    num_edges = onehot_ref.shape[0]
    basis_count = basis_in_ref.shape[1]
    wig = wig_ref[...].astype(jnp.float32)
    owners = src_ref.shape[0]
    span_chan = CHANNELS // owners
    pick = (
        lax.broadcasted_iota(jnp.int32, (CHANNELS, span_chan), 0) % span_chan
        == lax.broadcasted_iota(jnp.int32, (CHANNELS, span_chan), 1)
    ) & (lax.broadcasted_iota(jnp.int32, (CHANNELS, span_chan), 0) < 3 * span_chan)
    pick = pick.astype(jnp.bfloat16)
    gain = jnp.concatenate(
        [
            jnp.dot(
                src_ref[r, num_edges + span_chan : num_edges + 2 * span_chan, 3 * CHANNELS : 4 * CHANNELS],
                pick,
                preferred_element_type=jnp.float32,
            )
            for r in range(owners)
        ],
        axis=0,
    )
    projection = [
        jnp.concatenate(
            [
                src_ref[
                    r,
                    num_edges + (degree // 4) * span_chan : num_edges + (degree // 4 + 1) * span_chan,
                    (degree % 4) * CHANNELS : (degree % 4 + 1) * CHANNELS,
                ].astype(jnp.float32)
                for r in range(owners)
            ],
            axis=0,
        ).astype(jnp.bfloat16)
        for degree in range(levels)
    ]

    turned = [src_ref[r, 0:num_edges].astype(jnp.float32).T for r in range(owners)]
    rows = [
        jnp.concatenate([block[j * span_chan : (j + 1) * span_chan] for block in turned], axis=0)
        for j in range(COEFFS)
    ]
    normed = [None] * len(rows)
    for degree in range(levels):
        span = range(degree * degree, (degree + 1) ** 2)
        total = None
        for j in span:
            part = jnp.sum(rows[j] * rows[j], axis=0, keepdims=True)
            total = part if total is None else total + part
        inverse = 1.0 / jnp.sqrt(total / float((2 * degree + 1) * CHANNELS) + EPSILON)
        scale = gain[:, degree : degree + 1]
        for j in span:
            normed[j] = (rows[j] * scale * inverse).astype(jnp.bfloat16).astype(jnp.float32)

    rotated = [None] * ROTATED
    for degree in range(levels):
        reach_order = min(degree, MAX_ORDER)
        span_cols = 2 * degree + 1
        first_row = wigner_start(degree)
        for position in range(2 * reach_order + 1):
            total = None
            for column in range(span_cols):
                row = first_row + position * span_cols + column
                term = wig[row : row + 1, :] * normed[degree * degree + column]
                total = term if total is None else total + term
            rotated[order_index(degree, position - reach_order)] = total.astype(jnp.bfloat16)

    spacing = CUTOFF / (basis_count - 1)
    centers = lax.broadcasted_iota(jnp.int32, (basis_count, num_edges), 0).astype(jnp.float32) * spacing
    basis_rows = jnp.exp(
        -0.5 * jnp.square((length_ref[...] - centers) / (2.0 * spacing))
    ).astype(jnp.bfloat16)
    hidden = jnp.dot(basis_in_ref[...], basis_rows, preferred_element_type=jnp.float32) + jnp.dot(
        kind_table_ref[...], kind_ref[...], preferred_element_type=jnp.float32
    )
    hidden = (hidden * jax.nn.sigmoid(hidden)).astype(jnp.bfloat16)
    radial = jnp.dot(radial_out_ref[...], hidden, preferred_element_type=jnp.float32)

    lowest = jnp.concatenate(
        [
            (rotated[degree].astype(jnp.float32) * radial[degree * channel_count : (degree + 1) * channel_count]).astype(
                jnp.bfloat16
            )
            for degree in range(levels)
        ],
        axis=0,
    )
    mixed0 = jnp.dot(zero_ref[...], lowest, preferred_element_type=jnp.float32)
    mixed = [mixed0[degree * channel_count : (degree + 1) * channel_count] for degree in range(levels)]
    first_row = levels
    for harmonic, weight_ref in ((1, one_ref), (2, two_ref)):
        span_rows = levels - harmonic
        plus_rows = jnp.concatenate(rotated[first_row : first_row + span_rows], axis=0)
        minus_rows = jnp.concatenate(rotated[first_row + span_rows : first_row + 2 * span_rows], axis=0)
        real_plus = jnp.dot(weight_ref[0], plus_rows, preferred_element_type=jnp.float32)
        real_minus = jnp.dot(weight_ref[0], minus_rows, preferred_element_type=jnp.float32)
        cross_plus = jnp.dot(weight_ref[1], plus_rows, preferred_element_type=jnp.float32)
        cross_minus = jnp.dot(weight_ref[1], minus_rows, preferred_element_type=jnp.float32)
        new_plus = real_plus - cross_minus
        new_minus = cross_plus + real_minus
        mixed += [new_plus[k * channel_count : (k + 1) * channel_count] for k in range(span_rows)]
        mixed += [new_minus[k * channel_count : (k + 1) * channel_count] for k in range(span_rows)]
        first_row = first_row + 2 * span_rows

    scalar = mixed[0]
    gate = jax.nn.sigmoid(scalar)
    gated = [(scalar * gate).astype(jnp.bfloat16).astype(jnp.float32)] + [
        (piece * gate).astype(jnp.bfloat16).astype(jnp.float32) for piece in mixed[1:]
    ]

    messages = []
    for degree in range(levels):
        reach_order = min(degree, MAX_ORDER)
        span_cols = 2 * degree + 1
        first_row = wigner_start(degree)
        for column in range(span_cols):
            total = None
            for position in range(2 * reach_order + 1):
                row = first_row + position * span_cols + column
                term = wig[row : row + 1, :] * gated[order_index(degree, position - reach_order)]
                total = term if total is None else total + term
            messages.append(total)
    stacked = jnp.concatenate(messages, axis=0)
    upper_part = stacked.astype(jnp.bfloat16)
    lower_part = (stacked - upper_part.astype(jnp.float32)).astype(jnp.bfloat16)
    onehot = onehot_ref[...]
    summed = jnp.dot(upper_part, onehot, preferred_element_type=jnp.float32) + jnp.dot(
        lower_part, onehot, preferred_element_type=jnp.float32
    )
    half = span_chan // 2
    pieces = [[] for _ in range(owners)]
    for degree in range(levels):
        weight = projection[degree]
        for j in range(degree * degree, (degree + 1) ** 2):
            piece = summed[j * channel_count : (j + 1) * channel_count]
            high = piece.astype(jnp.bfloat16)
            low = (piece - high.astype(jnp.float32)).astype(jnp.bfloat16)
            result = jnp.dot(weight, high, preferred_element_type=jnp.float32) + jnp.dot(
                weight, low, preferred_element_type=jnp.float32
            )
            for r in range(owners):
                block = result[r * span_chan : (r + 1) * span_chan]
                pieces[r].append(jnp.concatenate([block[:half], block[half:]], axis=1))
    fill = out_ref.shape[1] - COEFFS * half
    for r in range(owners):
        out_ref[r] = jnp.concatenate(
            pieces[r] + [jnp.zeros((fill, out_ref.shape[2]), jnp.float32)], axis=0
        ).astype(out_ref.dtype)


def convolve_edges(source, wig_mine, lengths, kind_onehot, radial_in, species_table, radial_out,
                   order_zero, order_one, order_two, onehot, per_owner):
    coeffs, channel_count = COEFFS, CHANNELS
    num_edges = per_owner
    atom_count = onehot.shape[1]
    owners = source.shape[0]
    out_rows = 16 * pl.cdiv(coeffs * (channel_count // owners) // 2, 16)
    operands = (
        source,
        wig_mine,
        lengths[None, :],
        kind_onehot,
        radial_in.T,
        species_table.T,
        radial_out.T,
        order_zero.T,
        jnp.transpose(order_one, (0, 2, 1)),
        jnp.transpose(order_two, (0, 2, 1)),
        onehot,
    )
    flops = 2 * num_edges * (order_zero.size + 2 * order_one.size + 2 * order_two.size + radial_out.size + radial_in.size)
    return pl.pallas_call(
        conv_kernel,
        out_shape=jax.ShapeDtypeStruct((owners, out_rows, 2 * atom_count), jnp.bfloat16),
        in_specs=[pl.BlockSpec(memory_space=pltpu.VMEM)] * len(operands),
        out_specs=pl.BlockSpec(memory_space=pltpu.VMEM),
        cost_estimate=pl.CostEstimate(
            flops=flops,
            transcendentals=num_edges * (radial_in.shape[0] + 2 * channel_count),
            bytes_accessed=sum(int(x.size) * x.dtype.itemsize for x in operands) + owners * out_rows * atom_count * 4,
        ),
    )(*operands)


def gather_kernel(index_ref, local_ref, arrived_ref, extra_ref, out_ref):
    owners, _, row_width = out_ref.shape
    per_owner = out_ref.shape[1] - extra_ref.shape[0]
    row_used = local_ref.shape[1]
    table = jnp.concatenate([local_ref[...], arrived_ref[...]], axis=0)
    hot = (
        index_ref[...] == lax.broadcasted_iota(jnp.int32, (index_ref.shape[0], table.shape[0]), 1)
    ).astype(jnp.bfloat16)
    picked = jnp.dot(hot, table, preferred_element_type=jnp.float32).astype(out_ref.dtype)
    blank = jnp.zeros((per_owner, row_width - row_used), out_ref.dtype)
    extra = extra_ref[...]
    for q in range(owners):
        out_ref[q, 0:per_owner, 0:row_used] = picked[q * per_owner : (q + 1) * per_owner]
        out_ref[q, 0:per_owner, row_used:row_width] = blank
        out_ref[q, per_owner:, :] = extra


def gather_rows(edge_source, node_rows, arrived, extra, owners, row_width):
    per_owner = edge_source.shape[0] // owners
    operands = (edge_source[:, None], node_rows, arrived, extra)
    return pl.pallas_call(
        gather_kernel,
        out_shape=jax.ShapeDtypeStruct((owners, per_owner + extra.shape[0], row_width), jnp.bfloat16),
        in_specs=[pl.BlockSpec(memory_space=pltpu.VMEM)] * len(operands),
        out_specs=pl.BlockSpec(memory_space=pltpu.VMEM),
        cost_estimate=pl.CostEstimate(
            flops=2 * edge_source.shape[0] * (node_rows.shape[0] + arrived.shape[0]) * node_rows.shape[1],
            transcendentals=0,
            bytes_accessed=sum(int(x.size) * x.dtype.itemsize for x in operands)
            + owners * (per_owner + extra.shape[0]) * row_width * 2,
        ),
    )(*operands)


def split_dot(values, weight):
    upper_part = values.astype(jnp.bfloat16)
    lower_part = (values - upper_part.astype(jnp.float32)).astype(jnp.bfloat16)
    return jnp.dot(upper_part, weight, preferred_element_type=jnp.float32) + jnp.dot(
        lower_part, weight, preferred_element_type=jnp.float32
    )


def body(
    node_feats,
    norm_gain,
    species,
    send_list,
    edge_source,
    edge_target,
    edge_count,
    edge_length,
    wigner,
    radial_in,
    species_table,
    radial_out,
    order_zero,
    order_one,
    order_two,
    project_weight,
):
    levels = MAX_DEGREE + 1
    owners = lax.axis_size("irreps")
    quarter = lax.axis_index("irreps")
    coeffs, span_chan, atom_count = node_feats.shape
    per_owner = edge_source.shape[0] // owners
    first_edge = quarter * per_owner

    row_used = coeffs * span_chan
    row_width = 128 * pl.cdiv(row_used, 128)
    node_rows = node_feats.reshape(row_used, atom_count).T
    arrived = lax.all_to_all(node_rows[send_list], "graph", 0, 0, tiled=True)

    gain_high = lax.reduce_precision(norm_gain, exponent_bits=8, mantissa_bits=7)
    gain_rest = norm_gain - gain_high
    gain_mid = lax.reduce_precision(gain_rest, exponent_bits=8, mantissa_bits=7)
    gain_low = gain_rest - gain_mid
    gain_block = jnp.transpose(jnp.stack([gain_high, gain_mid, gain_low]), (2, 0, 1))
    gain_block = jnp.pad(gain_block, ((0, 0), (0, 0), (0, 1))).reshape(span_chan, 3 * (levels + 1))
    gain_block = jnp.pad(gain_block, ((0, 0), (0, CHANNELS - gain_block.shape[1]))).astype(jnp.bfloat16)
    pair_order = np.concatenate([np.arange(0, span_chan, 2), np.arange(1, span_chan, 2)])
    weight_block = jnp.concatenate(
        [jnp.transpose(project_weight[:, :, pair_order], (2, 0, 1)), gain_block[:, None, :]], axis=1
    )
    extra = jnp.transpose(weight_block.reshape(span_chan, 2, 4, CHANNELS), (1, 0, 2, 3)).reshape(
        2 * span_chan, 4 * CHANNELS
    )

    outgoing = gather_rows(edge_source, node_rows, arrived, extra, owners, row_width)
    source = lax.all_to_all(outgoing, "irreps", 0, 0, tiled=True)

    wig_mine = lax.dynamic_slice_in_dim(wigner, first_edge, per_owner, 1)
    targets_mine = lax.dynamic_slice_in_dim(edge_target, first_edge, per_owner)
    lengths_mine = lax.dynamic_slice_in_dim(edge_length, first_edge, per_owner)
    kinds = species[targets_mine]
    kind_onehot = (
        kinds[None, :] == jnp.arange(species_table.shape[0], dtype=jnp.int32)[:, None]
    ).astype(jnp.bfloat16)
    edge_weight = jnp.where(
        first_edge + jnp.arange(per_owner, dtype=jnp.int32) < edge_count[0], 0.25, 0.0
    ).astype(jnp.float32)
    onehot = jnp.where(
        targets_mine[:, None] == jnp.arange(atom_count, dtype=jnp.int32)[None, :],
        edge_weight[:, None],
        0.0,
    ).astype(jnp.bfloat16)
    projected = convolve_edges(
        source, wig_mine, lengths_mine, kind_onehot, radial_in, species_table, radial_out,
        order_zero, order_one, order_two, onehot, per_owner,
    )
    returned = lax.all_to_all(projected, "irreps", 0, 0, tiled=True)
    total = jnp.sum(returned.astype(jnp.float32), axis=0)[: coeffs * span_chan // 2]
    total = total.reshape(coeffs, span_chan // 2, 2, atom_count).reshape(coeffs, span_chan, atom_count)
    return (node_feats.astype(jnp.float32) + total).astype(jnp.bfloat16)


def solution(mesh):
    return jax.shard_map(
        body,
        mesh=mesh,
        in_specs=(
            P(None, "irreps", "graph"),
            P(None, "irreps"),
            P("graph"),
            P("graph"),
            P("graph"),
            P("graph"),
            P("graph"),
            P("graph"),
            P(None, "graph"),
            P(),
            P(),
            P(),
            P(),
            P(),
            P(),
            P(None, None, "irreps"),
        ),
        out_specs=P(None, "irreps", "graph"),
        check_vma=False,
    )
```

```python
import jax
import jax.numpy as jnp
import numpy as np
from jax import lax
from jax.sharding import PartitionSpec as P
from jax.experimental import pallas as pl
from jax.experimental.pallas import tpu as pltpu

CHANNELS = 128
MAX_DEGREE = 6
MAX_ORDER = 2
ROTATED = 29
COEFFS = 49


EPSILON = 1e-06
CUTOFF = 6.0


def order_index(degree, harmonic):
    if harmonic == 0:
        return degree
    first_row = MAX_DEGREE + 1
    for level in range(1, abs(harmonic)):
        first_row = first_row + 2 * (MAX_DEGREE + 1 - level)
    if harmonic < 0:
        first_row = first_row + MAX_DEGREE + 1 - abs(harmonic)
    return first_row + degree - abs(harmonic)


def wigner_start(degree):
    running = 0
    for level in range(degree):
        running = running + (2 * min(level, MAX_ORDER) + 1) * (2 * level + 1)
    return running


def left_dot(weight, values):
    return lax.dot_general(
        weight, values, (((0,), (0,)), ((), ())), preferred_element_type=jnp.float32
    )


def degree_sums(squares):
    return jnp.stack(
        [
            jnp.sum(squares[degree * degree : (degree + 1) ** 2], axis=0)
            for degree in range(MAX_DEGREE + 1)
        ]
    )


def normalize(node_feats, norm_gain, totals):
    levels = MAX_DEGREE + 1
    degree_of = np.repeat(np.arange(levels), 2 * np.arange(levels) + 1)
    entry_counts = (2 * np.arange(levels) + 1) * CHANNELS
    inverse = 1.0 / jnp.sqrt(totals / jnp.asarray(entry_counts, jnp.float32)[:, None] + EPSILON)
    gain_rows = norm_gain[degree_of]
    scale_rows = inverse[degree_of]
    return (node_feats.astype(jnp.float32) * gain_rows[:, :, None] * scale_rows[:, None, :]).astype(
        jnp.bfloat16
    )


def normalize_rows(values, gain_full, totals):
    levels = MAX_DEGREE + 1
    degree_of = np.repeat(np.arange(levels), 2 * np.arange(levels) + 1)
    entry_counts = (2 * np.arange(levels) + 1) * CHANNELS
    inverse = 1.0 / jnp.sqrt(totals / jnp.asarray(entry_counts, jnp.float32)[:, None] + EPSILON)
    gain_rows = gain_full[degree_of]
    scale_rows = inverse[degree_of]
    return (values * gain_rows[:, :, None] * scale_rows[:, None, :]).astype(jnp.bfloat16)


def rotate(source, wig_rows):
    pieces = [None] * ROTATED
    for degree in range(MAX_DEGREE + 1):
        reach_order = min(degree, MAX_ORDER)
        span_cols = 2 * degree + 1
        first_row = wigner_start(degree)
        for position in range(2 * reach_order + 1):
            total = None
            for column in range(span_cols):
                term = wig_rows[first_row + position * span_cols + column][None, :] * source[degree * degree + column]
                total = term if total is None else total + term
            pieces[order_index(degree, position - reach_order)] = total
    return jnp.stack(pieces).astype(jnp.bfloat16)


def unrotate(gated, wig_rows):
    pieces = []
    for degree in range(MAX_DEGREE + 1):
        reach_order = min(degree, MAX_ORDER)
        span_cols = 2 * degree + 1
        first_row = wigner_start(degree)
        for column in range(span_cols):
            total = None
            for position in range(2 * reach_order + 1):
                term = wig_rows[first_row + position * span_cols + column][None, :] * gated[
                    order_index(degree, position - reach_order)
                ]
                total = term if total is None else total + term
            pieces.append(total)
    return jnp.stack(pieces)


def radial_weights(lengths, kind_ids, radial_in, species_table, radial_out):
    basis_count = radial_in.shape[0]
    spacing = CUTOFF / (basis_count - 1)
    centers = jnp.arange(basis_count, dtype=jnp.float32) * spacing
    basis_rows = jnp.exp(
        -0.5 * jnp.square((lengths[None, :] - centers[:, None]) / (2.0 * spacing))
    ).astype(jnp.bfloat16)
    onehot = (
        kind_ids[None, :] == jnp.arange(species_table.shape[0], dtype=jnp.int32)[:, None]
    ).astype(jnp.bfloat16)
    hidden = jax.nn.silu(left_dot(radial_in, basis_rows) + left_dot(species_table, onehot)).astype(
        jnp.bfloat16
    )
    return left_dot(radial_out, hidden)


def convolve(rotated, radial, order_zero, order_one, order_two):
    levels = MAX_DEGREE + 1
    channel_count = rotated.shape[1]
    num_edges = rotated.shape[2]
    lowest = (
        rotated[:levels].astype(jnp.float32).reshape(levels * channel_count, num_edges) * radial
    ).astype(jnp.bfloat16)
    outputs = [left_dot(order_zero, lowest).reshape(levels, channel_count, num_edges)]
    first_row = levels
    for harmonic, weight in ((1, order_one), (2, order_two)):
        span_rows = levels - harmonic
        plus_rows = rotated[first_row : first_row + span_rows].reshape(
            span_rows * channel_count, num_edges
        )
        minus_rows = rotated[first_row + span_rows : first_row + 2 * span_rows].reshape(
            span_rows * channel_count, num_edges
        )
        joined = jnp.concatenate([plus_rows, minus_rows], axis=1)
        real_part = left_dot(weight[0], joined)
        cross_part = left_dot(weight[1], joined)
        outputs.append(
            (real_part[:, :num_edges] - cross_part[:, num_edges:]).reshape(
                span_rows, channel_count, num_edges
            )
        )
        outputs.append(
            (cross_part[:, :num_edges] + real_part[:, num_edges:]).reshape(
                span_rows, channel_count, num_edges
            )
        )
        first_row = first_row + 2 * span_rows
    mixed = jnp.concatenate(outputs, axis=0)
    scalar = mixed[0]
    return jnp.concatenate(
        [jax.nn.silu(scalar)[None], mixed[1:] * jax.nn.sigmoid(scalar)[None]], axis=0
    ).astype(jnp.bfloat16)


def conv_kernel(
    src_ref, wig_ref, length_ref, kind_ref, basis_in_ref, kind_table_ref, radial_out_ref,
    zero_ref, one_ref, two_ref, onehot_ref, out_ref,
):
    levels = MAX_DEGREE + 1
    channel_count = CHANNELS
    num_edges = onehot_ref.shape[0]
    basis_count = basis_in_ref.shape[1]
    wig = wig_ref[...].astype(jnp.float32)
    owners = src_ref.shape[0]
    span_chan = CHANNELS // owners
    pick = (
        lax.broadcasted_iota(jnp.int32, (CHANNELS, span_chan), 0) % span_chan
        == lax.broadcasted_iota(jnp.int32, (CHANNELS, span_chan), 1)
    ) & (lax.broadcasted_iota(jnp.int32, (CHANNELS, span_chan), 0) < 3 * span_chan)
    pick = pick.astype(jnp.bfloat16)
    gain = jnp.concatenate(
        [
            jnp.dot(
                src_ref[r, num_edges + span_chan : num_edges + 2 * span_chan, 3 * CHANNELS : 4 * CHANNELS],
                pick,
                preferred_element_type=jnp.float32,
            )
            for r in range(owners)
        ],
        axis=0,
    )
    projection = [
        jnp.concatenate(
            [
                src_ref[
                    r,
                    num_edges + (degree // 4) * span_chan : num_edges + (degree // 4 + 1) * span_chan,
                    (degree % 4) * CHANNELS : (degree % 4 + 1) * CHANNELS,
                ].astype(jnp.float32)
                for r in range(owners)
            ],
            axis=0,
        ).astype(jnp.bfloat16)
        for degree in range(levels)
    ]

    turned = [src_ref[r, 0:num_edges].astype(jnp.float32).T for r in range(owners)]
    rows = [
        jnp.concatenate([block[j * span_chan : (j + 1) * span_chan] for block in turned], axis=0)
        for j in range(COEFFS)
    ]
    normed = [None] * len(rows)
    for degree in range(levels):
        span = range(degree * degree, (degree + 1) ** 2)
        total = None
        for j in span:
            part = jnp.sum(rows[j] * rows[j], axis=0, keepdims=True)
            total = part if total is None else total + part
        inverse = 1.0 / jnp.sqrt(total / float((2 * degree + 1) * CHANNELS) + EPSILON)
        scale = gain[:, degree : degree + 1]
        for j in span:
            normed[j] = (rows[j] * scale * inverse).astype(jnp.bfloat16).astype(jnp.float32)

    rotated = [None] * ROTATED
    for degree in range(levels):
        reach_order = min(degree, MAX_ORDER)
        span_cols = 2 * degree + 1
        first_row = wigner_start(degree)
        for position in range(2 * reach_order + 1):
            total = None
            for column in range(span_cols):
                row = first_row + position * span_cols + column
                term = wig[row : row + 1, :] * normed[degree * degree + column]
                total = term if total is None else total + term
            rotated[order_index(degree, position - reach_order)] = total.astype(jnp.bfloat16)

    spacing = CUTOFF / (basis_count - 1)
    centers = lax.broadcasted_iota(jnp.int32, (basis_count, num_edges), 0).astype(jnp.float32) * spacing
    basis_rows = jnp.exp(
        -0.5 * jnp.square((length_ref[...] - centers) / (2.0 * spacing))
    ).astype(jnp.bfloat16)
    hidden = jnp.dot(basis_in_ref[...], basis_rows, preferred_element_type=jnp.float32) + jnp.dot(
        kind_table_ref[...], kind_ref[...], preferred_element_type=jnp.float32
    )
    hidden = (hidden * jax.nn.sigmoid(hidden)).astype(jnp.bfloat16)
    radial = jnp.dot(radial_out_ref[...], hidden, preferred_element_type=jnp.float32)

    lowest = jnp.concatenate(
        [
            (rotated[degree].astype(jnp.float32) * radial[degree * channel_count : (degree + 1) * channel_count]).astype(
                jnp.bfloat16
            )
            for degree in range(levels)
        ],
        axis=0,
    )
    mixed0 = jnp.dot(zero_ref[...], lowest, preferred_element_type=jnp.float32)
    mixed = [mixed0[degree * channel_count : (degree + 1) * channel_count] for degree in range(levels)]
    first_row = levels
    for harmonic, weight_ref in ((1, one_ref), (2, two_ref)):
        span_rows = levels - harmonic
        plus_rows = jnp.concatenate(rotated[first_row : first_row + span_rows], axis=0)
        minus_rows = jnp.concatenate(rotated[first_row + span_rows : first_row + 2 * span_rows], axis=0)
        real_plus = jnp.dot(weight_ref[0], plus_rows, preferred_element_type=jnp.float32)
        real_minus = jnp.dot(weight_ref[0], minus_rows, preferred_element_type=jnp.float32)
        cross_plus = jnp.dot(weight_ref[1], plus_rows, preferred_element_type=jnp.float32)
        cross_minus = jnp.dot(weight_ref[1], minus_rows, preferred_element_type=jnp.float32)
        new_plus = real_plus - cross_minus
        new_minus = cross_plus + real_minus
        mixed += [new_plus[k * channel_count : (k + 1) * channel_count] for k in range(span_rows)]
        mixed += [new_minus[k * channel_count : (k + 1) * channel_count] for k in range(span_rows)]
        first_row = first_row + 2 * span_rows

    scalar = mixed[0]
    gate = jax.nn.sigmoid(scalar)
    gated = [(scalar * gate).astype(jnp.bfloat16).astype(jnp.float32)] + [
        (piece * gate).astype(jnp.bfloat16).astype(jnp.float32) for piece in mixed[1:]
    ]

    messages = []
    for degree in range(levels):
        reach_order = min(degree, MAX_ORDER)
        span_cols = 2 * degree + 1
        first_row = wigner_start(degree)
        for column in range(span_cols):
            total = None
            for position in range(2 * reach_order + 1):
                row = first_row + position * span_cols + column
                term = wig[row : row + 1, :] * gated[order_index(degree, position - reach_order)]
                total = term if total is None else total + term
            messages.append(total)
    stacked = jnp.concatenate(messages, axis=0)
    upper_part = stacked.astype(jnp.bfloat16)
    lower_part = (stacked - upper_part.astype(jnp.float32)).astype(jnp.bfloat16)
    onehot = onehot_ref[...]
    summed = jnp.dot(upper_part, onehot, preferred_element_type=jnp.float32) + jnp.dot(
        lower_part, onehot, preferred_element_type=jnp.float32
    )
    half = span_chan // 2
    pieces = [[] for _ in range(owners)]
    for degree in range(levels):
        weight = projection[degree]
        for j in range(degree * degree, (degree + 1) ** 2):
            piece = summed[j * channel_count : (j + 1) * channel_count]
            high = piece.astype(jnp.bfloat16)
            low = (piece - high.astype(jnp.float32)).astype(jnp.bfloat16)
            result = jnp.dot(weight, high, preferred_element_type=jnp.float32) + jnp.dot(
                weight, low, preferred_element_type=jnp.float32
            )
            for r in range(owners):
                block = result[r * span_chan : (r + 1) * span_chan]
                pieces[r].append(jnp.concatenate([block[:half], block[half:]], axis=1))
    fill = out_ref.shape[1] - COEFFS * half
    for r in range(owners):
        out_ref[r] = jnp.concatenate(
            pieces[r] + [jnp.zeros((fill, out_ref.shape[2]), jnp.float32)], axis=0
        ).astype(out_ref.dtype)


def edge_operands(wig_mine, lengths, kind_onehot, radial_in, species_table, radial_out,
                  order_zero, order_one, order_two, onehot):
    return (
        wig_mine,
        lengths[None, :],
        kind_onehot,
        radial_in.T,
        species_table.T,
        radial_out.T,
        order_zero.T,
        jnp.transpose(order_one, (0, 2, 1)),
        jnp.transpose(order_two, (0, 2, 1)),
        onehot,
    )


def convolve_edges(source, side):
    coeffs, channel_count = COEFFS, CHANNELS
    onehot = side[-1]
    num_edges, atom_count = onehot.shape
    owners = source.shape[0]
    out_rows = 16 * pl.cdiv(coeffs * (channel_count // owners) // 2, 16)
    operands = (source,) + tuple(side)
    radial_in, radial_out = side[4], side[6]
    order_zero, order_one, order_two = side[7], side[8], side[9]
    flops = 2 * num_edges * (order_zero.size + 2 * order_one.size + 2 * order_two.size + radial_out.size + radial_in.size)
    return pl.pallas_call(
        conv_kernel,
        out_shape=jax.ShapeDtypeStruct((owners, out_rows, 2 * atom_count), jnp.bfloat16),
        in_specs=[pl.BlockSpec(memory_space=pltpu.VMEM)] * len(operands),
        out_specs=pl.BlockSpec(memory_space=pltpu.VMEM),
        cost_estimate=pl.CostEstimate(
            flops=flops,
            transcendentals=num_edges * (radial_in.shape[1] + 2 * channel_count),
            bytes_accessed=sum(int(x.size) * x.dtype.itemsize for x in operands) + owners * out_rows * atom_count * 4,
        ),
    )(*operands)


def gather_kernel(index_ref, local_ref, arrived_ref, extra_ref, *refs):
    out_ref = refs[-1]
    owners, _, row_width = out_ref.shape
    per_owner = out_ref.shape[1] - extra_ref.shape[0]
    row_used = local_ref.shape[1]
    table = jnp.concatenate([local_ref[...], arrived_ref[...]], axis=0)
    hot = (
        index_ref[...] == lax.broadcasted_iota(jnp.int32, (index_ref.shape[0], table.shape[0]), 1)
    ).astype(jnp.bfloat16)
    picked = jnp.dot(hot, table, preferred_element_type=jnp.float32).astype(out_ref.dtype)
    blank = jnp.zeros((per_owner, row_width - row_used), out_ref.dtype)
    extra = extra_ref[...]
    for q in range(owners):
        out_ref[q, 0:per_owner, 0:row_used] = picked[q * per_owner : (q + 1) * per_owner]
        out_ref[q, 0:per_owner, row_used:row_width] = blank
        out_ref[q, per_owner:, :] = extra


def gather_rows(edge_source, node_rows, arrived, extra, owners, row_width, side):
    per_owner = edge_source.shape[0] // owners
    operands = (edge_source[:, None], node_rows, arrived, extra)
    return pl.pallas_call(
        gather_kernel,
        out_shape=jax.ShapeDtypeStruct((owners, per_owner + extra.shape[0], row_width), jnp.bfloat16),
        in_specs=[pl.BlockSpec(memory_space=pltpu.VMEM)] * len(operands)
        + [pl.BlockSpec(memory_space=pl.ANY)] * len(side),
        out_specs=pl.BlockSpec(memory_space=pltpu.VMEM),
        cost_estimate=pl.CostEstimate(
            flops=2 * edge_source.shape[0] * (node_rows.shape[0] + arrived.shape[0]) * node_rows.shape[1],
            transcendentals=0,
            bytes_accessed=sum(int(x.size) * x.dtype.itemsize for x in operands)
            + owners * (per_owner + extra.shape[0]) * row_width * 2,
        ),
    )(*operands, *side)


def split_dot(values, weight):
    upper_part = values.astype(jnp.bfloat16)
    lower_part = (values - upper_part.astype(jnp.float32)).astype(jnp.bfloat16)
    return jnp.dot(upper_part, weight, preferred_element_type=jnp.float32) + jnp.dot(
        lower_part, weight, preferred_element_type=jnp.float32
    )


def body(
    node_feats,
    norm_gain,
    species,
    send_list,
    edge_source,
    edge_target,
    edge_count,
    edge_length,
    wigner,
    radial_in,
    species_table,
    radial_out,
    order_zero,
    order_one,
    order_two,
    project_weight,
):
    levels = MAX_DEGREE + 1
    owners = lax.axis_size("irreps")
    quarter = lax.axis_index("irreps")
    coeffs, span_chan, atom_count = node_feats.shape
    per_owner = edge_source.shape[0] // owners
    first_edge = quarter * per_owner

    row_used = coeffs * span_chan
    row_width = 128 * pl.cdiv(row_used, 128)
    node_rows = node_feats.reshape(row_used, atom_count).T
    arrived = lax.all_to_all(node_rows[send_list], "graph", 0, 0, tiled=True)

    gain_high = lax.reduce_precision(norm_gain, exponent_bits=8, mantissa_bits=7)
    gain_rest = norm_gain - gain_high
    gain_mid = lax.reduce_precision(gain_rest, exponent_bits=8, mantissa_bits=7)
    gain_low = gain_rest - gain_mid
    gain_block = jnp.transpose(jnp.stack([gain_high, gain_mid, gain_low]), (2, 0, 1))
    gain_block = jnp.pad(gain_block, ((0, 0), (0, 0), (0, 1))).reshape(span_chan, 3 * (levels + 1))
    gain_block = jnp.pad(gain_block, ((0, 0), (0, CHANNELS - gain_block.shape[1]))).astype(jnp.bfloat16)
    pair_order = np.concatenate([np.arange(0, span_chan, 2), np.arange(1, span_chan, 2)])
    weight_block = jnp.concatenate(
        [jnp.transpose(project_weight[:, :, pair_order], (2, 0, 1)), gain_block[:, None, :]], axis=1
    )
    extra = jnp.transpose(weight_block.reshape(span_chan, 2, 4, CHANNELS), (1, 0, 2, 3)).reshape(
        2 * span_chan, 4 * CHANNELS
    )

    wig_mine = lax.dynamic_slice_in_dim(wigner, first_edge, per_owner, 1)
    targets_mine = lax.dynamic_slice_in_dim(edge_target, first_edge, per_owner)
    lengths_mine = lax.dynamic_slice_in_dim(edge_length, first_edge, per_owner)
    kinds = species[targets_mine]
    kind_onehot = (
        kinds[None, :] == jnp.arange(species_table.shape[0], dtype=jnp.int32)[:, None]
    ).astype(jnp.bfloat16)
    edge_weight = jnp.where(
        first_edge + jnp.arange(per_owner, dtype=jnp.int32) < edge_count[0], 0.25, 0.0
    ).astype(jnp.float32)
    onehot = jnp.where(
        targets_mine[:, None] == jnp.arange(atom_count, dtype=jnp.int32)[None, :],
        edge_weight[:, None],
        0.0,
    ).astype(jnp.bfloat16)
    side = edge_operands(
        wig_mine, lengths_mine, kind_onehot, radial_in, species_table, radial_out,
        order_zero, order_one, order_two, onehot,
    )
    outgoing = gather_rows(edge_source, node_rows, arrived, extra, owners, row_width, side)
    source = lax.all_to_all(outgoing, "irreps", 0, 0, tiled=True)
    projected = convolve_edges(source, side)
    returned = lax.all_to_all(projected, "irreps", 0, 0, tiled=True)
    total = jnp.sum(returned.astype(jnp.float32), axis=0)[: coeffs * span_chan // 2]
    total = total.reshape(coeffs, span_chan // 2, 2, atom_count).reshape(coeffs, span_chan, atom_count)
    return (node_feats.astype(jnp.float32) + total).astype(jnp.bfloat16)


def solution(mesh):
    return jax.shard_map(
        body,
        mesh=mesh,
        in_specs=(
            P(None, "irreps", "graph"),
            P(None, "irreps"),
            P("graph"),
            P("graph"),
            P("graph"),
            P("graph"),
            P("graph"),
            P("graph"),
            P(None, "graph"),
            P(),
            P(),
            P(),
            P(),
            P(),
            P(),
            P(None, None, "irreps"),
        ),
        out_specs=P(None, "irreps", "graph"),
        check_vma=False,
    )
```

```python
import jax
import jax.numpy as jnp
import numpy as np
from jax import lax
from jax.sharding import PartitionSpec as P
from jax.experimental import pallas as pl
from jax.experimental.pallas import tpu as pltpu

CHANNELS = 128
MAX_DEGREE = 6
MAX_ORDER = 2
ROTATED = 29
COEFFS = 49


EPSILON = 1e-06
CUTOFF = 6.0


def order_index(degree, harmonic):
    if harmonic == 0:
        return degree
    first_row = MAX_DEGREE + 1
    for level in range(1, abs(harmonic)):
        first_row = first_row + 2 * (MAX_DEGREE + 1 - level)
    if harmonic < 0:
        first_row = first_row + MAX_DEGREE + 1 - abs(harmonic)
    return first_row + degree - abs(harmonic)


def wigner_start(degree):
    running = 0
    for level in range(degree):
        running = running + (2 * min(level, MAX_ORDER) + 1) * (2 * level + 1)
    return running


def left_dot(weight, values):
    return lax.dot_general(
        weight, values, (((0,), (0,)), ((), ())), preferred_element_type=jnp.float32
    )


def degree_sums(squares):
    return jnp.stack(
        [
            jnp.sum(squares[degree * degree : (degree + 1) ** 2], axis=0)
            for degree in range(MAX_DEGREE + 1)
        ]
    )


def normalize(node_feats, norm_gain, totals):
    levels = MAX_DEGREE + 1
    degree_of = np.repeat(np.arange(levels), 2 * np.arange(levels) + 1)
    entry_counts = (2 * np.arange(levels) + 1) * CHANNELS
    inverse = 1.0 / jnp.sqrt(totals / jnp.asarray(entry_counts, jnp.float32)[:, None] + EPSILON)
    gain_rows = norm_gain[degree_of]
    scale_rows = inverse[degree_of]
    return (node_feats.astype(jnp.float32) * gain_rows[:, :, None] * scale_rows[:, None, :]).astype(
        jnp.bfloat16
    )


def normalize_rows(values, gain_full, totals):
    levels = MAX_DEGREE + 1
    degree_of = np.repeat(np.arange(levels), 2 * np.arange(levels) + 1)
    entry_counts = (2 * np.arange(levels) + 1) * CHANNELS
    inverse = 1.0 / jnp.sqrt(totals / jnp.asarray(entry_counts, jnp.float32)[:, None] + EPSILON)
    gain_rows = gain_full[degree_of]
    scale_rows = inverse[degree_of]
    return (values * gain_rows[:, :, None] * scale_rows[:, None, :]).astype(jnp.bfloat16)


def rotate(source, wig_rows):
    pieces = [None] * ROTATED
    for degree in range(MAX_DEGREE + 1):
        reach_order = min(degree, MAX_ORDER)
        span_cols = 2 * degree + 1
        first_row = wigner_start(degree)
        for position in range(2 * reach_order + 1):
            total = None
            for column in range(span_cols):
                term = wig_rows[first_row + position * span_cols + column][None, :] * source[degree * degree + column]
                total = term if total is None else total + term
            pieces[order_index(degree, position - reach_order)] = total
    return jnp.stack(pieces).astype(jnp.bfloat16)


def unrotate(gated, wig_rows):
    pieces = []
    for degree in range(MAX_DEGREE + 1):
        reach_order = min(degree, MAX_ORDER)
        span_cols = 2 * degree + 1
        first_row = wigner_start(degree)
        for column in range(span_cols):
            total = None
            for position in range(2 * reach_order + 1):
                term = wig_rows[first_row + position * span_cols + column][None, :] * gated[
                    order_index(degree, position - reach_order)
                ]
                total = term if total is None else total + term
            pieces.append(total)
    return jnp.stack(pieces)


def radial_weights(lengths, kind_ids, radial_in, species_table, radial_out):
    basis_count = radial_in.shape[0]
    spacing = CUTOFF / (basis_count - 1)
    centers = jnp.arange(basis_count, dtype=jnp.float32) * spacing
    basis_rows = jnp.exp(
        -0.5 * jnp.square((lengths[None, :] - centers[:, None]) / (2.0 * spacing))
    ).astype(jnp.bfloat16)
    onehot = (
        kind_ids[None, :] == jnp.arange(species_table.shape[0], dtype=jnp.int32)[:, None]
    ).astype(jnp.bfloat16)
    hidden = jax.nn.silu(left_dot(radial_in, basis_rows) + left_dot(species_table, onehot)).astype(
        jnp.bfloat16
    )
    return left_dot(radial_out, hidden)


def convolve(rotated, radial, order_zero, order_one, order_two):
    levels = MAX_DEGREE + 1
    channel_count = rotated.shape[1]
    num_edges = rotated.shape[2]
    lowest = (
        rotated[:levels].astype(jnp.float32).reshape(levels * channel_count, num_edges) * radial
    ).astype(jnp.bfloat16)
    outputs = [left_dot(order_zero, lowest).reshape(levels, channel_count, num_edges)]
    first_row = levels
    for harmonic, weight in ((1, order_one), (2, order_two)):
        span_rows = levels - harmonic
        plus_rows = rotated[first_row : first_row + span_rows].reshape(
            span_rows * channel_count, num_edges
        )
        minus_rows = rotated[first_row + span_rows : first_row + 2 * span_rows].reshape(
            span_rows * channel_count, num_edges
        )
        joined = jnp.concatenate([plus_rows, minus_rows], axis=1)
        real_part = left_dot(weight[0], joined)
        cross_part = left_dot(weight[1], joined)
        outputs.append(
            (real_part[:, :num_edges] - cross_part[:, num_edges:]).reshape(
                span_rows, channel_count, num_edges
            )
        )
        outputs.append(
            (cross_part[:, :num_edges] + real_part[:, num_edges:]).reshape(
                span_rows, channel_count, num_edges
            )
        )
        first_row = first_row + 2 * span_rows
    mixed = jnp.concatenate(outputs, axis=0)
    scalar = mixed[0]
    return jnp.concatenate(
        [jax.nn.silu(scalar)[None], mixed[1:] * jax.nn.sigmoid(scalar)[None]], axis=0
    ).astype(jnp.bfloat16)


def conv_kernel(
    src_ref, wig_ref, length_ref, kind_ref, basis_in_ref, kind_table_ref, radial_out_ref,
    zero_ref, one_ref, two_ref, onehot_ref, out_ref,
):
    levels = MAX_DEGREE + 1
    channel_count = CHANNELS
    num_edges = onehot_ref.shape[0]
    basis_count = basis_in_ref.shape[1]
    wig = wig_ref[...].astype(jnp.float32)
    owners = src_ref.shape[0]
    span_chan = CHANNELS // owners
    turned = [src_ref[r].astype(jnp.float32).T for r in range(owners)]
    base = COEFFS * span_chan
    half = num_edges
    pick = (
        lax.broadcasted_iota(jnp.int32, (half, span_chan), 0) % span_chan
        == lax.broadcasted_iota(jnp.int32, (half, span_chan), 1)
    ) & (lax.broadcasted_iota(jnp.int32, (half, span_chan), 0) < 3 * span_chan)
    pick = pick.astype(jnp.float32)
    gain_at = base + levels * 2 * span_chan
    gain = jnp.concatenate(
        [
            jnp.dot(block[gain_at : gain_at + span_chan], pick, preferred_element_type=jnp.float32)
            for block in turned
        ],
        axis=0,
    )
    projection = []
    for degree in range(levels):
        start = base + degree * 2 * span_chan
        projection.append(
            jnp.concatenate(
                [
                    jnp.concatenate(
                        [block[start : start + span_chan], block[start + span_chan : start + 2 * span_chan]],
                        axis=1,
                    )
                    for block in turned
                ],
                axis=0,
            ).astype(jnp.bfloat16)
        )

    rows = [
        jnp.concatenate([block[j * span_chan : (j + 1) * span_chan] for block in turned], axis=0)
        for j in range(COEFFS)
    ]
    normed = [None] * len(rows)
    for degree in range(levels):
        span = range(degree * degree, (degree + 1) ** 2)
        total = None
        for j in span:
            part = jnp.sum(rows[j] * rows[j], axis=0, keepdims=True)
            total = part if total is None else total + part
        inverse = 1.0 / jnp.sqrt(total / float((2 * degree + 1) * CHANNELS) + EPSILON)
        scale = gain[:, degree : degree + 1]
        for j in span:
            normed[j] = (rows[j] * scale * inverse).astype(jnp.bfloat16).astype(jnp.float32)

    rotated = [None] * ROTATED
    for degree in range(levels):
        reach_order = min(degree, MAX_ORDER)
        span_cols = 2 * degree + 1
        first_row = wigner_start(degree)
        for position in range(2 * reach_order + 1):
            total = None
            for column in range(span_cols):
                row = first_row + position * span_cols + column
                term = wig[row : row + 1, :] * normed[degree * degree + column]
                total = term if total is None else total + term
            rotated[order_index(degree, position - reach_order)] = total.astype(jnp.bfloat16)

    spacing = CUTOFF / (basis_count - 1)
    centers = lax.broadcasted_iota(jnp.int32, (basis_count, num_edges), 0).astype(jnp.float32) * spacing
    basis_rows = jnp.exp(
        -0.5 * jnp.square((length_ref[...] - centers) / (2.0 * spacing))
    ).astype(jnp.bfloat16)
    hidden = jnp.dot(basis_in_ref[...], basis_rows, preferred_element_type=jnp.float32) + jnp.dot(
        kind_table_ref[...], kind_ref[...], preferred_element_type=jnp.float32
    )
    hidden = (hidden * jax.nn.sigmoid(hidden)).astype(jnp.bfloat16)
    radial = jnp.dot(radial_out_ref[...], hidden, preferred_element_type=jnp.float32)

    lowest = jnp.concatenate(
        [
            (rotated[degree].astype(jnp.float32) * radial[degree * channel_count : (degree + 1) * channel_count]).astype(
                jnp.bfloat16
            )
            for degree in range(levels)
        ],
        axis=0,
    )
    mixed0 = jnp.dot(zero_ref[...], lowest, preferred_element_type=jnp.float32)
    mixed = [mixed0[degree * channel_count : (degree + 1) * channel_count] for degree in range(levels)]
    first_row = levels
    for harmonic, weight_ref in ((1, one_ref), (2, two_ref)):
        span_rows = levels - harmonic
        plus_rows = jnp.concatenate(rotated[first_row : first_row + span_rows], axis=0)
        minus_rows = jnp.concatenate(rotated[first_row + span_rows : first_row + 2 * span_rows], axis=0)
        real_plus = jnp.dot(weight_ref[0], plus_rows, preferred_element_type=jnp.float32)
        real_minus = jnp.dot(weight_ref[0], minus_rows, preferred_element_type=jnp.float32)
        cross_plus = jnp.dot(weight_ref[1], plus_rows, preferred_element_type=jnp.float32)
        cross_minus = jnp.dot(weight_ref[1], minus_rows, preferred_element_type=jnp.float32)
        new_plus = real_plus - cross_minus
        new_minus = cross_plus + real_minus
        mixed += [new_plus[k * channel_count : (k + 1) * channel_count] for k in range(span_rows)]
        mixed += [new_minus[k * channel_count : (k + 1) * channel_count] for k in range(span_rows)]
        first_row = first_row + 2 * span_rows

    scalar = mixed[0]
    gate = jax.nn.sigmoid(scalar)
    gated = [(scalar * gate).astype(jnp.bfloat16).astype(jnp.float32)] + [
        (piece * gate).astype(jnp.bfloat16).astype(jnp.float32) for piece in mixed[1:]
    ]

    messages = []
    for degree in range(levels):
        reach_order = min(degree, MAX_ORDER)
        span_cols = 2 * degree + 1
        first_row = wigner_start(degree)
        for column in range(span_cols):
            total = None
            for position in range(2 * reach_order + 1):
                row = first_row + position * span_cols + column
                term = wig[row : row + 1, :] * gated[order_index(degree, position - reach_order)]
                total = term if total is None else total + term
            messages.append(total)
    stacked = jnp.concatenate(messages, axis=0)
    upper_part = stacked.astype(jnp.bfloat16)
    lower_part = (stacked - upper_part.astype(jnp.float32)).astype(jnp.bfloat16)
    onehot = onehot_ref[...]
    summed = jnp.dot(upper_part, onehot, preferred_element_type=jnp.float32) + jnp.dot(
        lower_part, onehot, preferred_element_type=jnp.float32
    )
    half = span_chan // 2
    pieces = [[] for _ in range(owners)]
    for degree in range(levels):
        weight = projection[degree]
        for j in range(degree * degree, (degree + 1) ** 2):
            piece = summed[j * channel_count : (j + 1) * channel_count]
            high = piece.astype(jnp.bfloat16)
            low = (piece - high.astype(jnp.float32)).astype(jnp.bfloat16)
            result = jnp.dot(weight, high, preferred_element_type=jnp.float32) + jnp.dot(
                weight, low, preferred_element_type=jnp.float32
            )
            for r in range(owners):
                block = result[r * span_chan : (r + 1) * span_chan]
                pieces[r].append(jnp.concatenate([block[:half], block[half:]], axis=1))
    fill = out_ref.shape[1] - COEFFS * half
    for r in range(owners):
        out_ref[r] = jnp.concatenate(
            pieces[r] + [jnp.zeros((fill, out_ref.shape[2]), jnp.float32)], axis=0
        ).astype(out_ref.dtype)


def edge_operands(wig_mine, lengths, kind_onehot, radial_in, species_table, radial_out,
                  order_zero, order_one, order_two, onehot):
    return (
        wig_mine,
        lengths[None, :],
        kind_onehot,
        radial_in.T,
        species_table.T,
        radial_out.T,
        order_zero.T,
        jnp.transpose(order_one, (0, 2, 1)),
        jnp.transpose(order_two, (0, 2, 1)),
        onehot,
    )


def convolve_edges(source, side):
    coeffs, channel_count = COEFFS, CHANNELS
    onehot = side[-1]
    num_edges, atom_count = onehot.shape
    owners = source.shape[0]
    out_rows = 16 * pl.cdiv(coeffs * (channel_count // owners) // 2, 16)
    operands = (source,) + tuple(side)
    radial_in, radial_out = side[4], side[6]
    order_zero, order_one, order_two = side[7], side[8], side[9]
    flops = 2 * num_edges * (order_zero.size + 2 * order_one.size + 2 * order_two.size + radial_out.size + radial_in.size)
    return pl.pallas_call(
        conv_kernel,
        out_shape=jax.ShapeDtypeStruct((owners, out_rows, 2 * atom_count), jnp.bfloat16),
        in_specs=[pl.BlockSpec(memory_space=pltpu.VMEM)] * len(operands),
        out_specs=pl.BlockSpec(memory_space=pltpu.VMEM),
        cost_estimate=pl.CostEstimate(
            flops=flops,
            transcendentals=num_edges * (radial_in.shape[1] + 2 * channel_count),
            bytes_accessed=sum(int(x.size) * x.dtype.itemsize for x in operands) + owners * out_rows * atom_count * 4,
        ),
    )(*operands)


def gather_kernel(index_ref, local_ref, arrived_ref, extra_ref, *refs):
    out_ref = refs[-1]
    owners, per_owner, row_width = out_ref.shape
    row_used = local_ref.shape[1]
    table = jnp.concatenate([local_ref[...], arrived_ref[...]], axis=0)
    hot = (
        index_ref[...] == lax.broadcasted_iota(jnp.int32, (index_ref.shape[0], table.shape[0]), 1)
    ).astype(jnp.bfloat16)
    picked = jnp.dot(hot, table, preferred_element_type=jnp.float32).astype(out_ref.dtype)
    extra = extra_ref[...]
    for q in range(owners):
        out_ref[q, :, 0:row_used] = picked[q * per_owner : (q + 1) * per_owner]
        out_ref[q, :, row_used:row_width] = extra


def gather_rows(edge_source, node_rows, arrived, extra, owners, row_width, side):
    per_owner = edge_source.shape[0] // owners
    operands = (edge_source[:, None], node_rows, arrived, extra)
    return pl.pallas_call(
        gather_kernel,
        out_shape=jax.ShapeDtypeStruct((owners, per_owner, row_width), jnp.bfloat16),
        in_specs=[pl.BlockSpec(memory_space=pltpu.VMEM)] * len(operands)
        + [pl.BlockSpec(memory_space=pl.ANY)] * len(side),
        out_specs=pl.BlockSpec(memory_space=pltpu.VMEM),
        cost_estimate=pl.CostEstimate(
            flops=2 * edge_source.shape[0] * (node_rows.shape[0] + arrived.shape[0]) * node_rows.shape[1],
            transcendentals=0,
            bytes_accessed=sum(int(x.size) * x.dtype.itemsize for x in operands)
            + owners * per_owner * row_width * 2,
        ),
    )(*operands, *side)


def split_dot(values, weight):
    upper_part = values.astype(jnp.bfloat16)
    lower_part = (values - upper_part.astype(jnp.float32)).astype(jnp.bfloat16)
    return jnp.dot(upper_part, weight, preferred_element_type=jnp.float32) + jnp.dot(
        lower_part, weight, preferred_element_type=jnp.float32
    )


def body(
    node_feats,
    norm_gain,
    species,
    send_list,
    edge_source,
    edge_target,
    edge_count,
    edge_length,
    wigner,
    radial_in,
    species_table,
    radial_out,
    order_zero,
    order_one,
    order_two,
    project_weight,
):
    levels = MAX_DEGREE + 1
    owners = lax.axis_size("irreps")
    quarter = lax.axis_index("irreps")
    coeffs, span_chan, atom_count = node_feats.shape
    per_owner = edge_source.shape[0] // owners
    first_edge = quarter * per_owner

    row_used = coeffs * span_chan
    row_width = 128 * pl.cdiv(row_used, 128)
    node_rows = node_feats.reshape(row_used, atom_count).T
    arrived = lax.all_to_all(node_rows[send_list], "graph", 0, 0, tiled=True)

    gain_high = lax.reduce_precision(norm_gain, exponent_bits=8, mantissa_bits=7)
    gain_rest = norm_gain - gain_high
    gain_mid = lax.reduce_precision(gain_rest, exponent_bits=8, mantissa_bits=7)
    gain_low = gain_rest - gain_mid
    gain_block = jnp.transpose(jnp.stack([gain_high, gain_mid, gain_low]), (2, 0, 1))
    gain_block = jnp.pad(gain_block, ((0, 0), (0, 0), (0, 1))).reshape(span_chan, 3 * (levels + 1))
    gain_block = jnp.pad(gain_block, ((0, 0), (0, per_owner - gain_block.shape[1]))).astype(jnp.bfloat16)
    pair_order = np.concatenate([np.arange(0, span_chan, 2), np.arange(1, span_chan, 2)])
    weight_block = jnp.transpose(
        project_weight[:, :, pair_order].reshape(levels, CHANNELS // per_owner, per_owner, span_chan), (0, 1, 3, 2)
    ).reshape(-1, per_owner)
    extra = jnp.concatenate([weight_block, gain_block], axis=0).T

    wig_mine = lax.dynamic_slice_in_dim(wigner, first_edge, per_owner, 1)
    targets_mine = lax.dynamic_slice_in_dim(edge_target, first_edge, per_owner)
    lengths_mine = lax.dynamic_slice_in_dim(edge_length, first_edge, per_owner)
    kinds = species[targets_mine]
    kind_onehot = (
        kinds[None, :] == jnp.arange(species_table.shape[0], dtype=jnp.int32)[:, None]
    ).astype(jnp.bfloat16)
    edge_weight = jnp.where(
        first_edge + jnp.arange(per_owner, dtype=jnp.int32) < edge_count[0], 0.25, 0.0
    ).astype(jnp.float32)
    onehot = jnp.where(
        targets_mine[:, None] == jnp.arange(atom_count, dtype=jnp.int32)[None, :],
        edge_weight[:, None],
        0.0,
    ).astype(jnp.bfloat16)
    side = edge_operands(
        wig_mine, lengths_mine, kind_onehot, radial_in, species_table, radial_out,
        order_zero, order_one, order_two, onehot,
    )
    outgoing = gather_rows(edge_source, node_rows, arrived, extra, owners, row_width, side)
    source = lax.all_to_all(outgoing, "irreps", 0, 0, tiled=True)
    projected = convolve_edges(source, side)
    returned = lax.all_to_all(projected, "irreps", 0, 0, tiled=True)
    total = jnp.sum(returned.astype(jnp.float32), axis=0)[: coeffs * span_chan // 2]
    total = total.reshape(coeffs, span_chan // 2, 2, atom_count).reshape(coeffs, span_chan, atom_count)
    return (node_feats.astype(jnp.float32) + total).astype(jnp.bfloat16)


def solution(mesh):
    return jax.shard_map(
        body,
        mesh=mesh,
        in_specs=(
            P(None, "irreps", "graph"),
            P(None, "irreps"),
            P("graph"),
            P("graph"),
            P("graph"),
            P("graph"),
            P("graph"),
            P("graph"),
            P(None, "graph"),
            P(),
            P(),
            P(),
            P(),
            P(),
            P(),
            P(None, None, "irreps"),
        ),
        out_specs=P(None, "irreps", "graph"),
        check_vma=False,
    )
```

```python
import jax
import jax.numpy as jnp
import numpy as np
from jax import lax
from jax.sharding import PartitionSpec as P
from jax.experimental import pallas as pl
from jax.experimental.pallas import tpu as pltpu

CHANNELS = 128
MAX_DEGREE = 6
MAX_ORDER = 2
ROTATED = 29
COEFFS = 49


EPSILON = 1e-06
CUTOFF = 6.0


def order_index(degree, harmonic):
    if harmonic == 0:
        return degree
    first_row = MAX_DEGREE + 1
    for level in range(1, abs(harmonic)):
        first_row = first_row + 2 * (MAX_DEGREE + 1 - level)
    if harmonic < 0:
        first_row = first_row + MAX_DEGREE + 1 - abs(harmonic)
    return first_row + degree - abs(harmonic)


def wigner_start(degree):
    running = 0
    for level in range(degree):
        running = running + (2 * min(level, MAX_ORDER) + 1) * (2 * level + 1)
    return running


def left_dot(weight, values):
    return lax.dot_general(
        weight, values, (((0,), (0,)), ((), ())), preferred_element_type=jnp.float32
    )


def degree_sums(squares):
    return jnp.stack(
        [
            jnp.sum(squares[degree * degree : (degree + 1) ** 2], axis=0)
            for degree in range(MAX_DEGREE + 1)
        ]
    )


def normalize(node_feats, norm_gain, totals):
    levels = MAX_DEGREE + 1
    degree_of = np.repeat(np.arange(levels), 2 * np.arange(levels) + 1)
    entry_counts = (2 * np.arange(levels) + 1) * CHANNELS
    inverse = 1.0 / jnp.sqrt(totals / jnp.asarray(entry_counts, jnp.float32)[:, None] + EPSILON)
    gain_rows = norm_gain[degree_of]
    scale_rows = inverse[degree_of]
    return (node_feats.astype(jnp.float32) * gain_rows[:, :, None] * scale_rows[:, None, :]).astype(
        jnp.bfloat16
    )


def normalize_rows(values, gain_full, totals):
    levels = MAX_DEGREE + 1
    degree_of = np.repeat(np.arange(levels), 2 * np.arange(levels) + 1)
    entry_counts = (2 * np.arange(levels) + 1) * CHANNELS
    inverse = 1.0 / jnp.sqrt(totals / jnp.asarray(entry_counts, jnp.float32)[:, None] + EPSILON)
    gain_rows = gain_full[degree_of]
    scale_rows = inverse[degree_of]
    return (values * gain_rows[:, :, None] * scale_rows[:, None, :]).astype(jnp.bfloat16)


def rotate(source, wig_rows):
    pieces = [None] * ROTATED
    for degree in range(MAX_DEGREE + 1):
        reach_order = min(degree, MAX_ORDER)
        span_cols = 2 * degree + 1
        first_row = wigner_start(degree)
        for position in range(2 * reach_order + 1):
            total = None
            for column in range(span_cols):
                term = wig_rows[first_row + position * span_cols + column][None, :] * source[degree * degree + column]
                total = term if total is None else total + term
            pieces[order_index(degree, position - reach_order)] = total
    return jnp.stack(pieces).astype(jnp.bfloat16)


def unrotate(gated, wig_rows):
    pieces = []
    for degree in range(MAX_DEGREE + 1):
        reach_order = min(degree, MAX_ORDER)
        span_cols = 2 * degree + 1
        first_row = wigner_start(degree)
        for column in range(span_cols):
            total = None
            for position in range(2 * reach_order + 1):
                term = wig_rows[first_row + position * span_cols + column][None, :] * gated[
                    order_index(degree, position - reach_order)
                ]
                total = term if total is None else total + term
            pieces.append(total)
    return jnp.stack(pieces)


def radial_weights(lengths, kind_ids, radial_in, species_table, radial_out):
    basis_count = radial_in.shape[0]
    spacing = CUTOFF / (basis_count - 1)
    centers = jnp.arange(basis_count, dtype=jnp.float32) * spacing
    basis_rows = jnp.exp(
        -0.5 * jnp.square((lengths[None, :] - centers[:, None]) / (2.0 * spacing))
    ).astype(jnp.bfloat16)
    onehot = (
        kind_ids[None, :] == jnp.arange(species_table.shape[0], dtype=jnp.int32)[:, None]
    ).astype(jnp.bfloat16)
    hidden = jax.nn.silu(left_dot(radial_in, basis_rows) + left_dot(species_table, onehot)).astype(
        jnp.bfloat16
    )
    return left_dot(radial_out, hidden)


def convolve(rotated, radial, order_zero, order_one, order_two):
    levels = MAX_DEGREE + 1
    channel_count = rotated.shape[1]
    num_edges = rotated.shape[2]
    lowest = (
        rotated[:levels].astype(jnp.float32).reshape(levels * channel_count, num_edges) * radial
    ).astype(jnp.bfloat16)
    outputs = [left_dot(order_zero, lowest).reshape(levels, channel_count, num_edges)]
    first_row = levels
    for harmonic, weight in ((1, order_one), (2, order_two)):
        span_rows = levels - harmonic
        plus_rows = rotated[first_row : first_row + span_rows].reshape(
            span_rows * channel_count, num_edges
        )
        minus_rows = rotated[first_row + span_rows : first_row + 2 * span_rows].reshape(
            span_rows * channel_count, num_edges
        )
        joined = jnp.concatenate([plus_rows, minus_rows], axis=1)
        real_part = left_dot(weight[0], joined)
        cross_part = left_dot(weight[1], joined)
        outputs.append(
            (real_part[:, :num_edges] - cross_part[:, num_edges:]).reshape(
                span_rows, channel_count, num_edges
            )
        )
        outputs.append(
            (cross_part[:, :num_edges] + real_part[:, num_edges:]).reshape(
                span_rows, channel_count, num_edges
            )
        )
        first_row = first_row + 2 * span_rows
    mixed = jnp.concatenate(outputs, axis=0)
    scalar = mixed[0]
    return jnp.concatenate(
        [jax.nn.silu(scalar)[None], mixed[1:] * jax.nn.sigmoid(scalar)[None]], axis=0
    ).astype(jnp.bfloat16)


def conv_kernel(
    src_ref, wig_ref, length_ref, kind_ref, basis_in_ref, kind_table_ref, radial_out_ref,
    zero_hbm, one_hbm, two_hbm, onehot_ref, out_ref, zero_ref, one_ref, two_ref, copy_sems,
):
    loads = [
        pltpu.make_async_copy(zero_hbm, zero_ref, copy_sems.at[0]),
        pltpu.make_async_copy(one_hbm, one_ref, copy_sems.at[1]),
        pltpu.make_async_copy(two_hbm, two_ref, copy_sems.at[2]),
    ]
    for load in loads:
        load.start()
    levels = MAX_DEGREE + 1
    channel_count = CHANNELS
    num_edges = onehot_ref.shape[0]
    basis_count = basis_in_ref.shape[1]
    wig = wig_ref[...].astype(jnp.float32)
    owners = src_ref.shape[0]
    span_chan = CHANNELS // owners
    turned = [src_ref[r].astype(jnp.float32).T for r in range(owners)]
    base = COEFFS * span_chan
    half = num_edges
    pick = (
        lax.broadcasted_iota(jnp.int32, (half, span_chan), 0) % span_chan
        == lax.broadcasted_iota(jnp.int32, (half, span_chan), 1)
    ) & (lax.broadcasted_iota(jnp.int32, (half, span_chan), 0) < 3 * span_chan)
    pick = pick.astype(jnp.float32)
    gain_at = base + levels * 2 * span_chan
    gain = jnp.concatenate(
        [
            jnp.dot(block[gain_at : gain_at + span_chan], pick, preferred_element_type=jnp.float32)
            for block in turned
        ],
        axis=0,
    )
    projection = []
    for degree in range(levels):
        start = base + degree * 2 * span_chan
        projection.append(
            jnp.concatenate(
                [
                    jnp.concatenate(
                        [block[start : start + span_chan], block[start + span_chan : start + 2 * span_chan]],
                        axis=1,
                    )
                    for block in turned
                ],
                axis=0,
            ).astype(jnp.bfloat16)
        )

    rows = [
        jnp.concatenate([block[j * span_chan : (j + 1) * span_chan] for block in turned], axis=0)
        for j in range(COEFFS)
    ]
    normed = [None] * len(rows)
    for degree in range(levels):
        span = range(degree * degree, (degree + 1) ** 2)
        total = None
        for j in span:
            part = jnp.sum(rows[j] * rows[j], axis=0, keepdims=True)
            total = part if total is None else total + part
        inverse = 1.0 / jnp.sqrt(total / float((2 * degree + 1) * CHANNELS) + EPSILON)
        scale = gain[:, degree : degree + 1]
        for j in span:
            normed[j] = (rows[j] * scale * inverse).astype(jnp.bfloat16).astype(jnp.float32)

    rotated = [None] * ROTATED
    for degree in range(levels):
        reach_order = min(degree, MAX_ORDER)
        span_cols = 2 * degree + 1
        first_row = wigner_start(degree)
        for position in range(2 * reach_order + 1):
            total = None
            for column in range(span_cols):
                row = first_row + position * span_cols + column
                term = wig[row : row + 1, :] * normed[degree * degree + column]
                total = term if total is None else total + term
            rotated[order_index(degree, position - reach_order)] = total.astype(jnp.bfloat16)

    spacing = CUTOFF / (basis_count - 1)
    centers = lax.broadcasted_iota(jnp.int32, (basis_count, num_edges), 0).astype(jnp.float32) * spacing
    basis_rows = jnp.exp(
        -0.5 * jnp.square((length_ref[...] - centers) / (2.0 * spacing))
    ).astype(jnp.bfloat16)
    hidden = jnp.dot(basis_in_ref[...], basis_rows, preferred_element_type=jnp.float32) + jnp.dot(
        kind_table_ref[...], kind_ref[...], preferred_element_type=jnp.float32
    )
    hidden = (hidden * jax.nn.sigmoid(hidden)).astype(jnp.bfloat16)
    radial = jnp.dot(radial_out_ref[...], hidden, preferred_element_type=jnp.float32)

    lowest = jnp.concatenate(
        [
            (rotated[degree].astype(jnp.float32) * radial[degree * channel_count : (degree + 1) * channel_count]).astype(
                jnp.bfloat16
            )
            for degree in range(levels)
        ],
        axis=0,
    )
    loads[0].wait()
    mixed0 = jnp.dot(zero_ref[...], lowest, preferred_element_type=jnp.float32)
    mixed = [mixed0[degree * channel_count : (degree + 1) * channel_count] for degree in range(levels)]
    first_row = levels
    for harmonic, weight_ref, load in ((1, one_ref, loads[1]), (2, two_ref, loads[2])):
        load.wait()
        span_rows = levels - harmonic
        plus_rows = jnp.concatenate(rotated[first_row : first_row + span_rows], axis=0)
        minus_rows = jnp.concatenate(rotated[first_row + span_rows : first_row + 2 * span_rows], axis=0)
        real_plus = jnp.dot(weight_ref[0], plus_rows, preferred_element_type=jnp.float32)
        real_minus = jnp.dot(weight_ref[0], minus_rows, preferred_element_type=jnp.float32)
        cross_plus = jnp.dot(weight_ref[1], plus_rows, preferred_element_type=jnp.float32)
        cross_minus = jnp.dot(weight_ref[1], minus_rows, preferred_element_type=jnp.float32)
        new_plus = real_plus - cross_minus
        new_minus = cross_plus + real_minus
        mixed += [new_plus[k * channel_count : (k + 1) * channel_count] for k in range(span_rows)]
        mixed += [new_minus[k * channel_count : (k + 1) * channel_count] for k in range(span_rows)]
        first_row = first_row + 2 * span_rows

    scalar = mixed[0]
    gate = jax.nn.sigmoid(scalar)
    gated = [(scalar * gate).astype(jnp.bfloat16).astype(jnp.float32)] + [
        (piece * gate).astype(jnp.bfloat16).astype(jnp.float32) for piece in mixed[1:]
    ]

    messages = []
    for degree in range(levels):
        reach_order = min(degree, MAX_ORDER)
        span_cols = 2 * degree + 1
        first_row = wigner_start(degree)
        for column in range(span_cols):
            total = None
            for position in range(2 * reach_order + 1):
                row = first_row + position * span_cols + column
                term = wig[row : row + 1, :] * gated[order_index(degree, position - reach_order)]
                total = term if total is None else total + term
            messages.append(total)
    stacked = jnp.concatenate(messages, axis=0)
    upper_part = stacked.astype(jnp.bfloat16)
    lower_part = (stacked - upper_part.astype(jnp.float32)).astype(jnp.bfloat16)
    onehot = onehot_ref[...]
    summed = jnp.dot(upper_part, onehot, preferred_element_type=jnp.float32) + jnp.dot(
        lower_part, onehot, preferred_element_type=jnp.float32
    )
    half = span_chan // 2
    pieces = [[] for _ in range(owners)]
    for degree in range(levels):
        weight = projection[degree]
        for j in range(degree * degree, (degree + 1) ** 2):
            piece = summed[j * channel_count : (j + 1) * channel_count]
            high = piece.astype(jnp.bfloat16)
            low = (piece - high.astype(jnp.float32)).astype(jnp.bfloat16)
            result = jnp.dot(weight, high, preferred_element_type=jnp.float32) + jnp.dot(
                weight, low, preferred_element_type=jnp.float32
            )
            for r in range(owners):
                block = result[r * span_chan : (r + 1) * span_chan]
                pieces[r].append(jnp.concatenate([block[:half], block[half:]], axis=1))
    fill = out_ref.shape[1] - COEFFS * half
    for r in range(owners):
        out_ref[r] = jnp.concatenate(
            pieces[r] + [jnp.zeros((fill, out_ref.shape[2]), jnp.float32)], axis=0
        ).astype(out_ref.dtype)


def edge_operands(wig_mine, lengths, kind_onehot, radial_in, species_table, radial_out,
                  order_zero, order_one, order_two, onehot):
    return (
        wig_mine,
        lengths[None, :],
        kind_onehot,
        radial_in.T,
        species_table.T,
        radial_out.T,
        order_zero.T,
        jnp.transpose(order_one, (0, 2, 1)),
        jnp.transpose(order_two, (0, 2, 1)),
        onehot,
    )


def convolve_edges(source, side):
    coeffs, channel_count = COEFFS, CHANNELS
    onehot = side[-1]
    num_edges, atom_count = onehot.shape
    owners = source.shape[0]
    out_rows = 16 * pl.cdiv(coeffs * (channel_count // owners) // 2, 16)
    operands = (source,) + tuple(side)
    radial_in, radial_out = side[3], side[5]
    order_zero, order_one, order_two = side[6], side[7], side[8]
    flops = 2 * num_edges * (order_zero.size + 2 * order_one.size + 2 * order_two.size + radial_out.size + radial_in.size)
    return pl.pallas_call(
        conv_kernel,
        out_shape=jax.ShapeDtypeStruct((owners, out_rows, 2 * atom_count), jnp.bfloat16),
        in_specs=[pl.BlockSpec(memory_space=pltpu.VMEM)] * 7
        + [pl.BlockSpec(memory_space=pl.ANY)] * 3
        + [pl.BlockSpec(memory_space=pltpu.VMEM)],
        out_specs=pl.BlockSpec(memory_space=pltpu.VMEM),
        scratch_shapes=[
            pltpu.VMEM(order_zero.shape, order_zero.dtype),
            pltpu.VMEM(order_one.shape, order_one.dtype),
            pltpu.VMEM(order_two.shape, order_two.dtype),
            pltpu.SemaphoreType.DMA((3,)),
        ],
        cost_estimate=pl.CostEstimate(
            flops=flops,
            transcendentals=num_edges * (radial_in.shape[1] + 2 * channel_count),
            bytes_accessed=sum(int(x.size) * x.dtype.itemsize for x in operands) + owners * out_rows * atom_count * 4,
        ),
    )(*operands)


def gather_kernel(index_ref, local_ref, arrived_ref, extra_ref, *refs):
    out_ref = refs[-1]
    owners, per_owner, row_width = out_ref.shape
    row_used = local_ref.shape[1]
    table = jnp.concatenate([local_ref[...], arrived_ref[...]], axis=0)
    hot = (
        index_ref[...] == lax.broadcasted_iota(jnp.int32, (index_ref.shape[0], table.shape[0]), 1)
    ).astype(jnp.bfloat16)
    picked = jnp.dot(hot, table, preferred_element_type=jnp.float32).astype(out_ref.dtype)
    extra = extra_ref[...]
    for q in range(owners):
        out_ref[q, :, 0:row_used] = picked[q * per_owner : (q + 1) * per_owner]
        out_ref[q, :, row_used:row_width] = extra


def gather_rows(edge_source, node_rows, arrived, extra, owners, row_width, side):
    per_owner = edge_source.shape[0] // owners
    operands = (edge_source[:, None], node_rows, arrived, extra)
    return pl.pallas_call(
        gather_kernel,
        out_shape=jax.ShapeDtypeStruct((owners, per_owner, row_width), jnp.bfloat16),
        in_specs=[pl.BlockSpec(memory_space=pltpu.VMEM)] * len(operands)
        + [pl.BlockSpec(memory_space=pl.ANY)] * len(side),
        out_specs=pl.BlockSpec(memory_space=pltpu.VMEM),
        cost_estimate=pl.CostEstimate(
            flops=2 * edge_source.shape[0] * (node_rows.shape[0] + arrived.shape[0]) * node_rows.shape[1],
            transcendentals=0,
            bytes_accessed=sum(int(x.size) * x.dtype.itemsize for x in operands)
            + owners * per_owner * row_width * 2,
        ),
    )(*operands, *side)


def split_dot(values, weight):
    upper_part = values.astype(jnp.bfloat16)
    lower_part = (values - upper_part.astype(jnp.float32)).astype(jnp.bfloat16)
    return jnp.dot(upper_part, weight, preferred_element_type=jnp.float32) + jnp.dot(
        lower_part, weight, preferred_element_type=jnp.float32
    )


def body(
    node_feats,
    norm_gain,
    species,
    send_list,
    edge_source,
    edge_target,
    edge_count,
    edge_length,
    wigner,
    radial_in,
    species_table,
    radial_out,
    order_zero,
    order_one,
    order_two,
    project_weight,
):
    levels = MAX_DEGREE + 1
    owners = lax.axis_size("irreps")
    quarter = lax.axis_index("irreps")
    coeffs, span_chan, atom_count = node_feats.shape
    per_owner = edge_source.shape[0] // owners
    first_edge = quarter * per_owner

    row_used = coeffs * span_chan
    row_width = 128 * pl.cdiv(row_used, 128)
    node_rows = node_feats.reshape(row_used, atom_count).T
    arrived = lax.all_to_all(node_rows[send_list], "graph", 0, 0, tiled=True)

    gain_high = lax.reduce_precision(norm_gain, exponent_bits=8, mantissa_bits=7)
    gain_rest = norm_gain - gain_high
    gain_mid = lax.reduce_precision(gain_rest, exponent_bits=8, mantissa_bits=7)
    gain_low = gain_rest - gain_mid
    gain_block = jnp.transpose(jnp.stack([gain_high, gain_mid, gain_low]), (2, 0, 1))
    gain_block = jnp.pad(gain_block, ((0, 0), (0, 0), (0, 1))).reshape(span_chan, 3 * (levels + 1))
    gain_block = jnp.pad(gain_block, ((0, 0), (0, per_owner - gain_block.shape[1]))).astype(jnp.bfloat16)
    pair_order = np.concatenate([np.arange(0, span_chan, 2), np.arange(1, span_chan, 2)])
    weight_block = jnp.transpose(
        project_weight[:, :, pair_order].reshape(levels, CHANNELS // per_owner, per_owner, span_chan), (0, 1, 3, 2)
    ).reshape(-1, per_owner)
    extra = jnp.concatenate([weight_block, gain_block], axis=0).T

    wig_mine = lax.dynamic_slice_in_dim(wigner, first_edge, per_owner, 1)
    targets_mine = lax.dynamic_slice_in_dim(edge_target, first_edge, per_owner)
    lengths_mine = lax.dynamic_slice_in_dim(edge_length, first_edge, per_owner)
    kinds = species[targets_mine]
    kind_onehot = (
        kinds[None, :] == jnp.arange(species_table.shape[0], dtype=jnp.int32)[:, None]
    ).astype(jnp.bfloat16)
    edge_weight = jnp.where(
        first_edge + jnp.arange(per_owner, dtype=jnp.int32) < edge_count[0], 0.25, 0.0
    ).astype(jnp.float32)
    onehot = jnp.where(
        targets_mine[:, None] == jnp.arange(atom_count, dtype=jnp.int32)[None, :],
        edge_weight[:, None],
        0.0,
    ).astype(jnp.bfloat16)
    side = edge_operands(
        wig_mine, lengths_mine, kind_onehot, radial_in, species_table, radial_out,
        order_zero, order_one, order_two, onehot,
    )
    outgoing = gather_rows(edge_source, node_rows, arrived, extra, owners, row_width, side)
    source = lax.all_to_all(outgoing, "irreps", 0, 0, tiled=True)
    projected = convolve_edges(source, side)
    returned = lax.all_to_all(projected, "irreps", 0, 0, tiled=True)
    total = jnp.sum(returned.astype(jnp.float32), axis=0)[: coeffs * span_chan // 2]
    total = total.reshape(coeffs, span_chan // 2, 2, atom_count).reshape(coeffs, span_chan, atom_count)
    return (node_feats.astype(jnp.float32) + total).astype(jnp.bfloat16)


def solution(mesh):
    return jax.shard_map(
        body,
        mesh=mesh,
        in_specs=(
            P(None, "irreps", "graph"),
            P(None, "irreps"),
            P("graph"),
            P("graph"),
            P("graph"),
            P("graph"),
            P("graph"),
            P("graph"),
            P(None, "graph"),
            P(),
            P(),
            P(),
            P(),
            P(),
            P(),
            P(None, None, "irreps"),
        ),
        out_specs=P(None, "irreps", "graph"),
        check_vma=False,
    )
```

```python
import jax
import jax.numpy as jnp
import numpy as np
from jax import lax
from jax.sharding import PartitionSpec as P
from jax.experimental import pallas as pl
from jax.experimental.pallas import tpu as pltpu

CHANNELS = 128
MAX_DEGREE = 6
MAX_ORDER = 2
ROTATED = 29
COEFFS = 49


EPSILON = 1e-06
CUTOFF = 6.0


def order_index(degree, harmonic):
    if harmonic == 0:
        return degree
    first_row = MAX_DEGREE + 1
    for level in range(1, abs(harmonic)):
        first_row = first_row + 2 * (MAX_DEGREE + 1 - level)
    if harmonic < 0:
        first_row = first_row + MAX_DEGREE + 1 - abs(harmonic)
    return first_row + degree - abs(harmonic)


def wigner_start(degree):
    running = 0
    for level in range(degree):
        running = running + (2 * min(level, MAX_ORDER) + 1) * (2 * level + 1)
    return running


def left_dot(weight, values):
    return lax.dot_general(
        weight, values, (((0,), (0,)), ((), ())), preferred_element_type=jnp.float32
    )


def degree_sums(squares):
    return jnp.stack(
        [
            jnp.sum(squares[degree * degree : (degree + 1) ** 2], axis=0)
            for degree in range(MAX_DEGREE + 1)
        ]
    )


def normalize(node_feats, norm_gain, totals):
    levels = MAX_DEGREE + 1
    degree_of = np.repeat(np.arange(levels), 2 * np.arange(levels) + 1)
    entry_counts = (2 * np.arange(levels) + 1) * CHANNELS
    inverse = 1.0 / jnp.sqrt(totals / jnp.asarray(entry_counts, jnp.float32)[:, None] + EPSILON)
    gain_rows = norm_gain[degree_of]
    scale_rows = inverse[degree_of]
    return (node_feats.astype(jnp.float32) * gain_rows[:, :, None] * scale_rows[:, None, :]).astype(
        jnp.bfloat16
    )


def normalize_rows(values, gain_full, totals):
    levels = MAX_DEGREE + 1
    degree_of = np.repeat(np.arange(levels), 2 * np.arange(levels) + 1)
    entry_counts = (2 * np.arange(levels) + 1) * CHANNELS
    inverse = 1.0 / jnp.sqrt(totals / jnp.asarray(entry_counts, jnp.float32)[:, None] + EPSILON)
    gain_rows = gain_full[degree_of]
    scale_rows = inverse[degree_of]
    return (values * gain_rows[:, :, None] * scale_rows[:, None, :]).astype(jnp.bfloat16)


def rotate(source, wig_rows):
    pieces = [None] * ROTATED
    for degree in range(MAX_DEGREE + 1):
        reach_order = min(degree, MAX_ORDER)
        span_cols = 2 * degree + 1
        first_row = wigner_start(degree)
        for position in range(2 * reach_order + 1):
            total = None
            for column in range(span_cols):
                term = wig_rows[first_row + position * span_cols + column][None, :] * source[degree * degree + column]
                total = term if total is None else total + term
            pieces[order_index(degree, position - reach_order)] = total
    return jnp.stack(pieces).astype(jnp.bfloat16)


def unrotate(gated, wig_rows):
    pieces = []
    for degree in range(MAX_DEGREE + 1):
        reach_order = min(degree, MAX_ORDER)
        span_cols = 2 * degree + 1
        first_row = wigner_start(degree)
        for column in range(span_cols):
            total = None
            for position in range(2 * reach_order + 1):
                term = wig_rows[first_row + position * span_cols + column][None, :] * gated[
                    order_index(degree, position - reach_order)
                ]
                total = term if total is None else total + term
            pieces.append(total)
    return jnp.stack(pieces)


def radial_weights(lengths, kind_ids, radial_in, species_table, radial_out):
    basis_count = radial_in.shape[0]
    spacing = CUTOFF / (basis_count - 1)
    centers = jnp.arange(basis_count, dtype=jnp.float32) * spacing
    basis_rows = jnp.exp(
        -0.5 * jnp.square((lengths[None, :] - centers[:, None]) / (2.0 * spacing))
    ).astype(jnp.bfloat16)
    onehot = (
        kind_ids[None, :] == jnp.arange(species_table.shape[0], dtype=jnp.int32)[:, None]
    ).astype(jnp.bfloat16)
    hidden = jax.nn.silu(left_dot(radial_in, basis_rows) + left_dot(species_table, onehot)).astype(
        jnp.bfloat16
    )
    return left_dot(radial_out, hidden)


def convolve(rotated, radial, order_zero, order_one, order_two):
    levels = MAX_DEGREE + 1
    channel_count = rotated.shape[1]
    num_edges = rotated.shape[2]
    lowest = (
        rotated[:levels].astype(jnp.float32).reshape(levels * channel_count, num_edges) * radial
    ).astype(jnp.bfloat16)
    outputs = [left_dot(order_zero, lowest).reshape(levels, channel_count, num_edges)]
    first_row = levels
    for harmonic, weight in ((1, order_one), (2, order_two)):
        span_rows = levels - harmonic
        plus_rows = rotated[first_row : first_row + span_rows].reshape(
            span_rows * channel_count, num_edges
        )
        minus_rows = rotated[first_row + span_rows : first_row + 2 * span_rows].reshape(
            span_rows * channel_count, num_edges
        )
        joined = jnp.concatenate([plus_rows, minus_rows], axis=1)
        real_part = left_dot(weight[0], joined)
        cross_part = left_dot(weight[1], joined)
        outputs.append(
            (real_part[:, :num_edges] - cross_part[:, num_edges:]).reshape(
                span_rows, channel_count, num_edges
            )
        )
        outputs.append(
            (cross_part[:, :num_edges] + real_part[:, num_edges:]).reshape(
                span_rows, channel_count, num_edges
            )
        )
        first_row = first_row + 2 * span_rows
    mixed = jnp.concatenate(outputs, axis=0)
    scalar = mixed[0]
    return jnp.concatenate(
        [jax.nn.silu(scalar)[None], mixed[1:] * jax.nn.sigmoid(scalar)[None]], axis=0
    ).astype(jnp.bfloat16)


def conv_kernel(
    src_ref, wig_ref, length_ref, kind_ref, basis_in_ref, kind_table_ref, radial_out_ref,
    zero_hbm, one_hbm, two_hbm, onehot_ref, out_ref, zero_ref, one_ref, two_ref, copy_sems,
):
    loads = [
        pltpu.make_async_copy(zero_hbm, zero_ref, copy_sems.at[0]),
        pltpu.make_async_copy(one_hbm, one_ref, copy_sems.at[1]),
        pltpu.make_async_copy(two_hbm, two_ref, copy_sems.at[2]),
    ]
    for load in loads:
        load.start()
    levels = MAX_DEGREE + 1
    channel_count = CHANNELS
    num_edges = onehot_ref.shape[0]
    basis_count = basis_in_ref.shape[1]
    wig = wig_ref[...].astype(jnp.float32)
    owners = src_ref.shape[0]
    span_chan = CHANNELS // owners
    turned = [src_ref[r].astype(jnp.float32).T for r in range(owners)]
    base = COEFFS * span_chan
    half = num_edges
    pick = (
        lax.broadcasted_iota(jnp.int32, (half, span_chan), 0) % span_chan
        == lax.broadcasted_iota(jnp.int32, (half, span_chan), 1)
    ) & (lax.broadcasted_iota(jnp.int32, (half, span_chan), 0) < 3 * span_chan)
    pick = pick.astype(jnp.float32)
    gain_at = base + levels * 2 * span_chan
    gain = jnp.concatenate(
        [
            jnp.dot(block[gain_at : gain_at + span_chan], pick, preferred_element_type=jnp.float32)
            for block in turned
        ],
        axis=0,
    )
    projection = []
    for degree in range(levels):
        start = base + degree * 2 * span_chan
        projection.append(
            jnp.concatenate(
                [
                    jnp.concatenate(
                        [block[start : start + span_chan], block[start + span_chan : start + 2 * span_chan]],
                        axis=1,
                    )
                    for block in turned
                ],
                axis=0,
            ).astype(jnp.bfloat16)
        )

    rows = [
        jnp.concatenate([block[j * span_chan : (j + 1) * span_chan] for block in turned], axis=0)
        for j in range(COEFFS)
    ]
    normed = [None] * len(rows)
    for degree in range(levels):
        span = range(degree * degree, (degree + 1) ** 2)
        total = None
        for j in span:
            part = jnp.sum(rows[j] * rows[j], axis=0, keepdims=True)
            total = part if total is None else total + part
        inverse = 1.0 / jnp.sqrt(total / float((2 * degree + 1) * CHANNELS) + EPSILON)
        scale = gain[:, degree : degree + 1]
        for j in span:
            normed[j] = (rows[j] * scale * inverse).astype(jnp.bfloat16).astype(jnp.float32)

    rotated = [None] * ROTATED
    for degree in range(levels):
        reach_order = min(degree, MAX_ORDER)
        span_cols = 2 * degree + 1
        first_row = wigner_start(degree)
        for position in range(2 * reach_order + 1):
            total = None
            for column in range(span_cols):
                row = first_row + position * span_cols + column
                term = wig[row : row + 1, :] * normed[degree * degree + column]
                total = term if total is None else total + term
            rotated[order_index(degree, position - reach_order)] = total.astype(jnp.bfloat16)

    spacing = CUTOFF / (basis_count - 1)
    centers = lax.broadcasted_iota(jnp.int32, (basis_count, num_edges), 0).astype(jnp.float32) * spacing
    basis_rows = jnp.exp(
        -0.5 * jnp.square((length_ref[...] - centers) / (2.0 * spacing))
    ).astype(jnp.bfloat16)
    hidden = jnp.dot(basis_in_ref[...], basis_rows, preferred_element_type=jnp.float32) + jnp.dot(
        kind_table_ref[...], kind_ref[...], preferred_element_type=jnp.float32
    )
    hidden = (hidden * jax.nn.sigmoid(hidden)).astype(jnp.bfloat16)
    radial = jnp.dot(radial_out_ref[...], hidden, preferred_element_type=jnp.float32)

    lowest = jnp.concatenate(
        [
            (rotated[degree].astype(jnp.float32) * radial[degree * channel_count : (degree + 1) * channel_count]).astype(
                jnp.bfloat16
            )
            for degree in range(levels)
        ],
        axis=0,
    )
    loads[0].wait()
    mixed0 = jnp.dot(zero_ref[...], lowest, preferred_element_type=jnp.float32)
    mixed = [mixed0[degree * channel_count : (degree + 1) * channel_count] for degree in range(levels)]
    first_row = levels
    for harmonic, weight_ref, load in ((1, one_ref, loads[1]), (2, two_ref, loads[2])):
        load.wait()
        span_rows = levels - harmonic
        plus_rows = jnp.concatenate(rotated[first_row : first_row + span_rows], axis=0)
        minus_rows = jnp.concatenate(rotated[first_row + span_rows : first_row + 2 * span_rows], axis=0)
        joined = jnp.concatenate([plus_rows, minus_rows], axis=1)
        real_part = jnp.dot(weight_ref[0], joined, preferred_element_type=jnp.float32)
        cross_part = jnp.dot(weight_ref[1], joined, preferred_element_type=jnp.float32)
        new_plus = real_part[:, :num_edges] - cross_part[:, num_edges:]
        new_minus = cross_part[:, :num_edges] + real_part[:, num_edges:]
        mixed += [new_plus[k * channel_count : (k + 1) * channel_count] for k in range(span_rows)]
        mixed += [new_minus[k * channel_count : (k + 1) * channel_count] for k in range(span_rows)]
        first_row = first_row + 2 * span_rows

    scalar = mixed[0]
    gate = jax.nn.sigmoid(scalar)
    gated = [(scalar * gate).astype(jnp.bfloat16).astype(jnp.float32)] + [
        (piece * gate).astype(jnp.bfloat16).astype(jnp.float32) for piece in mixed[1:]
    ]

    messages = []
    for degree in range(levels):
        reach_order = min(degree, MAX_ORDER)
        span_cols = 2 * degree + 1
        first_row = wigner_start(degree)
        for column in range(span_cols):
            total = None
            for position in range(2 * reach_order + 1):
                row = first_row + position * span_cols + column
                term = wig[row : row + 1, :] * gated[order_index(degree, position - reach_order)]
                total = term if total is None else total + term
            messages.append(total)
    stacked = jnp.concatenate(messages, axis=0)
    upper_part = stacked.astype(jnp.bfloat16)
    lower_part = (stacked - upper_part.astype(jnp.float32)).astype(jnp.bfloat16)
    onehot = onehot_ref[...]
    summed = jnp.dot(upper_part, onehot, preferred_element_type=jnp.float32) + jnp.dot(
        lower_part, onehot, preferred_element_type=jnp.float32
    )
    half = span_chan // 2
    pieces = [[] for _ in range(owners)]
    for degree in range(levels):
        weight = projection[degree]
        for j in range(degree * degree, (degree + 1) ** 2):
            piece = summed[j * channel_count : (j + 1) * channel_count]
            high = piece.astype(jnp.bfloat16)
            low = (piece - high.astype(jnp.float32)).astype(jnp.bfloat16)
            both = jnp.dot(weight, jnp.concatenate([high, low], axis=1), preferred_element_type=jnp.float32)
            result = both[:, :num_edges] + both[:, num_edges:]
            for r in range(owners):
                block = result[r * span_chan : (r + 1) * span_chan]
                pieces[r].append(jnp.concatenate([block[:half], block[half:]], axis=1))
    fill = out_ref.shape[1] - COEFFS * half
    for r in range(owners):
        out_ref[r] = jnp.concatenate(
            pieces[r] + [jnp.zeros((fill, out_ref.shape[2]), jnp.float32)], axis=0
        ).astype(out_ref.dtype)


def edge_operands(wig_mine, lengths, kind_onehot, radial_in, species_table, radial_out,
                  order_zero, order_one, order_two, onehot):
    return (
        wig_mine,
        lengths[None, :],
        kind_onehot,
        radial_in.T,
        species_table.T,
        radial_out.T,
        order_zero.T,
        jnp.transpose(order_one, (0, 2, 1)),
        jnp.transpose(order_two, (0, 2, 1)),
        onehot,
    )


def convolve_edges(source, side):
    coeffs, channel_count = COEFFS, CHANNELS
    onehot = side[-1]
    num_edges, atom_count = onehot.shape
    owners = source.shape[0]
    out_rows = 16 * pl.cdiv(coeffs * (channel_count // owners) // 2, 16)
    operands = (source,) + tuple(side)
    radial_in, radial_out = side[3], side[5]
    order_zero, order_one, order_two = side[6], side[7], side[8]
    flops = 2 * num_edges * (order_zero.size + 2 * order_one.size + 2 * order_two.size + radial_out.size + radial_in.size)
    return pl.pallas_call(
        conv_kernel,
        out_shape=jax.ShapeDtypeStruct((owners, out_rows, 2 * atom_count), jnp.bfloat16),
        in_specs=[pl.BlockSpec(memory_space=pltpu.VMEM)] * 7
        + [pl.BlockSpec(memory_space=pl.ANY)] * 3
        + [pl.BlockSpec(memory_space=pltpu.VMEM)],
        out_specs=pl.BlockSpec(memory_space=pltpu.VMEM),
        scratch_shapes=[
            pltpu.VMEM(order_zero.shape, order_zero.dtype),
            pltpu.VMEM(order_one.shape, order_one.dtype),
            pltpu.VMEM(order_two.shape, order_two.dtype),
            pltpu.SemaphoreType.DMA((3,)),
        ],
        cost_estimate=pl.CostEstimate(
            flops=flops,
            transcendentals=num_edges * (radial_in.shape[1] + 2 * channel_count),
            bytes_accessed=sum(int(x.size) * x.dtype.itemsize for x in operands) + owners * out_rows * atom_count * 4,
        ),
    )(*operands)


def gather_kernel(index_ref, local_ref, arrived_ref, extra_ref, *refs):
    out_ref = refs[-1]
    owners, per_owner, row_width = out_ref.shape
    row_used = local_ref.shape[1]
    table = jnp.concatenate([local_ref[...], arrived_ref[...]], axis=0)
    hot = (
        index_ref[...] == lax.broadcasted_iota(jnp.int32, (index_ref.shape[0], table.shape[0]), 1)
    ).astype(jnp.bfloat16)
    picked = jnp.dot(hot, table, preferred_element_type=jnp.float32).astype(out_ref.dtype)
    extra = extra_ref[...]
    for q in range(owners):
        out_ref[q, :, 0:row_used] = picked[q * per_owner : (q + 1) * per_owner]
        out_ref[q, :, row_used:row_width] = extra


def gather_rows(edge_source, node_rows, arrived, extra, owners, row_width, side):
    per_owner = edge_source.shape[0] // owners
    operands = (edge_source[:, None], node_rows, arrived, extra)
    return pl.pallas_call(
        gather_kernel,
        out_shape=jax.ShapeDtypeStruct((owners, per_owner, row_width), jnp.bfloat16),
        in_specs=[pl.BlockSpec(memory_space=pltpu.VMEM)] * len(operands)
        + [pl.BlockSpec(memory_space=pl.ANY)] * len(side),
        out_specs=pl.BlockSpec(memory_space=pltpu.VMEM),
        cost_estimate=pl.CostEstimate(
            flops=2 * edge_source.shape[0] * (node_rows.shape[0] + arrived.shape[0]) * node_rows.shape[1],
            transcendentals=0,
            bytes_accessed=sum(int(x.size) * x.dtype.itemsize for x in operands)
            + owners * per_owner * row_width * 2,
        ),
    )(*operands, *side)


def split_dot(values, weight):
    upper_part = values.astype(jnp.bfloat16)
    lower_part = (values - upper_part.astype(jnp.float32)).astype(jnp.bfloat16)
    return jnp.dot(upper_part, weight, preferred_element_type=jnp.float32) + jnp.dot(
        lower_part, weight, preferred_element_type=jnp.float32
    )


def body(
    node_feats,
    norm_gain,
    species,
    send_list,
    edge_source,
    edge_target,
    edge_count,
    edge_length,
    wigner,
    radial_in,
    species_table,
    radial_out,
    order_zero,
    order_one,
    order_two,
    project_weight,
):
    levels = MAX_DEGREE + 1
    owners = lax.axis_size("irreps")
    quarter = lax.axis_index("irreps")
    coeffs, span_chan, atom_count = node_feats.shape
    per_owner = edge_source.shape[0] // owners
    first_edge = quarter * per_owner

    row_used = coeffs * span_chan
    row_width = 128 * pl.cdiv(row_used, 128)
    node_rows = node_feats.reshape(row_used, atom_count).T
    arrived = lax.all_to_all(node_rows[send_list], "graph", 0, 0, tiled=True)

    gain_high = lax.reduce_precision(norm_gain, exponent_bits=8, mantissa_bits=7)
    gain_rest = norm_gain - gain_high
    gain_mid = lax.reduce_precision(gain_rest, exponent_bits=8, mantissa_bits=7)
    gain_low = gain_rest - gain_mid
    gain_block = jnp.transpose(jnp.stack([gain_high, gain_mid, gain_low]), (2, 0, 1))
    gain_block = jnp.pad(gain_block, ((0, 0), (0, 0), (0, 1))).reshape(span_chan, 3 * (levels + 1))
    gain_block = jnp.pad(gain_block, ((0, 0), (0, per_owner - gain_block.shape[1]))).astype(jnp.bfloat16)
    pair_order = np.concatenate([np.arange(0, span_chan, 2), np.arange(1, span_chan, 2)])
    weight_block = jnp.transpose(
        project_weight[:, :, pair_order].reshape(levels, CHANNELS // per_owner, per_owner, span_chan), (0, 1, 3, 2)
    ).reshape(-1, per_owner)
    extra = jnp.concatenate([weight_block, gain_block], axis=0).T

    wig_mine = lax.dynamic_slice_in_dim(wigner, first_edge, per_owner, 1)
    targets_mine = lax.dynamic_slice_in_dim(edge_target, first_edge, per_owner)
    lengths_mine = lax.dynamic_slice_in_dim(edge_length, first_edge, per_owner)
    kinds = species[targets_mine]
    kind_onehot = (
        kinds[None, :] == jnp.arange(species_table.shape[0], dtype=jnp.int32)[:, None]
    ).astype(jnp.bfloat16)
    edge_weight = jnp.where(
        first_edge + jnp.arange(per_owner, dtype=jnp.int32) < edge_count[0], 0.25, 0.0
    ).astype(jnp.float32)
    onehot = jnp.where(
        targets_mine[:, None] == jnp.arange(atom_count, dtype=jnp.int32)[None, :],
        edge_weight[:, None],
        0.0,
    ).astype(jnp.bfloat16)
    side = edge_operands(
        wig_mine, lengths_mine, kind_onehot, radial_in, species_table, radial_out,
        order_zero, order_one, order_two, onehot,
    )
    outgoing = gather_rows(edge_source, node_rows, arrived, extra, owners, row_width, side)
    source = lax.all_to_all(outgoing, "irreps", 0, 0, tiled=True)
    projected = convolve_edges(source, side)
    returned = lax.all_to_all(projected, "irreps", 0, 0, tiled=True)
    total = jnp.sum(returned.astype(jnp.float32), axis=0)[: coeffs * span_chan // 2]
    total = total.reshape(coeffs, span_chan // 2, 2, atom_count).reshape(coeffs, span_chan, atom_count)
    return (node_feats.astype(jnp.float32) + total).astype(jnp.bfloat16)


def solution(mesh):
    return jax.shard_map(
        body,
        mesh=mesh,
        in_specs=(
            P(None, "irreps", "graph"),
            P(None, "irreps"),
            P("graph"),
            P("graph"),
            P("graph"),
            P("graph"),
            P("graph"),
            P("graph"),
            P(None, "graph"),
            P(),
            P(),
            P(),
            P(),
            P(),
            P(),
            P(None, None, "irreps"),
        ),
        out_specs=P(None, "irreps", "graph"),
        check_vma=False,
    )
```

```python
import jax
import jax.numpy as jnp
import numpy as np
from jax import lax
from jax.sharding import PartitionSpec as P
from jax.experimental import pallas as pl
from jax.experimental.pallas import tpu as pltpu

CHANNELS = 128
MAX_DEGREE = 6
MAX_ORDER = 2
ROTATED = 29
COEFFS = 49


EPSILON = 1e-06
CUTOFF = 6.0


def order_index(degree, harmonic):
    if harmonic == 0:
        return degree
    first_row = MAX_DEGREE + 1
    for level in range(1, abs(harmonic)):
        first_row = first_row + 2 * (MAX_DEGREE + 1 - level)
    if harmonic < 0:
        first_row = first_row + MAX_DEGREE + 1 - abs(harmonic)
    return first_row + degree - abs(harmonic)


def wigner_start(degree):
    running = 0
    for level in range(degree):
        running = running + (2 * min(level, MAX_ORDER) + 1) * (2 * level + 1)
    return running


def left_dot(weight, values):
    return lax.dot_general(
        weight, values, (((0,), (0,)), ((), ())), preferred_element_type=jnp.float32
    )


def degree_sums(squares):
    return jnp.stack(
        [
            jnp.sum(squares[degree * degree : (degree + 1) ** 2], axis=0)
            for degree in range(MAX_DEGREE + 1)
        ]
    )


def normalize(node_feats, norm_gain, totals):
    levels = MAX_DEGREE + 1
    degree_of = np.repeat(np.arange(levels), 2 * np.arange(levels) + 1)
    entry_counts = (2 * np.arange(levels) + 1) * CHANNELS
    inverse = 1.0 / jnp.sqrt(totals / jnp.asarray(entry_counts, jnp.float32)[:, None] + EPSILON)
    gain_rows = norm_gain[degree_of]
    scale_rows = inverse[degree_of]
    return (node_feats.astype(jnp.float32) * gain_rows[:, :, None] * scale_rows[:, None, :]).astype(
        jnp.bfloat16
    )


def normalize_rows(values, gain_full, totals):
    levels = MAX_DEGREE + 1
    degree_of = np.repeat(np.arange(levels), 2 * np.arange(levels) + 1)
    entry_counts = (2 * np.arange(levels) + 1) * CHANNELS
    inverse = 1.0 / jnp.sqrt(totals / jnp.asarray(entry_counts, jnp.float32)[:, None] + EPSILON)
    gain_rows = gain_full[degree_of]
    scale_rows = inverse[degree_of]
    return (values * gain_rows[:, :, None] * scale_rows[:, None, :]).astype(jnp.bfloat16)


def rotate(source, wig_rows):
    pieces = [None] * ROTATED
    for degree in range(MAX_DEGREE + 1):
        reach_order = min(degree, MAX_ORDER)
        span_cols = 2 * degree + 1
        first_row = wigner_start(degree)
        for position in range(2 * reach_order + 1):
            total = None
            for column in range(span_cols):
                term = wig_rows[first_row + position * span_cols + column][None, :] * source[degree * degree + column]
                total = term if total is None else total + term
            pieces[order_index(degree, position - reach_order)] = total
    return jnp.stack(pieces).astype(jnp.bfloat16)


def unrotate(gated, wig_rows):
    pieces = []
    for degree in range(MAX_DEGREE + 1):
        reach_order = min(degree, MAX_ORDER)
        span_cols = 2 * degree + 1
        first_row = wigner_start(degree)
        for column in range(span_cols):
            total = None
            for position in range(2 * reach_order + 1):
                term = wig_rows[first_row + position * span_cols + column][None, :] * gated[
                    order_index(degree, position - reach_order)
                ]
                total = term if total is None else total + term
            pieces.append(total)
    return jnp.stack(pieces)


def radial_weights(lengths, kind_ids, radial_in, species_table, radial_out):
    basis_count = radial_in.shape[0]
    spacing = CUTOFF / (basis_count - 1)
    centers = jnp.arange(basis_count, dtype=jnp.float32) * spacing
    basis_rows = jnp.exp(
        -0.5 * jnp.square((lengths[None, :] - centers[:, None]) / (2.0 * spacing))
    ).astype(jnp.bfloat16)
    onehot = (
        kind_ids[None, :] == jnp.arange(species_table.shape[0], dtype=jnp.int32)[:, None]
    ).astype(jnp.bfloat16)
    hidden = jax.nn.silu(left_dot(radial_in, basis_rows) + left_dot(species_table, onehot)).astype(
        jnp.bfloat16
    )
    return left_dot(radial_out, hidden)


def convolve(rotated, radial, order_zero, order_one, order_two):
    levels = MAX_DEGREE + 1
    channel_count = rotated.shape[1]
    num_edges = rotated.shape[2]
    lowest = (
        rotated[:levels].astype(jnp.float32).reshape(levels * channel_count, num_edges) * radial
    ).astype(jnp.bfloat16)
    outputs = [left_dot(order_zero, lowest).reshape(levels, channel_count, num_edges)]
    first_row = levels
    for harmonic, weight in ((1, order_one), (2, order_two)):
        span_rows = levels - harmonic
        plus_rows = rotated[first_row : first_row + span_rows].reshape(
            span_rows * channel_count, num_edges
        )
        minus_rows = rotated[first_row + span_rows : first_row + 2 * span_rows].reshape(
            span_rows * channel_count, num_edges
        )
        joined = jnp.concatenate([plus_rows, minus_rows], axis=1)
        real_part = left_dot(weight[0], joined)
        cross_part = left_dot(weight[1], joined)
        outputs.append(
            (real_part[:, :num_edges] - cross_part[:, num_edges:]).reshape(
                span_rows, channel_count, num_edges
            )
        )
        outputs.append(
            (cross_part[:, :num_edges] + real_part[:, num_edges:]).reshape(
                span_rows, channel_count, num_edges
            )
        )
        first_row = first_row + 2 * span_rows
    mixed = jnp.concatenate(outputs, axis=0)
    scalar = mixed[0]
    return jnp.concatenate(
        [jax.nn.silu(scalar)[None], mixed[1:] * jax.nn.sigmoid(scalar)[None]], axis=0
    ).astype(jnp.bfloat16)


def conv_kernel(
    src_ref, wig_ref, length_ref, kind_ref, basis_in_ref, kind_table_ref, radial_out_ref,
    zero_hbm, one_hbm, two_hbm, onehot_ref, out_ref, zero_ref, one_ref, two_ref, copy_sems,
):
    loads = [
        pltpu.make_async_copy(zero_hbm, zero_ref, copy_sems.at[0]),
        pltpu.make_async_copy(one_hbm, one_ref, copy_sems.at[1]),
        pltpu.make_async_copy(two_hbm, two_ref, copy_sems.at[2]),
    ]
    for load in loads:
        load.start()
    levels = MAX_DEGREE + 1
    channel_count = CHANNELS
    num_edges = onehot_ref.shape[0]
    basis_count = basis_in_ref.shape[1]
    wig = wig_ref[...].astype(jnp.float32)
    owners = src_ref.shape[0]
    span_chan = CHANNELS // owners
    turned = [src_ref[r].astype(jnp.float32).T for r in range(owners)]
    base = COEFFS * span_chan
    half = num_edges
    pick = (
        lax.broadcasted_iota(jnp.int32, (half, span_chan), 0) % span_chan
        == lax.broadcasted_iota(jnp.int32, (half, span_chan), 1)
    ) & (lax.broadcasted_iota(jnp.int32, (half, span_chan), 0) < 3 * span_chan)
    pick = pick.astype(jnp.float32)
    gain_at = base + levels * 2 * span_chan
    gain = jnp.concatenate(
        [
            jnp.dot(block[gain_at : gain_at + span_chan], pick, preferred_element_type=jnp.float32)
            for block in turned
        ],
        axis=0,
    )
    projection = []
    for degree in range(levels):
        start = base + degree * 2 * span_chan
        projection.append(
            jnp.concatenate(
                [
                    jnp.concatenate(
                        [block[start : start + span_chan], block[start + span_chan : start + 2 * span_chan]],
                        axis=1,
                    )
                    for block in turned
                ],
                axis=0,
            ).astype(jnp.bfloat16)
        )

    rows = [
        jnp.concatenate([block[j * span_chan : (j + 1) * span_chan] for block in turned], axis=0)
        for j in range(COEFFS)
    ]
    normed = [None] * len(rows)
    for degree in range(levels):
        span = range(degree * degree, (degree + 1) ** 2)
        total = None
        for j in span:
            part = jnp.sum(rows[j] * rows[j], axis=0, keepdims=True)
            total = part if total is None else total + part
        inverse = 1.0 / jnp.sqrt(total / float((2 * degree + 1) * CHANNELS) + EPSILON)
        scale = gain[:, degree : degree + 1]
        for j in span:
            normed[j] = (rows[j] * scale * inverse).astype(jnp.bfloat16).astype(jnp.float32)

    rotated = [None] * ROTATED
    for degree in range(levels):
        reach_order = min(degree, MAX_ORDER)
        span_cols = 2 * degree + 1
        first_row = wigner_start(degree)
        for position in range(2 * reach_order + 1):
            total = None
            for column in range(span_cols):
                row = first_row + position * span_cols + column
                term = wig[row : row + 1, :] * normed[degree * degree + column]
                total = term if total is None else total + term
            rotated[order_index(degree, position - reach_order)] = total.astype(jnp.bfloat16)

    spacing = CUTOFF / (basis_count - 1)
    centers = lax.broadcasted_iota(jnp.int32, (basis_count, num_edges), 0).astype(jnp.float32) * spacing
    basis_rows = jnp.exp(
        -0.5 * jnp.square((length_ref[...] - centers) / (2.0 * spacing))
    ).astype(jnp.bfloat16)
    hidden = jnp.dot(basis_in_ref[...], basis_rows, preferred_element_type=jnp.float32) + jnp.dot(
        kind_table_ref[...], kind_ref[...], preferred_element_type=jnp.float32
    )
    hidden = (hidden * jax.nn.sigmoid(hidden)).astype(jnp.bfloat16)
    radial = jnp.dot(radial_out_ref[...], hidden, preferred_element_type=jnp.float32)

    lowest = jnp.concatenate(
        [
            (rotated[degree].astype(jnp.float32) * radial[degree * channel_count : (degree + 1) * channel_count]).astype(
                jnp.bfloat16
            )
            for degree in range(levels)
        ],
        axis=0,
    )
    loads[0].wait()
    mixed0 = jnp.dot(zero_ref[...], lowest, preferred_element_type=jnp.float32)
    mixed = [mixed0[degree * channel_count : (degree + 1) * channel_count] for degree in range(levels)]
    first_row = levels
    for harmonic, weight_ref, load in ((1, one_ref, loads[1]), (2, two_ref, loads[2])):
        load.wait()
        span_rows = levels - harmonic
        plus_rows = jnp.concatenate(rotated[first_row : first_row + span_rows], axis=0)
        minus_rows = jnp.concatenate(rotated[first_row + span_rows : first_row + 2 * span_rows], axis=0)
        joined = jnp.concatenate([plus_rows, minus_rows], axis=1)
        real_part = jnp.dot(weight_ref[0], joined, preferred_element_type=jnp.float32)
        cross_part = jnp.dot(weight_ref[1], joined, preferred_element_type=jnp.float32)
        new_plus = real_part[:, :num_edges] - cross_part[:, num_edges:]
        new_minus = cross_part[:, :num_edges] + real_part[:, num_edges:]
        mixed += [new_plus[k * channel_count : (k + 1) * channel_count] for k in range(span_rows)]
        mixed += [new_minus[k * channel_count : (k + 1) * channel_count] for k in range(span_rows)]
        first_row = first_row + 2 * span_rows

    scalar = mixed[0]
    gate = jax.nn.sigmoid(scalar)
    gated = [(scalar * gate).astype(jnp.bfloat16).astype(jnp.float32)] + [
        (piece * gate).astype(jnp.bfloat16).astype(jnp.float32) for piece in mixed[1:]
    ]

    messages = []
    for degree in range(levels):
        reach_order = min(degree, MAX_ORDER)
        span_cols = 2 * degree + 1
        first_row = wigner_start(degree)
        for column in range(span_cols):
            total = None
            for position in range(2 * reach_order + 1):
                row = first_row + position * span_cols + column
                term = wig[row : row + 1, :] * gated[order_index(degree, position - reach_order)]
                total = term if total is None else total + term
            messages.append(total)
    stacked = jnp.concatenate(messages, axis=0)
    upper_part = stacked.astype(jnp.bfloat16)
    lower_part = (stacked - upper_part.astype(jnp.float32)).astype(jnp.bfloat16)
    onehot = onehot_ref[...]
    summed = jnp.dot(
        jnp.concatenate([upper_part, lower_part], axis=1),
        jnp.concatenate([onehot, onehot], axis=0),
        preferred_element_type=jnp.float32,
    )
    half = span_chan // 2
    pieces = [[] for _ in range(owners)]
    for degree in range(levels):
        weight = projection[degree]
        for j in range(degree * degree, (degree + 1) ** 2):
            piece = summed[j * channel_count : (j + 1) * channel_count]
            high = piece.astype(jnp.bfloat16)
            low = (piece - high.astype(jnp.float32)).astype(jnp.bfloat16)
            both = jnp.dot(weight, jnp.concatenate([high, low], axis=1), preferred_element_type=jnp.float32)
            result = both[:, :num_edges] + both[:, num_edges:]
            for r in range(owners):
                block = result[r * span_chan : (r + 1) * span_chan]
                pieces[r].append(jnp.concatenate([block[:half], block[half:]], axis=1))
    fill = out_ref.shape[1] - COEFFS * half
    for r in range(owners):
        out_ref[r] = jnp.concatenate(
            pieces[r] + [jnp.zeros((fill, out_ref.shape[2]), jnp.float32)], axis=0
        ).astype(out_ref.dtype)


def edge_operands(wig_mine, lengths, kind_onehot, radial_in, species_table, radial_out,
                  order_zero, order_one, order_two, onehot):
    return (
        wig_mine,
        lengths[None, :],
        kind_onehot,
        radial_in.T,
        species_table.T,
        radial_out.T,
        order_zero.T,
        jnp.transpose(order_one, (0, 2, 1)),
        jnp.transpose(order_two, (0, 2, 1)),
        onehot,
    )


def convolve_edges(source, side):
    coeffs, channel_count = COEFFS, CHANNELS
    onehot = side[-1]
    num_edges, atom_count = onehot.shape
    owners = source.shape[0]
    out_rows = 16 * pl.cdiv(coeffs * (channel_count // owners) // 2, 16)
    operands = (source,) + tuple(side)
    radial_in, radial_out = side[3], side[5]
    order_zero, order_one, order_two = side[6], side[7], side[8]
    flops = 2 * num_edges * (order_zero.size + 2 * order_one.size + 2 * order_two.size + radial_out.size + radial_in.size)
    return pl.pallas_call(
        conv_kernel,
        out_shape=jax.ShapeDtypeStruct((owners, out_rows, 2 * atom_count), jnp.bfloat16),
        in_specs=[pl.BlockSpec(memory_space=pltpu.VMEM)] * 7
        + [pl.BlockSpec(memory_space=pl.ANY)] * 3
        + [pl.BlockSpec(memory_space=pltpu.VMEM)],
        out_specs=pl.BlockSpec(memory_space=pltpu.VMEM),
        scratch_shapes=[
            pltpu.VMEM(order_zero.shape, order_zero.dtype),
            pltpu.VMEM(order_one.shape, order_one.dtype),
            pltpu.VMEM(order_two.shape, order_two.dtype),
            pltpu.SemaphoreType.DMA((3,)),
        ],
        cost_estimate=pl.CostEstimate(
            flops=flops,
            transcendentals=num_edges * (radial_in.shape[1] + 2 * channel_count),
            bytes_accessed=sum(int(x.size) * x.dtype.itemsize for x in operands) + owners * out_rows * atom_count * 4,
        ),
    )(*operands)


def gather_kernel(index_ref, local_ref, arrived_ref, extra_ref, *refs):
    out_ref = refs[-1]
    owners, per_owner, row_width = out_ref.shape
    row_used = local_ref.shape[1]
    table = jnp.concatenate([local_ref[...], arrived_ref[...]], axis=0)
    hot = (
        index_ref[...] == lax.broadcasted_iota(jnp.int32, (index_ref.shape[0], table.shape[0]), 1)
    ).astype(jnp.bfloat16)
    picked = jnp.dot(hot, table, preferred_element_type=jnp.float32).astype(out_ref.dtype)
    extra = extra_ref[...]
    for q in range(owners):
        out_ref[q, :, 0:row_used] = picked[q * per_owner : (q + 1) * per_owner]
        out_ref[q, :, row_used:row_width] = extra


def gather_rows(edge_source, node_rows, arrived, extra, owners, row_width, side):
    per_owner = edge_source.shape[0] // owners
    operands = (edge_source[:, None], node_rows, arrived, extra)
    return pl.pallas_call(
        gather_kernel,
        out_shape=jax.ShapeDtypeStruct((owners, per_owner, row_width), jnp.bfloat16),
        in_specs=[pl.BlockSpec(memory_space=pltpu.VMEM)] * len(operands)
        + [pl.BlockSpec(memory_space=pl.ANY)] * len(side),
        out_specs=pl.BlockSpec(memory_space=pltpu.VMEM),
        cost_estimate=pl.CostEstimate(
            flops=2 * edge_source.shape[0] * (node_rows.shape[0] + arrived.shape[0]) * node_rows.shape[1],
            transcendentals=0,
            bytes_accessed=sum(int(x.size) * x.dtype.itemsize for x in operands)
            + owners * per_owner * row_width * 2,
        ),
    )(*operands, *side)


def split_dot(values, weight):
    upper_part = values.astype(jnp.bfloat16)
    lower_part = (values - upper_part.astype(jnp.float32)).astype(jnp.bfloat16)
    return jnp.dot(upper_part, weight, preferred_element_type=jnp.float32) + jnp.dot(
        lower_part, weight, preferred_element_type=jnp.float32
    )


def body(
    node_feats,
    norm_gain,
    species,
    send_list,
    edge_source,
    edge_target,
    edge_count,
    edge_length,
    wigner,
    radial_in,
    species_table,
    radial_out,
    order_zero,
    order_one,
    order_two,
    project_weight,
):
    levels = MAX_DEGREE + 1
    owners = lax.axis_size("irreps")
    quarter = lax.axis_index("irreps")
    coeffs, span_chan, atom_count = node_feats.shape
    per_owner = edge_source.shape[0] // owners
    first_edge = quarter * per_owner

    row_used = coeffs * span_chan
    row_width = 128 * pl.cdiv(row_used, 128)
    node_rows = node_feats.reshape(row_used, atom_count).T
    arrived = lax.all_to_all(node_rows[send_list], "graph", 0, 0, tiled=True)

    gain_high = lax.reduce_precision(norm_gain, exponent_bits=8, mantissa_bits=7)
    gain_rest = norm_gain - gain_high
    gain_mid = lax.reduce_precision(gain_rest, exponent_bits=8, mantissa_bits=7)
    gain_low = gain_rest - gain_mid
    gain_block = jnp.transpose(jnp.stack([gain_high, gain_mid, gain_low]), (2, 0, 1))
    gain_block = jnp.pad(gain_block, ((0, 0), (0, 0), (0, 1))).reshape(span_chan, 3 * (levels + 1))
    gain_block = jnp.pad(gain_block, ((0, 0), (0, per_owner - gain_block.shape[1]))).astype(jnp.bfloat16)
    pair_order = np.concatenate([np.arange(0, span_chan, 2), np.arange(1, span_chan, 2)])
    weight_block = jnp.transpose(
        project_weight[:, :, pair_order].reshape(levels, CHANNELS // per_owner, per_owner, span_chan), (0, 1, 3, 2)
    ).reshape(-1, per_owner)
    extra = jnp.concatenate([weight_block, gain_block], axis=0).T

    wig_mine = lax.dynamic_slice_in_dim(wigner, first_edge, per_owner, 1)
    targets_mine = lax.dynamic_slice_in_dim(edge_target, first_edge, per_owner)
    lengths_mine = lax.dynamic_slice_in_dim(edge_length, first_edge, per_owner)
    kinds = species[targets_mine]
    kind_onehot = (
        kinds[None, :] == jnp.arange(species_table.shape[0], dtype=jnp.int32)[:, None]
    ).astype(jnp.bfloat16)
    edge_weight = jnp.where(
        first_edge + jnp.arange(per_owner, dtype=jnp.int32) < edge_count[0], 0.25, 0.0
    ).astype(jnp.float32)
    onehot = jnp.where(
        targets_mine[:, None] == jnp.arange(atom_count, dtype=jnp.int32)[None, :],
        edge_weight[:, None],
        0.0,
    ).astype(jnp.bfloat16)
    side = edge_operands(
        wig_mine, lengths_mine, kind_onehot, radial_in, species_table, radial_out,
        order_zero, order_one, order_two, onehot,
    )
    outgoing = gather_rows(edge_source, node_rows, arrived, extra, owners, row_width, side)
    source = lax.all_to_all(outgoing, "irreps", 0, 0, tiled=True)
    projected = convolve_edges(source, side)
    returned = lax.all_to_all(projected, "irreps", 0, 0, tiled=True)
    total = jnp.sum(returned.astype(jnp.float32), axis=0)[: coeffs * span_chan // 2]
    total = total.reshape(coeffs, span_chan // 2, 2, atom_count).reshape(coeffs, span_chan, atom_count)
    return (node_feats.astype(jnp.float32) + total).astype(jnp.bfloat16)


def solution(mesh):
    return jax.shard_map(
        body,
        mesh=mesh,
        in_specs=(
            P(None, "irreps", "graph"),
            P(None, "irreps"),
            P("graph"),
            P("graph"),
            P("graph"),
            P("graph"),
            P("graph"),
            P("graph"),
            P(None, "graph"),
            P(),
            P(),
            P(),
            P(),
            P(),
            P(),
            P(None, None, "irreps"),
        ),
        out_specs=P(None, "irreps", "graph"),
        check_vma=False,
    )
```

```python
import jax
import jax.numpy as jnp
import numpy as np
from jax import lax
from jax.sharding import PartitionSpec as P
from jax.experimental import pallas as pl
from jax.experimental.pallas import tpu as pltpu

CHANNELS = 128
MAX_DEGREE = 6
MAX_ORDER = 2
ROTATED = 29
COEFFS = 49


EPSILON = 1e-06
CUTOFF = 6.0


def order_index(degree, harmonic):
    if harmonic == 0:
        return degree
    first_row = MAX_DEGREE + 1
    for level in range(1, abs(harmonic)):
        first_row = first_row + 2 * (MAX_DEGREE + 1 - level)
    if harmonic < 0:
        first_row = first_row + MAX_DEGREE + 1 - abs(harmonic)
    return first_row + degree - abs(harmonic)


def wigner_start(degree):
    running = 0
    for level in range(degree):
        running = running + (2 * min(level, MAX_ORDER) + 1) * (2 * level + 1)
    return running


def left_dot(weight, values):
    return lax.dot_general(
        weight, values, (((0,), (0,)), ((), ())), preferred_element_type=jnp.float32
    )


def degree_sums(squares):
    return jnp.stack(
        [
            jnp.sum(squares[degree * degree : (degree + 1) ** 2], axis=0)
            for degree in range(MAX_DEGREE + 1)
        ]
    )


def normalize(node_feats, norm_gain, totals):
    levels = MAX_DEGREE + 1
    degree_of = np.repeat(np.arange(levels), 2 * np.arange(levels) + 1)
    entry_counts = (2 * np.arange(levels) + 1) * CHANNELS
    inverse = 1.0 / jnp.sqrt(totals / jnp.asarray(entry_counts, jnp.float32)[:, None] + EPSILON)
    gain_rows = norm_gain[degree_of]
    scale_rows = inverse[degree_of]
    return (node_feats.astype(jnp.float32) * gain_rows[:, :, None] * scale_rows[:, None, :]).astype(
        jnp.bfloat16
    )


def normalize_rows(values, gain_full, totals):
    levels = MAX_DEGREE + 1
    degree_of = np.repeat(np.arange(levels), 2 * np.arange(levels) + 1)
    entry_counts = (2 * np.arange(levels) + 1) * CHANNELS
    inverse = 1.0 / jnp.sqrt(totals / jnp.asarray(entry_counts, jnp.float32)[:, None] + EPSILON)
    gain_rows = gain_full[degree_of]
    scale_rows = inverse[degree_of]
    return (values * gain_rows[:, :, None] * scale_rows[:, None, :]).astype(jnp.bfloat16)


def rotate(source, wig_rows):
    pieces = [None] * ROTATED
    for degree in range(MAX_DEGREE + 1):
        reach_order = min(degree, MAX_ORDER)
        span_cols = 2 * degree + 1
        first_row = wigner_start(degree)
        for position in range(2 * reach_order + 1):
            total = None
            for column in range(span_cols):
                term = wig_rows[first_row + position * span_cols + column][None, :] * source[degree * degree + column]
                total = term if total is None else total + term
            pieces[order_index(degree, position - reach_order)] = total
    return jnp.stack(pieces).astype(jnp.bfloat16)


def unrotate(gated, wig_rows):
    pieces = []
    for degree in range(MAX_DEGREE + 1):
        reach_order = min(degree, MAX_ORDER)
        span_cols = 2 * degree + 1
        first_row = wigner_start(degree)
        for column in range(span_cols):
            total = None
            for position in range(2 * reach_order + 1):
                term = wig_rows[first_row + position * span_cols + column][None, :] * gated[
                    order_index(degree, position - reach_order)
                ]
                total = term if total is None else total + term
            pieces.append(total)
    return jnp.stack(pieces)


def radial_weights(lengths, kind_ids, radial_in, species_table, radial_out):
    basis_count = radial_in.shape[0]
    spacing = CUTOFF / (basis_count - 1)
    centers = jnp.arange(basis_count, dtype=jnp.float32) * spacing
    basis_rows = jnp.exp(
        -0.5 * jnp.square((lengths[None, :] - centers[:, None]) / (2.0 * spacing))
    ).astype(jnp.bfloat16)
    onehot = (
        kind_ids[None, :] == jnp.arange(species_table.shape[0], dtype=jnp.int32)[:, None]
    ).astype(jnp.bfloat16)
    hidden = jax.nn.silu(left_dot(radial_in, basis_rows) + left_dot(species_table, onehot)).astype(
        jnp.bfloat16
    )
    return left_dot(radial_out, hidden)


def convolve(rotated, radial, order_zero, order_one, order_two):
    levels = MAX_DEGREE + 1
    channel_count = rotated.shape[1]
    num_edges = rotated.shape[2]
    lowest = (
        rotated[:levels].astype(jnp.float32).reshape(levels * channel_count, num_edges) * radial
    ).astype(jnp.bfloat16)
    outputs = [left_dot(order_zero, lowest).reshape(levels, channel_count, num_edges)]
    first_row = levels
    for harmonic, weight in ((1, order_one), (2, order_two)):
        span_rows = levels - harmonic
        plus_rows = rotated[first_row : first_row + span_rows].reshape(
            span_rows * channel_count, num_edges
        )
        minus_rows = rotated[first_row + span_rows : first_row + 2 * span_rows].reshape(
            span_rows * channel_count, num_edges
        )
        joined = jnp.concatenate([plus_rows, minus_rows], axis=1)
        real_part = left_dot(weight[0], joined)
        cross_part = left_dot(weight[1], joined)
        outputs.append(
            (real_part[:, :num_edges] - cross_part[:, num_edges:]).reshape(
                span_rows, channel_count, num_edges
            )
        )
        outputs.append(
            (cross_part[:, :num_edges] + real_part[:, num_edges:]).reshape(
                span_rows, channel_count, num_edges
            )
        )
        first_row = first_row + 2 * span_rows
    mixed = jnp.concatenate(outputs, axis=0)
    scalar = mixed[0]
    return jnp.concatenate(
        [jax.nn.silu(scalar)[None], mixed[1:] * jax.nn.sigmoid(scalar)[None]], axis=0
    ).astype(jnp.bfloat16)


def conv_kernel(
    src_ref, wig_ref, length_ref, kind_ref, basis_in_ref, kind_table_ref, radial_out_ref,
    zero_hbm, one_hbm, two_hbm, onehot_ref, out_ref, zero_ref, one_ref, two_ref, copy_sems,
):
    loads = [
        pltpu.make_async_copy(zero_hbm, zero_ref, copy_sems.at[0]),
        pltpu.make_async_copy(one_hbm, one_ref, copy_sems.at[1]),
        pltpu.make_async_copy(two_hbm, two_ref, copy_sems.at[2]),
    ]
    for load in loads:
        load.start()
    levels = MAX_DEGREE + 1
    channel_count = CHANNELS
    num_edges = onehot_ref.shape[0]
    basis_count = basis_in_ref.shape[1]
    wig = wig_ref[...].astype(jnp.float32)
    owners = src_ref.shape[0]
    span_chan = CHANNELS // owners
    turned = [src_ref[r].astype(jnp.float32).T for r in range(owners)]
    base = COEFFS * span_chan
    half = num_edges
    pick = (
        lax.broadcasted_iota(jnp.int32, (half, span_chan), 0) % span_chan
        == lax.broadcasted_iota(jnp.int32, (half, span_chan), 1)
    ) & (lax.broadcasted_iota(jnp.int32, (half, span_chan), 0) < 3 * span_chan)
    pick = pick.astype(jnp.float32)
    gain_at = base + levels * 2 * span_chan
    gain = jnp.concatenate(
        [
            jnp.dot(block[gain_at : gain_at + span_chan], pick, preferred_element_type=jnp.float32)
            for block in turned
        ],
        axis=0,
    )
    projection = []
    for degree in range(levels):
        start = base + degree * 2 * span_chan
        projection.append(
            jnp.concatenate(
                [
                    jnp.concatenate(
                        [block[start : start + span_chan], block[start + span_chan : start + 2 * span_chan]],
                        axis=1,
                    )
                    for block in turned
                ],
                axis=0,
            ).astype(jnp.bfloat16)
        )

    rows = [
        jnp.concatenate([block[j * span_chan : (j + 1) * span_chan] for block in turned], axis=0)
        for j in range(COEFFS)
    ]
    normed = [None] * len(rows)
    for degree in range(levels):
        span = range(degree * degree, (degree + 1) ** 2)
        total = None
        for j in span:
            part = jnp.sum(rows[j] * rows[j], axis=0, keepdims=True)
            total = part if total is None else total + part
        inverse = 1.0 / jnp.sqrt(total / float((2 * degree + 1) * CHANNELS) + EPSILON)
        scale = gain[:, degree : degree + 1]
        for j in span:
            normed[j] = (rows[j] * scale * inverse).astype(jnp.bfloat16).astype(jnp.float32)

    rotated = [None] * ROTATED
    for degree in range(levels):
        reach_order = min(degree, MAX_ORDER)
        span_cols = 2 * degree + 1
        first_row = wigner_start(degree)
        for position in range(2 * reach_order + 1):
            total = None
            for column in range(span_cols):
                row = first_row + position * span_cols + column
                term = wig[row : row + 1, :] * normed[degree * degree + column]
                total = term if total is None else total + term
            rotated[order_index(degree, position - reach_order)] = total.astype(jnp.bfloat16)

    spacing = CUTOFF / (basis_count - 1)
    centers = lax.broadcasted_iota(jnp.int32, (basis_count, num_edges), 0).astype(jnp.float32) * spacing
    basis_rows = jnp.exp(
        -0.5 * jnp.square((length_ref[...] - centers) / (2.0 * spacing))
    ).astype(jnp.bfloat16)
    hidden = jnp.dot(basis_in_ref[...], basis_rows, preferred_element_type=jnp.float32) + jnp.dot(
        kind_table_ref[...], kind_ref[...], preferred_element_type=jnp.float32
    )
    hidden = (hidden * jax.nn.sigmoid(hidden)).astype(jnp.bfloat16)
    radial = jnp.dot(radial_out_ref[...], hidden, preferred_element_type=jnp.float32)

    lowest = jnp.concatenate(
        [
            (rotated[degree].astype(jnp.float32) * radial[degree * channel_count : (degree + 1) * channel_count]).astype(
                jnp.bfloat16
            )
            for degree in range(levels)
        ],
        axis=0,
    )
    loads[0].wait()
    mixed0 = jnp.dot(zero_ref[...], lowest, preferred_element_type=jnp.float32)
    mixed = [mixed0[degree * channel_count : (degree + 1) * channel_count] for degree in range(levels)]
    first_row = levels
    for harmonic, weight_ref, load in ((1, one_ref, loads[1]), (2, two_ref, loads[2])):
        load.wait()
        span_rows = levels - harmonic
        plus_rows = jnp.concatenate(rotated[first_row : first_row + span_rows], axis=0)
        minus_rows = jnp.concatenate(rotated[first_row + span_rows : first_row + 2 * span_rows], axis=0)
        joined = jnp.concatenate([plus_rows, minus_rows], axis=1)
        real_part = jnp.dot(weight_ref[0], joined, preferred_element_type=jnp.float32)
        cross_part = jnp.dot(weight_ref[1], joined, preferred_element_type=jnp.float32)
        new_plus = real_part[:, :num_edges] - cross_part[:, num_edges:]
        new_minus = cross_part[:, :num_edges] + real_part[:, num_edges:]
        mixed += [new_plus[k * channel_count : (k + 1) * channel_count] for k in range(span_rows)]
        mixed += [new_minus[k * channel_count : (k + 1) * channel_count] for k in range(span_rows)]
        first_row = first_row + 2 * span_rows

    scalar = mixed[0]
    gate = jax.nn.sigmoid(scalar)
    gated = [(scalar * gate).astype(jnp.bfloat16).astype(jnp.float32)] + [
        (piece * gate).astype(jnp.bfloat16).astype(jnp.float32) for piece in mixed[1:]
    ]

    messages = []
    for degree in range(levels):
        reach_order = min(degree, MAX_ORDER)
        span_cols = 2 * degree + 1
        first_row = wigner_start(degree)
        for column in range(span_cols):
            total = None
            for position in range(2 * reach_order + 1):
                row = first_row + position * span_cols + column
                term = wig[row : row + 1, :] * gated[order_index(degree, position - reach_order)]
                total = term if total is None else total + term
            messages.append(total)
    stacked = jnp.concatenate(messages, axis=0)
    upper_part = stacked.astype(jnp.bfloat16)
    lower_part = (stacked - upper_part.astype(jnp.float32)).astype(jnp.bfloat16)
    onehot = onehot_ref[...]
    summed = jnp.dot(upper_part, onehot, preferred_element_type=jnp.float32) + jnp.dot(
        lower_part, onehot, preferred_element_type=jnp.float32
    )
    half = span_chan // 2
    pieces = [[] for _ in range(owners)]
    for degree in range(levels):
        weight = projection[degree]
        for j in range(degree * degree, (degree + 1) ** 2):
            piece = summed[j * channel_count : (j + 1) * channel_count]
            high = piece.astype(jnp.bfloat16)
            low = (piece - high.astype(jnp.float32)).astype(jnp.bfloat16)
            both = jnp.dot(weight, jnp.concatenate([high, low], axis=1), preferred_element_type=jnp.float32)
            result = both[:, :num_edges] + both[:, num_edges:]
            for r in range(owners):
                block = result[r * span_chan : (r + 1) * span_chan]
                pieces[r].append(jnp.concatenate([block[:half], block[half:]], axis=1))
    fill = out_ref.shape[1] - COEFFS * half
    for r in range(owners):
        out_ref[r] = jnp.concatenate(
            pieces[r] + [jnp.zeros((fill, out_ref.shape[2]), jnp.float32)], axis=0
        ).astype(out_ref.dtype)


def edge_operands(wig_mine, lengths, kind_onehot, radial_in, species_table, radial_out,
                  order_zero, order_one, order_two, onehot):
    return (
        wig_mine,
        lengths[None, :],
        kind_onehot,
        radial_in.T,
        species_table.T,
        radial_out.T,
        order_zero.T,
        jnp.transpose(order_one, (0, 2, 1)),
        jnp.transpose(order_two, (0, 2, 1)),
        onehot,
    )


def convolve_edges(source, side):
    coeffs, channel_count = COEFFS, CHANNELS
    onehot = side[-1]
    num_edges, atom_count = onehot.shape
    owners = source.shape[0]
    out_rows = 16 * pl.cdiv(coeffs * (channel_count // owners) // 2, 16)
    operands = (source,) + tuple(side)
    radial_in, radial_out = side[3], side[5]
    order_zero, order_one, order_two = side[6], side[7], side[8]
    flops = 2 * num_edges * (order_zero.size + 2 * order_one.size + 2 * order_two.size + radial_out.size + radial_in.size)
    return pl.pallas_call(
        conv_kernel,
        out_shape=jax.ShapeDtypeStruct((owners, out_rows, 2 * atom_count), jnp.bfloat16),
        in_specs=[pl.BlockSpec(memory_space=pltpu.VMEM)] * 7
        + [pl.BlockSpec(memory_space=pl.ANY)] * 3
        + [pl.BlockSpec(memory_space=pltpu.VMEM)],
        out_specs=pl.BlockSpec(memory_space=pltpu.VMEM),
        scratch_shapes=[
            pltpu.VMEM(order_zero.shape, order_zero.dtype),
            pltpu.VMEM(order_one.shape, order_one.dtype),
            pltpu.VMEM(order_two.shape, order_two.dtype),
            pltpu.SemaphoreType.DMA((3,)),
        ],
        cost_estimate=pl.CostEstimate(
            flops=flops,
            transcendentals=num_edges * (radial_in.shape[1] + 2 * channel_count),
            bytes_accessed=sum(int(x.size) * x.dtype.itemsize for x in operands) + owners * out_rows * atom_count * 4,
        ),
    )(*operands)


def gather_kernel(index_ref, local_ref, arrived_ref, extra_ref, *refs):
    out_ref = refs[-1]
    owners, per_owner, row_width = out_ref.shape
    row_used = local_ref.shape[1]
    table = jnp.concatenate([local_ref[...], arrived_ref[...]], axis=0)
    hot = (
        index_ref[...] == lax.broadcasted_iota(jnp.int32, (index_ref.shape[0], table.shape[0]), 1)
    ).astype(jnp.bfloat16)
    picked = jnp.dot(hot, table, preferred_element_type=jnp.float32).astype(out_ref.dtype)
    extra = extra_ref[...]
    for q in range(owners):
        out_ref[q, :, 0:row_used] = picked[q * per_owner : (q + 1) * per_owner]
        out_ref[q, :, row_used:row_width] = extra


def gather_rows(edge_source, node_rows, arrived, extra, owners, row_width, side):
    per_owner = edge_source.shape[0] // owners
    operands = (edge_source[:, None], node_rows, arrived, extra)
    return pl.pallas_call(
        gather_kernel,
        out_shape=jax.ShapeDtypeStruct((owners, per_owner, row_width), jnp.bfloat16),
        in_specs=[pl.BlockSpec(memory_space=pltpu.VMEM)] * len(operands)
        + [pl.BlockSpec(memory_space=pl.ANY)] * len(side),
        out_specs=pl.BlockSpec(memory_space=pltpu.VMEM),
        cost_estimate=pl.CostEstimate(
            flops=2 * edge_source.shape[0] * (node_rows.shape[0] + arrived.shape[0]) * node_rows.shape[1],
            transcendentals=0,
            bytes_accessed=sum(int(x.size) * x.dtype.itemsize for x in operands)
            + owners * per_owner * row_width * 2,
        ),
    )(*operands, *side)


def split_dot(values, weight):
    upper_part = values.astype(jnp.bfloat16)
    lower_part = (values - upper_part.astype(jnp.float32)).astype(jnp.bfloat16)
    return jnp.dot(upper_part, weight, preferred_element_type=jnp.float32) + jnp.dot(
        lower_part, weight, preferred_element_type=jnp.float32
    )


def body(
    node_feats,
    norm_gain,
    species,
    send_list,
    edge_source,
    edge_target,
    edge_count,
    edge_length,
    wigner,
    radial_in,
    species_table,
    radial_out,
    order_zero,
    order_one,
    order_two,
    project_weight,
):
    levels = MAX_DEGREE + 1
    owners = lax.axis_size("irreps")
    quarter = lax.axis_index("irreps")
    coeffs, span_chan, atom_count = node_feats.shape
    per_owner = edge_source.shape[0] // owners
    first_edge = quarter * per_owner

    row_used = coeffs * span_chan
    row_width = 128 * pl.cdiv(row_used, 128)
    node_rows = node_feats.reshape(row_used, atom_count).T
    send_hot = (send_list[:, None] == jnp.arange(atom_count, dtype=jnp.int32)[None, :]).astype(jnp.bfloat16)
    outgoing_rows = lax.dot_general(
        send_hot, node_feats.reshape(row_used, atom_count), (((1,), (1,)), ((), ())),
        preferred_element_type=jnp.float32,
    ).astype(jnp.bfloat16)
    arrived = lax.all_to_all(outgoing_rows, "graph", 0, 0, tiled=True)

    gain_high = lax.reduce_precision(norm_gain, exponent_bits=8, mantissa_bits=7)
    gain_rest = norm_gain - gain_high
    gain_mid = lax.reduce_precision(gain_rest, exponent_bits=8, mantissa_bits=7)
    gain_low = gain_rest - gain_mid
    gain_block = jnp.transpose(jnp.stack([gain_high, gain_mid, gain_low]), (2, 0, 1))
    gain_block = jnp.pad(gain_block, ((0, 0), (0, 0), (0, 1))).reshape(span_chan, 3 * (levels + 1))
    gain_block = jnp.pad(gain_block, ((0, 0), (0, per_owner - gain_block.shape[1]))).astype(jnp.bfloat16)
    pair_order = np.concatenate([np.arange(0, span_chan, 2), np.arange(1, span_chan, 2)])
    weight_block = jnp.transpose(
        project_weight[:, :, pair_order].reshape(levels, CHANNELS // per_owner, per_owner, span_chan), (0, 1, 3, 2)
    ).reshape(-1, per_owner)
    extra = jnp.concatenate([weight_block, gain_block], axis=0).T

    wig_mine = lax.dynamic_slice_in_dim(wigner, first_edge, per_owner, 1)
    targets_mine = lax.dynamic_slice_in_dim(edge_target, first_edge, per_owner)
    lengths_mine = lax.dynamic_slice_in_dim(edge_length, first_edge, per_owner)
    kinds = species[targets_mine]
    kind_onehot = (
        kinds[None, :] == jnp.arange(species_table.shape[0], dtype=jnp.int32)[:, None]
    ).astype(jnp.bfloat16)
    edge_weight = jnp.where(
        first_edge + jnp.arange(per_owner, dtype=jnp.int32) < edge_count[0], 0.25, 0.0
    ).astype(jnp.float32)
    onehot = jnp.where(
        targets_mine[:, None] == jnp.arange(atom_count, dtype=jnp.int32)[None, :],
        edge_weight[:, None],
        0.0,
    ).astype(jnp.bfloat16)
    side = edge_operands(
        wig_mine, lengths_mine, kind_onehot, radial_in, species_table, radial_out,
        order_zero, order_one, order_two, onehot,
    )
    outgoing = gather_rows(edge_source, node_rows, arrived, extra, owners, row_width, side)
    source = lax.all_to_all(outgoing, "irreps", 0, 0, tiled=True)
    projected = convolve_edges(source, side)
    returned = lax.all_to_all(projected, "irreps", 0, 0, tiled=True)
    total = jnp.sum(returned.astype(jnp.float32), axis=0)[: coeffs * span_chan // 2]
    total = total.reshape(coeffs, span_chan // 2, 2, atom_count).reshape(coeffs, span_chan, atom_count)
    return (node_feats.astype(jnp.float32) + total).astype(jnp.bfloat16)


def solution(mesh):
    return jax.shard_map(
        body,
        mesh=mesh,
        in_specs=(
            P(None, "irreps", "graph"),
            P(None, "irreps"),
            P("graph"),
            P("graph"),
            P("graph"),
            P("graph"),
            P("graph"),
            P("graph"),
            P(None, "graph"),
            P(),
            P(),
            P(),
            P(),
            P(),
            P(),
            P(None, None, "irreps"),
        ),
        out_specs=P(None, "irreps", "graph"),
        check_vma=False,
    )
```

```python
import jax
import jax.numpy as jnp
import numpy as np
from jax import lax
from jax.sharding import PartitionSpec as P
from jax.experimental import pallas as pl
from jax.experimental.pallas import tpu as pltpu

CHANNELS = 128
MAX_DEGREE = 6
MAX_ORDER = 2
ROTATED = 29
COEFFS = 49


EPSILON = 1e-06
CUTOFF = 6.0


def order_index(degree, harmonic):
    if harmonic == 0:
        return degree
    first_row = MAX_DEGREE + 1
    for level in range(1, abs(harmonic)):
        first_row = first_row + 2 * (MAX_DEGREE + 1 - level)
    if harmonic < 0:
        first_row = first_row + MAX_DEGREE + 1 - abs(harmonic)
    return first_row + degree - abs(harmonic)


def wigner_start(degree):
    running = 0
    for level in range(degree):
        running = running + (2 * min(level, MAX_ORDER) + 1) * (2 * level + 1)
    return running


def left_dot(weight, values):
    return lax.dot_general(
        weight, values, (((0,), (0,)), ((), ())), preferred_element_type=jnp.float32
    )


def degree_sums(squares):
    return jnp.stack(
        [
            jnp.sum(squares[degree * degree : (degree + 1) ** 2], axis=0)
            for degree in range(MAX_DEGREE + 1)
        ]
    )


def normalize(node_feats, norm_gain, totals):
    levels = MAX_DEGREE + 1
    degree_of = np.repeat(np.arange(levels), 2 * np.arange(levels) + 1)
    entry_counts = (2 * np.arange(levels) + 1) * CHANNELS
    inverse = 1.0 / jnp.sqrt(totals / jnp.asarray(entry_counts, jnp.float32)[:, None] + EPSILON)
    gain_rows = norm_gain[degree_of]
    scale_rows = inverse[degree_of]
    return (node_feats.astype(jnp.float32) * gain_rows[:, :, None] * scale_rows[:, None, :]).astype(
        jnp.bfloat16
    )


def normalize_rows(values, gain_full, totals):
    levels = MAX_DEGREE + 1
    degree_of = np.repeat(np.arange(levels), 2 * np.arange(levels) + 1)
    entry_counts = (2 * np.arange(levels) + 1) * CHANNELS
    inverse = 1.0 / jnp.sqrt(totals / jnp.asarray(entry_counts, jnp.float32)[:, None] + EPSILON)
    gain_rows = gain_full[degree_of]
    scale_rows = inverse[degree_of]
    return (values * gain_rows[:, :, None] * scale_rows[:, None, :]).astype(jnp.bfloat16)


def rotate(source, wig_rows):
    pieces = [None] * ROTATED
    for degree in range(MAX_DEGREE + 1):
        reach_order = min(degree, MAX_ORDER)
        span_cols = 2 * degree + 1
        first_row = wigner_start(degree)
        for position in range(2 * reach_order + 1):
            total = None
            for column in range(span_cols):
                term = wig_rows[first_row + position * span_cols + column][None, :] * source[degree * degree + column]
                total = term if total is None else total + term
            pieces[order_index(degree, position - reach_order)] = total
    return jnp.stack(pieces).astype(jnp.bfloat16)


def unrotate(gated, wig_rows):
    pieces = []
    for degree in range(MAX_DEGREE + 1):
        reach_order = min(degree, MAX_ORDER)
        span_cols = 2 * degree + 1
        first_row = wigner_start(degree)
        for column in range(span_cols):
            total = None
            for position in range(2 * reach_order + 1):
                term = wig_rows[first_row + position * span_cols + column][None, :] * gated[
                    order_index(degree, position - reach_order)
                ]
                total = term if total is None else total + term
            pieces.append(total)
    return jnp.stack(pieces)


def radial_weights(lengths, kind_ids, radial_in, species_table, radial_out):
    basis_count = radial_in.shape[0]
    spacing = CUTOFF / (basis_count - 1)
    centers = jnp.arange(basis_count, dtype=jnp.float32) * spacing
    basis_rows = jnp.exp(
        -0.5 * jnp.square((lengths[None, :] - centers[:, None]) / (2.0 * spacing))
    ).astype(jnp.bfloat16)
    onehot = (
        kind_ids[None, :] == jnp.arange(species_table.shape[0], dtype=jnp.int32)[:, None]
    ).astype(jnp.bfloat16)
    hidden = jax.nn.silu(left_dot(radial_in, basis_rows) + left_dot(species_table, onehot)).astype(
        jnp.bfloat16
    )
    return left_dot(radial_out, hidden)


def convolve(rotated, radial, order_zero, order_one, order_two):
    levels = MAX_DEGREE + 1
    channel_count = rotated.shape[1]
    num_edges = rotated.shape[2]
    lowest = (
        rotated[:levels].astype(jnp.float32).reshape(levels * channel_count, num_edges) * radial
    ).astype(jnp.bfloat16)
    outputs = [left_dot(order_zero, lowest).reshape(levels, channel_count, num_edges)]
    first_row = levels
    for harmonic, weight in ((1, order_one), (2, order_two)):
        span_rows = levels - harmonic
        plus_rows = rotated[first_row : first_row + span_rows].reshape(
            span_rows * channel_count, num_edges
        )
        minus_rows = rotated[first_row + span_rows : first_row + 2 * span_rows].reshape(
            span_rows * channel_count, num_edges
        )
        joined = jnp.concatenate([plus_rows, minus_rows], axis=1)
        real_part = left_dot(weight[0], joined)
        cross_part = left_dot(weight[1], joined)
        outputs.append(
            (real_part[:, :num_edges] - cross_part[:, num_edges:]).reshape(
                span_rows, channel_count, num_edges
            )
        )
        outputs.append(
            (cross_part[:, :num_edges] + real_part[:, num_edges:]).reshape(
                span_rows, channel_count, num_edges
            )
        )
        first_row = first_row + 2 * span_rows
    mixed = jnp.concatenate(outputs, axis=0)
    scalar = mixed[0]
    return jnp.concatenate(
        [jax.nn.silu(scalar)[None], mixed[1:] * jax.nn.sigmoid(scalar)[None]], axis=0
    ).astype(jnp.bfloat16)


def conv_kernel(
    src_ref, wig_ref, length_ref, kind_ref, basis_in_ref, kind_table_ref, radial_out_ref,
    zero_hbm, one_hbm, two_hbm, onehot_ref, out_ref, zero_ref, one_ref, two_ref, copy_sems,
):
    loads = [
        pltpu.make_async_copy(zero_hbm, zero_ref, copy_sems.at[0]),
        pltpu.make_async_copy(one_hbm, one_ref, copy_sems.at[1]),
        pltpu.make_async_copy(two_hbm, two_ref, copy_sems.at[2]),
    ]
    for load in loads:
        load.start()
    levels = MAX_DEGREE + 1
    channel_count = CHANNELS
    num_edges = onehot_ref.shape[0]
    basis_count = basis_in_ref.shape[1]
    wig = wig_ref[...].astype(jnp.float32)
    owners = src_ref.shape[0]
    span_chan = CHANNELS // owners
    turned = [src_ref[r].astype(jnp.float32).T for r in range(owners)]
    base = COEFFS * span_chan
    half = num_edges
    pick = (
        lax.broadcasted_iota(jnp.int32, (half, span_chan), 0) % span_chan
        == lax.broadcasted_iota(jnp.int32, (half, span_chan), 1)
    ) & (lax.broadcasted_iota(jnp.int32, (half, span_chan), 0) < 3 * span_chan)
    pick = pick.astype(jnp.float32)
    gain_at = base + levels * 2 * span_chan
    gain = jnp.concatenate(
        [
            jnp.dot(block[gain_at : gain_at + span_chan], pick, preferred_element_type=jnp.float32)
            for block in turned
        ],
        axis=0,
    )
    projection = []
    for degree in range(levels):
        start = base + degree * 2 * span_chan
        projection.append(
            jnp.concatenate(
                [
                    jnp.concatenate(
                        [block[start : start + span_chan], block[start + span_chan : start + 2 * span_chan]],
                        axis=1,
                    )
                    for block in turned
                ],
                axis=0,
            ).astype(jnp.bfloat16)
        )

    rows = [
        jnp.concatenate([block[j * span_chan : (j + 1) * span_chan] for block in turned], axis=0)
        for j in range(COEFFS)
    ]
    normed = [None] * len(rows)
    for degree in range(levels):
        span = range(degree * degree, (degree + 1) ** 2)
        total = None
        for j in span:
            part = jnp.sum(rows[j] * rows[j], axis=0, keepdims=True)
            total = part if total is None else total + part
        inverse = 1.0 / jnp.sqrt(total / float((2 * degree + 1) * CHANNELS) + EPSILON)
        scale = gain[:, degree : degree + 1]
        for j in span:
            normed[j] = (rows[j] * scale * inverse).astype(jnp.bfloat16).astype(jnp.float32)

    rotated = [None] * ROTATED
    for degree in range(levels):
        reach_order = min(degree, MAX_ORDER)
        span_cols = 2 * degree + 1
        first_row = wigner_start(degree)
        for position in range(2 * reach_order + 1):
            total = None
            for column in range(span_cols):
                row = first_row + position * span_cols + column
                term = wig[row : row + 1, :] * normed[degree * degree + column]
                total = term if total is None else total + term
            rotated[order_index(degree, position - reach_order)] = total.astype(jnp.bfloat16)

    spacing = CUTOFF / (basis_count - 1)
    centers = lax.broadcasted_iota(jnp.int32, (basis_count, num_edges), 0).astype(jnp.float32) * spacing
    basis_rows = jnp.exp(
        -0.5 * jnp.square((length_ref[...] - centers) / (2.0 * spacing))
    ).astype(jnp.bfloat16)
    hidden = jnp.dot(basis_in_ref[...], basis_rows, preferred_element_type=jnp.float32) + jnp.dot(
        kind_table_ref[...], kind_ref[...], preferred_element_type=jnp.float32
    )
    hidden = (hidden * jax.nn.sigmoid(hidden)).astype(jnp.bfloat16)
    radial = jnp.dot(radial_out_ref[...], hidden, preferred_element_type=jnp.float32)

    lowest = jnp.concatenate(
        [
            (rotated[degree].astype(jnp.float32) * radial[degree * channel_count : (degree + 1) * channel_count]).astype(
                jnp.bfloat16
            )
            for degree in range(levels)
        ],
        axis=0,
    )
    loads[0].wait()
    mixed0 = jnp.dot(zero_ref[...], lowest, preferred_element_type=jnp.float32)
    mixed = [mixed0[degree * channel_count : (degree + 1) * channel_count] for degree in range(levels)]
    first_row = levels
    for harmonic, weight_ref, load in ((1, one_ref, loads[1]), (2, two_ref, loads[2])):
        load.wait()
        span_rows = levels - harmonic
        plus_rows = jnp.concatenate(rotated[first_row : first_row + span_rows], axis=0)
        minus_rows = jnp.concatenate(rotated[first_row + span_rows : first_row + 2 * span_rows], axis=0)
        joined = jnp.concatenate([plus_rows, minus_rows], axis=1)
        real_part = jnp.dot(weight_ref[0], joined, preferred_element_type=jnp.float32)
        cross_part = jnp.dot(weight_ref[1], joined, preferred_element_type=jnp.float32)
        new_plus = real_part[:, :num_edges] - cross_part[:, num_edges:]
        new_minus = cross_part[:, :num_edges] + real_part[:, num_edges:]
        mixed += [new_plus[k * channel_count : (k + 1) * channel_count] for k in range(span_rows)]
        mixed += [new_minus[k * channel_count : (k + 1) * channel_count] for k in range(span_rows)]
        first_row = first_row + 2 * span_rows

    scalar = mixed[0]
    gate = jax.nn.sigmoid(scalar)
    gated = [(scalar * gate).astype(jnp.bfloat16).astype(jnp.float32)] + [
        (piece * gate).astype(jnp.bfloat16).astype(jnp.float32) for piece in mixed[1:]
    ]

    messages = []
    for degree in range(levels):
        reach_order = min(degree, MAX_ORDER)
        span_cols = 2 * degree + 1
        first_row = wigner_start(degree)
        for column in range(span_cols):
            total = None
            for position in range(2 * reach_order + 1):
                row = first_row + position * span_cols + column
                term = wig[row : row + 1, :] * gated[order_index(degree, position - reach_order)]
                total = term if total is None else total + term
            messages.append(total)
    stacked = jnp.concatenate(messages, axis=0)
    upper_part = stacked.astype(jnp.bfloat16)
    lower_part = (stacked - upper_part.astype(jnp.float32)).astype(jnp.bfloat16)
    onehot = onehot_ref[...]
    summed = jnp.dot(upper_part, onehot, preferred_element_type=jnp.float32) + jnp.dot(
        lower_part, onehot, preferred_element_type=jnp.float32
    )
    half = span_chan // 2
    pieces = [[] for _ in range(owners)]
    for degree in range(levels):
        weight = projection[degree]
        for j in range(degree * degree, (degree + 1) ** 2):
            piece = summed[j * channel_count : (j + 1) * channel_count]
            high = piece.astype(jnp.bfloat16)
            low = (piece - high.astype(jnp.float32)).astype(jnp.bfloat16)
            both = jnp.dot(weight, jnp.concatenate([high, low], axis=1), preferred_element_type=jnp.float32)
            result = both[:, :num_edges] + both[:, num_edges:]
            for r in range(owners):
                block = result[r * span_chan : (r + 1) * span_chan]
                pieces[r].append(jnp.concatenate([block[:half], block[half:]], axis=1))
    fill = out_ref.shape[1] - COEFFS * half
    for r in range(owners):
        out_ref[r] = jnp.concatenate(
            pieces[r] + [jnp.zeros((fill, out_ref.shape[2]), jnp.float32)], axis=0
        ).astype(out_ref.dtype)


def edge_operands(wig_mine, lengths, kind_onehot, radial_in, species_table, radial_out,
                  order_zero, order_one, order_two, onehot):
    return (
        wig_mine,
        lengths[None, :],
        kind_onehot,
        radial_in.T,
        species_table.T,
        radial_out.T,
        order_zero.T,
        jnp.transpose(order_one, (0, 2, 1)),
        jnp.transpose(order_two, (0, 2, 1)),
        onehot,
    )


def convolve_edges(source, side):
    coeffs, channel_count = COEFFS, CHANNELS
    onehot = side[-1]
    num_edges, atom_count = onehot.shape
    owners = source.shape[0]
    out_rows = 16 * pl.cdiv(coeffs * (channel_count // owners) // 2, 16)
    operands = (source,) + tuple(side)
    radial_in, radial_out = side[3], side[5]
    order_zero, order_one, order_two = side[6], side[7], side[8]
    flops = 2 * num_edges * (order_zero.size + 2 * order_one.size + 2 * order_two.size + radial_out.size + radial_in.size)
    return pl.pallas_call(
        conv_kernel,
        out_shape=jax.ShapeDtypeStruct((owners, out_rows, 2 * atom_count), jnp.bfloat16),
        in_specs=[pl.BlockSpec(memory_space=pltpu.VMEM)] * 7
        + [pl.BlockSpec(memory_space=pl.ANY)] * 3
        + [pl.BlockSpec(memory_space=pltpu.VMEM)],
        out_specs=pl.BlockSpec(memory_space=pltpu.VMEM),
        scratch_shapes=[
            pltpu.VMEM(order_zero.shape, order_zero.dtype),
            pltpu.VMEM(order_one.shape, order_one.dtype),
            pltpu.VMEM(order_two.shape, order_two.dtype),
            pltpu.SemaphoreType.DMA((3,)),
        ],
        cost_estimate=pl.CostEstimate(
            flops=flops,
            transcendentals=num_edges * (radial_in.shape[1] + 2 * channel_count),
            bytes_accessed=sum(int(x.size) * x.dtype.itemsize for x in operands) + owners * out_rows * atom_count * 4,
        ),
    )(*operands)


def send_kernel(index_ref, feats_ref, out_ref):
    hot = (
        index_ref[...] == lax.broadcasted_iota(jnp.int32, (index_ref.shape[0], feats_ref.shape[1]), 1)
    ).astype(feats_ref.dtype)
    out_ref[...] = lax.dot_general(
        hot, feats_ref[...], (((1,), (1,)), ((), ())), preferred_element_type=jnp.float32
    ).astype(out_ref.dtype)


def send_rows(send_list, feats):
    return pl.pallas_call(
        send_kernel,
        out_shape=jax.ShapeDtypeStruct((send_list.shape[0], feats.shape[0]), feats.dtype),
        in_specs=[pl.BlockSpec(memory_space=pltpu.VMEM)] * 2,
        out_specs=pl.BlockSpec(memory_space=pltpu.VMEM),
    )(send_list[:, None], feats)


def gather_kernel(index_ref, local_ref, arrived_ref, extra_ref, *refs):
    out_ref = refs[-1]
    owners, per_owner, row_width = out_ref.shape
    row_used = local_ref.shape[1]
    table = jnp.concatenate([local_ref[...], arrived_ref[...]], axis=0)
    hot = (
        index_ref[...] == lax.broadcasted_iota(jnp.int32, (index_ref.shape[0], table.shape[0]), 1)
    ).astype(jnp.bfloat16)
    picked = jnp.dot(hot, table, preferred_element_type=jnp.float32).astype(out_ref.dtype)
    extra = extra_ref[...]
    for q in range(owners):
        out_ref[q, :, 0:row_used] = picked[q * per_owner : (q + 1) * per_owner]
        out_ref[q, :, row_used:row_width] = extra


def gather_rows(edge_source, node_rows, arrived, extra, owners, row_width, side):
    per_owner = edge_source.shape[0] // owners
    operands = (edge_source[:, None], node_rows, arrived, extra)
    return pl.pallas_call(
        gather_kernel,
        out_shape=jax.ShapeDtypeStruct((owners, per_owner, row_width), jnp.bfloat16),
        in_specs=[pl.BlockSpec(memory_space=pltpu.VMEM)] * len(operands)
        + [pl.BlockSpec(memory_space=pl.ANY)] * len(side),
        out_specs=pl.BlockSpec(memory_space=pltpu.VMEM),
        cost_estimate=pl.CostEstimate(
            flops=2 * edge_source.shape[0] * (node_rows.shape[0] + arrived.shape[0]) * node_rows.shape[1],
            transcendentals=0,
            bytes_accessed=sum(int(x.size) * x.dtype.itemsize for x in operands)
            + owners * per_owner * row_width * 2,
        ),
    )(*operands, *side)


def split_dot(values, weight):
    upper_part = values.astype(jnp.bfloat16)
    lower_part = (values - upper_part.astype(jnp.float32)).astype(jnp.bfloat16)
    return jnp.dot(upper_part, weight, preferred_element_type=jnp.float32) + jnp.dot(
        lower_part, weight, preferred_element_type=jnp.float32
    )


def body(
    node_feats,
    norm_gain,
    species,
    send_list,
    edge_source,
    edge_target,
    edge_count,
    edge_length,
    wigner,
    radial_in,
    species_table,
    radial_out,
    order_zero,
    order_one,
    order_two,
    project_weight,
):
    levels = MAX_DEGREE + 1
    owners = lax.axis_size("irreps")
    quarter = lax.axis_index("irreps")
    coeffs, span_chan, atom_count = node_feats.shape
    per_owner = edge_source.shape[0] // owners
    first_edge = quarter * per_owner

    row_used = coeffs * span_chan
    row_width = 128 * pl.cdiv(row_used, 128)
    node_rows = node_feats.reshape(row_used, atom_count).T
    outgoing_rows = send_rows(send_list, node_feats.reshape(row_used, atom_count))
    arrived = lax.all_to_all(outgoing_rows, "graph", 0, 0, tiled=True)

    gain_high = lax.reduce_precision(norm_gain, exponent_bits=8, mantissa_bits=7)
    gain_rest = norm_gain - gain_high
    gain_mid = lax.reduce_precision(gain_rest, exponent_bits=8, mantissa_bits=7)
    gain_low = gain_rest - gain_mid
    gain_block = jnp.transpose(jnp.stack([gain_high, gain_mid, gain_low]), (2, 0, 1))
    gain_block = jnp.pad(gain_block, ((0, 0), (0, 0), (0, 1))).reshape(span_chan, 3 * (levels + 1))
    gain_block = jnp.pad(gain_block, ((0, 0), (0, per_owner - gain_block.shape[1]))).astype(jnp.bfloat16)
    pair_order = np.concatenate([np.arange(0, span_chan, 2), np.arange(1, span_chan, 2)])
    weight_block = jnp.transpose(
        project_weight[:, :, pair_order].reshape(levels, CHANNELS // per_owner, per_owner, span_chan), (0, 1, 3, 2)
    ).reshape(-1, per_owner)
    extra = jnp.concatenate([weight_block, gain_block], axis=0).T

    wig_mine = lax.dynamic_slice_in_dim(wigner, first_edge, per_owner, 1)
    targets_mine = lax.dynamic_slice_in_dim(edge_target, first_edge, per_owner)
    lengths_mine = lax.dynamic_slice_in_dim(edge_length, first_edge, per_owner)
    kinds = species[targets_mine]
    kind_onehot = (
        kinds[None, :] == jnp.arange(species_table.shape[0], dtype=jnp.int32)[:, None]
    ).astype(jnp.bfloat16)
    edge_weight = jnp.where(
        first_edge + jnp.arange(per_owner, dtype=jnp.int32) < edge_count[0], 0.25, 0.0
    ).astype(jnp.float32)
    onehot = jnp.where(
        targets_mine[:, None] == jnp.arange(atom_count, dtype=jnp.int32)[None, :],
        edge_weight[:, None],
        0.0,
    ).astype(jnp.bfloat16)
    side = edge_operands(
        wig_mine, lengths_mine, kind_onehot, radial_in, species_table, radial_out,
        order_zero, order_one, order_two, onehot,
    )
    outgoing = gather_rows(edge_source, node_rows, arrived, extra, owners, row_width, side)
    source = lax.all_to_all(outgoing, "irreps", 0, 0, tiled=True)
    projected = convolve_edges(source, side)
    returned = lax.all_to_all(projected, "irreps", 0, 0, tiled=True)
    total = jnp.sum(returned.astype(jnp.float32), axis=0)[: coeffs * span_chan // 2]
    total = total.reshape(coeffs, span_chan // 2, 2, atom_count).reshape(coeffs, span_chan, atom_count)
    return (node_feats.astype(jnp.float32) + total).astype(jnp.bfloat16)


def solution(mesh):
    return jax.shard_map(
        body,
        mesh=mesh,
        in_specs=(
            P(None, "irreps", "graph"),
            P(None, "irreps"),
            P("graph"),
            P("graph"),
            P("graph"),
            P("graph"),
            P("graph"),
            P("graph"),
            P(None, "graph"),
            P(),
            P(),
            P(),
            P(),
            P(),
            P(),
            P(None, None, "irreps"),
        ),
        out_specs=P(None, "irreps", "graph"),
        check_vma=False,
    )
```

```python
import jax
import jax.numpy as jnp
import numpy as np
from jax import lax
from jax.sharding import PartitionSpec as P
from jax.experimental import pallas as pl
from jax.experimental.pallas import tpu as pltpu

CHANNELS = 128
MAX_DEGREE = 6
MAX_ORDER = 2
ROTATED = 29
COEFFS = 49


EPSILON = 1e-06
CUTOFF = 6.0


def order_index(degree, harmonic):
    if harmonic == 0:
        return degree
    first_row = MAX_DEGREE + 1
    for level in range(1, abs(harmonic)):
        first_row = first_row + 2 * (MAX_DEGREE + 1 - level)
    if harmonic < 0:
        first_row = first_row + MAX_DEGREE + 1 - abs(harmonic)
    return first_row + degree - abs(harmonic)


def wigner_start(degree):
    running = 0
    for level in range(degree):
        running = running + (2 * min(level, MAX_ORDER) + 1) * (2 * level + 1)
    return running


def left_dot(weight, values):
    return lax.dot_general(
        weight, values, (((0,), (0,)), ((), ())), preferred_element_type=jnp.float32
    )


def degree_sums(squares):
    return jnp.stack(
        [
            jnp.sum(squares[degree * degree : (degree + 1) ** 2], axis=0)
            for degree in range(MAX_DEGREE + 1)
        ]
    )


def normalize(node_feats, norm_gain, totals):
    levels = MAX_DEGREE + 1
    degree_of = np.repeat(np.arange(levels), 2 * np.arange(levels) + 1)
    entry_counts = (2 * np.arange(levels) + 1) * CHANNELS
    inverse = 1.0 / jnp.sqrt(totals / jnp.asarray(entry_counts, jnp.float32)[:, None] + EPSILON)
    gain_rows = norm_gain[degree_of]
    scale_rows = inverse[degree_of]
    return (node_feats.astype(jnp.float32) * gain_rows[:, :, None] * scale_rows[:, None, :]).astype(
        jnp.bfloat16
    )


def normalize_rows(values, gain_full, totals):
    levels = MAX_DEGREE + 1
    degree_of = np.repeat(np.arange(levels), 2 * np.arange(levels) + 1)
    entry_counts = (2 * np.arange(levels) + 1) * CHANNELS
    inverse = 1.0 / jnp.sqrt(totals / jnp.asarray(entry_counts, jnp.float32)[:, None] + EPSILON)
    gain_rows = gain_full[degree_of]
    scale_rows = inverse[degree_of]
    return (values * gain_rows[:, :, None] * scale_rows[:, None, :]).astype(jnp.bfloat16)


def rotate(source, wig_rows):
    pieces = [None] * ROTATED
    for degree in range(MAX_DEGREE + 1):
        reach_order = min(degree, MAX_ORDER)
        span_cols = 2 * degree + 1
        first_row = wigner_start(degree)
        for position in range(2 * reach_order + 1):
            total = None
            for column in range(span_cols):
                term = wig_rows[first_row + position * span_cols + column][None, :] * source[degree * degree + column]
                total = term if total is None else total + term
            pieces[order_index(degree, position - reach_order)] = total
    return jnp.stack(pieces).astype(jnp.bfloat16)


def unrotate(gated, wig_rows):
    pieces = []
    for degree in range(MAX_DEGREE + 1):
        reach_order = min(degree, MAX_ORDER)
        span_cols = 2 * degree + 1
        first_row = wigner_start(degree)
        for column in range(span_cols):
            total = None
            for position in range(2 * reach_order + 1):
                term = wig_rows[first_row + position * span_cols + column][None, :] * gated[
                    order_index(degree, position - reach_order)
                ]
                total = term if total is None else total + term
            pieces.append(total)
    return jnp.stack(pieces)


def radial_weights(lengths, kind_ids, radial_in, species_table, radial_out):
    basis_count = radial_in.shape[0]
    spacing = CUTOFF / (basis_count - 1)
    centers = jnp.arange(basis_count, dtype=jnp.float32) * spacing
    basis_rows = jnp.exp(
        -0.5 * jnp.square((lengths[None, :] - centers[:, None]) / (2.0 * spacing))
    ).astype(jnp.bfloat16)
    onehot = (
        kind_ids[None, :] == jnp.arange(species_table.shape[0], dtype=jnp.int32)[:, None]
    ).astype(jnp.bfloat16)
    hidden = jax.nn.silu(left_dot(radial_in, basis_rows) + left_dot(species_table, onehot)).astype(
        jnp.bfloat16
    )
    return left_dot(radial_out, hidden)


def convolve(rotated, radial, order_zero, order_one, order_two):
    levels = MAX_DEGREE + 1
    channel_count = rotated.shape[1]
    num_edges = rotated.shape[2]
    lowest = (
        rotated[:levels].astype(jnp.float32).reshape(levels * channel_count, num_edges) * radial
    ).astype(jnp.bfloat16)
    outputs = [left_dot(order_zero, lowest).reshape(levels, channel_count, num_edges)]
    first_row = levels
    for harmonic, weight in ((1, order_one), (2, order_two)):
        span_rows = levels - harmonic
        plus_rows = rotated[first_row : first_row + span_rows].reshape(
            span_rows * channel_count, num_edges
        )
        minus_rows = rotated[first_row + span_rows : first_row + 2 * span_rows].reshape(
            span_rows * channel_count, num_edges
        )
        joined = jnp.concatenate([plus_rows, minus_rows], axis=1)
        real_part = left_dot(weight[0], joined)
        cross_part = left_dot(weight[1], joined)
        outputs.append(
            (real_part[:, :num_edges] - cross_part[:, num_edges:]).reshape(
                span_rows, channel_count, num_edges
            )
        )
        outputs.append(
            (cross_part[:, :num_edges] + real_part[:, num_edges:]).reshape(
                span_rows, channel_count, num_edges
            )
        )
        first_row = first_row + 2 * span_rows
    mixed = jnp.concatenate(outputs, axis=0)
    scalar = mixed[0]
    return jnp.concatenate(
        [jax.nn.silu(scalar)[None], mixed[1:] * jax.nn.sigmoid(scalar)[None]], axis=0
    ).astype(jnp.bfloat16)


def conv_kernel(
    src_ref, wig_ref, length_ref, kind_ref, basis_in_ref, kind_table_ref, radial_out_ref,
    zero_hbm, one_hbm, two_hbm, onehot_ref, out_ref, zero_ref, one_ref, two_ref, copy_sems,
):
    loads = [
        pltpu.make_async_copy(zero_hbm, zero_ref, copy_sems.at[0]),
        pltpu.make_async_copy(one_hbm, one_ref, copy_sems.at[1]),
        pltpu.make_async_copy(two_hbm, two_ref, copy_sems.at[2]),
    ]
    for load in loads:
        load.start()
    levels = MAX_DEGREE + 1
    channel_count = CHANNELS
    num_edges = onehot_ref.shape[0]
    basis_count = basis_in_ref.shape[1]
    wig = wig_ref[...].astype(jnp.float32)
    owners = src_ref.shape[0]
    span_chan = CHANNELS // owners
    turned = [src_ref[r].astype(jnp.float32).T for r in range(owners)]
    base = COEFFS * span_chan
    half = num_edges
    pick = (
        lax.broadcasted_iota(jnp.int32, (half, span_chan), 0) % span_chan
        == lax.broadcasted_iota(jnp.int32, (half, span_chan), 1)
    ) & (lax.broadcasted_iota(jnp.int32, (half, span_chan), 0) < 3 * span_chan)
    pick = pick.astype(jnp.float32)
    gain_at = base + levels * 2 * span_chan
    gain = jnp.concatenate(
        [
            jnp.dot(block[gain_at : gain_at + span_chan], pick, preferred_element_type=jnp.float32)
            for block in turned
        ],
        axis=0,
    )
    projection = []
    for degree in range(levels):
        start = base + degree * 2 * span_chan
        projection.append(
            jnp.concatenate(
                [
                    jnp.concatenate(
                        [block[start : start + span_chan], block[start + span_chan : start + 2 * span_chan]],
                        axis=1,
                    )
                    for block in turned
                ],
                axis=0,
            ).astype(jnp.bfloat16)
        )

    rows = [
        jnp.concatenate([block[j * span_chan : (j + 1) * span_chan] for block in turned], axis=0)
        for j in range(COEFFS)
    ]
    normed = [None] * len(rows)
    for degree in range(levels):
        span = range(degree * degree, (degree + 1) ** 2)
        total = None
        for j in span:
            part = jnp.sum(rows[j] * rows[j], axis=0, keepdims=True)
            total = part if total is None else total + part
        inverse = 1.0 / jnp.sqrt(total / float((2 * degree + 1) * CHANNELS) + EPSILON)
        scale = gain[:, degree : degree + 1]
        for j in span:
            normed[j] = (rows[j] * scale * inverse).astype(jnp.bfloat16).astype(jnp.float32)

    rotated = [None] * ROTATED
    for degree in range(levels):
        reach_order = min(degree, MAX_ORDER)
        span_cols = 2 * degree + 1
        first_row = wigner_start(degree)
        for position in range(2 * reach_order + 1):
            total = None
            for column in range(span_cols):
                row = first_row + position * span_cols + column
                term = wig[row : row + 1, :] * normed[degree * degree + column]
                total = term if total is None else total + term
            rotated[order_index(degree, position - reach_order)] = total.astype(jnp.bfloat16)

    spacing = CUTOFF / (basis_count - 1)
    centers = lax.broadcasted_iota(jnp.int32, (basis_count, num_edges), 0).astype(jnp.float32) * spacing
    basis_rows = jnp.exp(
        -0.5 * jnp.square((length_ref[...] - centers) / (2.0 * spacing))
    ).astype(jnp.bfloat16)
    hidden = jnp.dot(basis_in_ref[...], basis_rows, preferred_element_type=jnp.float32) + jnp.dot(
        kind_table_ref[...], kind_ref[...], preferred_element_type=jnp.float32
    )
    hidden = (hidden * jax.nn.sigmoid(hidden)).astype(jnp.bfloat16)
    radial = jnp.dot(radial_out_ref[...], hidden, preferred_element_type=jnp.float32)

    lowest = jnp.concatenate(
        [
            (rotated[degree].astype(jnp.float32) * radial[degree * channel_count : (degree + 1) * channel_count]).astype(
                jnp.bfloat16
            )
            for degree in range(levels)
        ],
        axis=0,
    )
    loads[0].wait()
    mixed0 = jnp.dot(zero_ref[...], lowest, preferred_element_type=jnp.float32)
    mixed = [mixed0[degree * channel_count : (degree + 1) * channel_count] for degree in range(levels)]
    first_row = levels
    for harmonic, weight_ref, load in ((1, one_ref, loads[1]), (2, two_ref, loads[2])):
        load.wait()
        span_rows = levels - harmonic
        plus_rows = jnp.concatenate(rotated[first_row : first_row + span_rows], axis=0)
        minus_rows = jnp.concatenate(rotated[first_row + span_rows : first_row + 2 * span_rows], axis=0)
        joined = jnp.concatenate([plus_rows, minus_rows], axis=1)
        real_part = jnp.dot(weight_ref[0], joined, preferred_element_type=jnp.float32)
        cross_part = jnp.dot(weight_ref[1], joined, preferred_element_type=jnp.float32)
        new_plus = real_part[:, :num_edges] - cross_part[:, num_edges:]
        new_minus = cross_part[:, :num_edges] + real_part[:, num_edges:]
        mixed += [new_plus[k * channel_count : (k + 1) * channel_count] for k in range(span_rows)]
        mixed += [new_minus[k * channel_count : (k + 1) * channel_count] for k in range(span_rows)]
        first_row = first_row + 2 * span_rows

    scalar = mixed[0]
    gate = jax.nn.sigmoid(scalar)
    gated = [(scalar * gate).astype(jnp.bfloat16).astype(jnp.float32)] + [
        (piece * gate).astype(jnp.bfloat16).astype(jnp.float32) for piece in mixed[1:]
    ]

    messages = []
    for degree in range(levels):
        reach_order = min(degree, MAX_ORDER)
        span_cols = 2 * degree + 1
        first_row = wigner_start(degree)
        for column in range(span_cols):
            total = None
            for position in range(2 * reach_order + 1):
                row = first_row + position * span_cols + column
                term = wig[row : row + 1, :] * gated[order_index(degree, position - reach_order)]
                total = term if total is None else total + term
            messages.append(total)
    stacked = jnp.concatenate(messages, axis=0)
    upper_part = stacked.astype(jnp.bfloat16)
    lower_part = (stacked - upper_part.astype(jnp.float32)).astype(jnp.bfloat16)
    onehot = onehot_ref[...]
    summed = jnp.dot(upper_part, onehot, preferred_element_type=jnp.float32) + jnp.dot(
        lower_part, onehot, preferred_element_type=jnp.float32
    )
    half = span_chan // 2
    pieces = [[] for _ in range(owners)]
    for degree in range(levels):
        weight = projection[degree]
        for j in range(degree * degree, (degree + 1) ** 2):
            piece = summed[j * channel_count : (j + 1) * channel_count]
            high = piece.astype(jnp.bfloat16)
            low = (piece - high.astype(jnp.float32)).astype(jnp.bfloat16)
            both = jnp.dot(weight, jnp.concatenate([high, low], axis=1), preferred_element_type=jnp.float32)
            result = both[:, :num_edges] + both[:, num_edges:]
            for r in range(owners):
                block = result[r * span_chan : (r + 1) * span_chan]
                pieces[r].append(jnp.concatenate([block[:half], block[half:]], axis=1))
    fill = out_ref.shape[1] - COEFFS * half
    for r in range(owners):
        out_ref[r] = jnp.concatenate(
            pieces[r] + [jnp.zeros((fill, out_ref.shape[2]), jnp.float32)], axis=0
        ).astype(out_ref.dtype)


def edge_operands(wig_mine, lengths, kind_onehot, radial_in, species_table, radial_out,
                  order_zero, order_one, order_two, onehot):
    return (
        wig_mine,
        lengths[None, :],
        kind_onehot,
        radial_in.T,
        species_table.T,
        radial_out.T,
        order_zero.T,
        jnp.transpose(order_one, (0, 2, 1)),
        jnp.transpose(order_two, (0, 2, 1)),
        onehot,
    )


def convolve_edges(source, side):
    coeffs, channel_count = COEFFS, CHANNELS
    onehot = side[-1]
    num_edges, atom_count = onehot.shape
    owners = source.shape[0]
    out_rows = 8 * pl.cdiv(coeffs * (channel_count // owners) // 2, 8)
    operands = (source,) + tuple(side)
    radial_in, radial_out = side[3], side[5]
    order_zero, order_one, order_two = side[6], side[7], side[8]
    flops = 2 * num_edges * (order_zero.size + 2 * order_one.size + 2 * order_two.size + radial_out.size + radial_in.size)
    return pl.pallas_call(
        conv_kernel,
        out_shape=jax.ShapeDtypeStruct((owners, out_rows, 2 * atom_count), jnp.bfloat16),
        in_specs=[pl.BlockSpec(memory_space=pltpu.VMEM)] * 7
        + [pl.BlockSpec(memory_space=pl.ANY)] * 3
        + [pl.BlockSpec(memory_space=pltpu.VMEM)],
        out_specs=pl.BlockSpec(memory_space=pltpu.VMEM),
        scratch_shapes=[
            pltpu.VMEM(order_zero.shape, order_zero.dtype),
            pltpu.VMEM(order_one.shape, order_one.dtype),
            pltpu.VMEM(order_two.shape, order_two.dtype),
            pltpu.SemaphoreType.DMA((3,)),
        ],
        cost_estimate=pl.CostEstimate(
            flops=flops,
            transcendentals=num_edges * (radial_in.shape[1] + 2 * channel_count),
            bytes_accessed=sum(int(x.size) * x.dtype.itemsize for x in operands) + owners * out_rows * atom_count * 4,
        ),
    )(*operands)


def gather_kernel(index_ref, local_ref, arrived_ref, extra_ref, *refs):
    out_ref = refs[-1]
    owners, per_owner, row_width = out_ref.shape
    row_used = local_ref.shape[1]
    table = jnp.concatenate([local_ref[...], arrived_ref[...]], axis=0)
    hot = (
        index_ref[...] == lax.broadcasted_iota(jnp.int32, (index_ref.shape[0], table.shape[0]), 1)
    ).astype(jnp.bfloat16)
    picked = jnp.dot(hot, table, preferred_element_type=jnp.float32).astype(out_ref.dtype)
    extra = extra_ref[...]
    for q in range(owners):
        out_ref[q, :, 0:row_used] = picked[q * per_owner : (q + 1) * per_owner]
        out_ref[q, :, row_used:row_width] = extra


def gather_rows(edge_source, node_rows, arrived, extra, owners, row_width, side):
    per_owner = edge_source.shape[0] // owners
    operands = (edge_source[:, None], node_rows, arrived, extra)
    return pl.pallas_call(
        gather_kernel,
        out_shape=jax.ShapeDtypeStruct((owners, per_owner, row_width), jnp.bfloat16),
        in_specs=[pl.BlockSpec(memory_space=pltpu.VMEM)] * len(operands)
        + [pl.BlockSpec(memory_space=pl.ANY)] * len(side),
        out_specs=pl.BlockSpec(memory_space=pltpu.VMEM),
        cost_estimate=pl.CostEstimate(
            flops=2 * edge_source.shape[0] * (node_rows.shape[0] + arrived.shape[0]) * node_rows.shape[1],
            transcendentals=0,
            bytes_accessed=sum(int(x.size) * x.dtype.itemsize for x in operands)
            + owners * per_owner * row_width * 2,
        ),
    )(*operands, *side)


def split_dot(values, weight):
    upper_part = values.astype(jnp.bfloat16)
    lower_part = (values - upper_part.astype(jnp.float32)).astype(jnp.bfloat16)
    return jnp.dot(upper_part, weight, preferred_element_type=jnp.float32) + jnp.dot(
        lower_part, weight, preferred_element_type=jnp.float32
    )


def body(
    node_feats,
    norm_gain,
    species,
    send_list,
    edge_source,
    edge_target,
    edge_count,
    edge_length,
    wigner,
    radial_in,
    species_table,
    radial_out,
    order_zero,
    order_one,
    order_two,
    project_weight,
):
    levels = MAX_DEGREE + 1
    owners = lax.axis_size("irreps")
    quarter = lax.axis_index("irreps")
    coeffs, span_chan, atom_count = node_feats.shape
    per_owner = edge_source.shape[0] // owners
    first_edge = quarter * per_owner

    row_used = coeffs * span_chan
    row_width = 128 * pl.cdiv(row_used, 128)
    node_rows = node_feats.reshape(row_used, atom_count).T
    send_hot = (send_list[:, None] == jnp.arange(atom_count, dtype=jnp.int32)[None, :]).astype(jnp.bfloat16)
    outgoing_rows = lax.dot_general(
        send_hot, node_feats.reshape(row_used, atom_count), (((1,), (1,)), ((), ())),
        preferred_element_type=jnp.float32,
    ).astype(jnp.bfloat16)
    arrived = lax.all_to_all(outgoing_rows, "graph", 0, 0, tiled=True)

    gain_high = lax.reduce_precision(norm_gain, exponent_bits=8, mantissa_bits=7)
    gain_rest = norm_gain - gain_high
    gain_mid = lax.reduce_precision(gain_rest, exponent_bits=8, mantissa_bits=7)
    gain_low = gain_rest - gain_mid
    gain_block = jnp.transpose(jnp.stack([gain_high, gain_mid, gain_low]), (2, 0, 1))
    gain_block = jnp.pad(gain_block, ((0, 0), (0, 0), (0, 1))).reshape(span_chan, 3 * (levels + 1))
    gain_block = jnp.pad(gain_block, ((0, 0), (0, per_owner - gain_block.shape[1]))).astype(jnp.bfloat16)
    pair_order = np.concatenate([np.arange(0, span_chan, 2), np.arange(1, span_chan, 2)])
    weight_block = jnp.transpose(
        project_weight[:, :, pair_order].reshape(levels, CHANNELS // per_owner, per_owner, span_chan), (0, 1, 3, 2)
    ).reshape(-1, per_owner)
    extra = jnp.concatenate([weight_block, gain_block], axis=0).T

    wig_mine = lax.dynamic_slice_in_dim(wigner, first_edge, per_owner, 1)
    targets_mine = lax.dynamic_slice_in_dim(edge_target, first_edge, per_owner)
    lengths_mine = lax.dynamic_slice_in_dim(edge_length, first_edge, per_owner)
    kinds = species[targets_mine]
    kind_onehot = (
        kinds[None, :] == jnp.arange(species_table.shape[0], dtype=jnp.int32)[:, None]
    ).astype(jnp.bfloat16)
    edge_weight = jnp.where(
        first_edge + jnp.arange(per_owner, dtype=jnp.int32) < edge_count[0], 0.25, 0.0
    ).astype(jnp.float32)
    onehot = jnp.where(
        targets_mine[:, None] == jnp.arange(atom_count, dtype=jnp.int32)[None, :],
        edge_weight[:, None],
        0.0,
    ).astype(jnp.bfloat16)
    side = edge_operands(
        wig_mine, lengths_mine, kind_onehot, radial_in, species_table, radial_out,
        order_zero, order_one, order_two, onehot,
    )
    outgoing = gather_rows(edge_source, node_rows, arrived, extra, owners, row_width, side)
    source = lax.all_to_all(outgoing, "irreps", 0, 0, tiled=True)
    projected = convolve_edges(source, side)
    returned = lax.all_to_all(projected, "irreps", 0, 0, tiled=True)
    total = jnp.sum(returned.astype(jnp.float32), axis=0)[: coeffs * span_chan // 2]
    total = total.reshape(coeffs, span_chan // 2, 2, atom_count).reshape(coeffs, span_chan, atom_count)
    return (node_feats.astype(jnp.float32) + total).astype(jnp.bfloat16)


def solution(mesh):
    return jax.shard_map(
        body,
        mesh=mesh,
        in_specs=(
            P(None, "irreps", "graph"),
            P(None, "irreps"),
            P("graph"),
            P("graph"),
            P("graph"),
            P("graph"),
            P("graph"),
            P("graph"),
            P(None, "graph"),
            P(),
            P(),
            P(),
            P(),
            P(),
            P(),
            P(None, None, "irreps"),
        ),
        out_specs=P(None, "irreps", "graph"),
        check_vma=False,
    )
```

```python
import jax
import jax.numpy as jnp
import numpy as np
from jax import lax
from jax.sharding import PartitionSpec as P
from jax.experimental import pallas as pl
from jax.experimental.pallas import tpu as pltpu

CHANNELS = 128
MAX_DEGREE = 6
MAX_ORDER = 2
ROTATED = 29
COEFFS = 49


EPSILON = 1e-06
CUTOFF = 6.0


def order_index(degree, harmonic):
    if harmonic == 0:
        return degree
    first_row = MAX_DEGREE + 1
    for level in range(1, abs(harmonic)):
        first_row = first_row + 2 * (MAX_DEGREE + 1 - level)
    if harmonic < 0:
        first_row = first_row + MAX_DEGREE + 1 - abs(harmonic)
    return first_row + degree - abs(harmonic)


def wigner_start(degree):
    running = 0
    for level in range(degree):
        running = running + (2 * min(level, MAX_ORDER) + 1) * (2 * level + 1)
    return running


def left_dot(weight, values):
    return lax.dot_general(
        weight, values, (((0,), (0,)), ((), ())), preferred_element_type=jnp.float32
    )


def degree_sums(squares):
    return jnp.stack(
        [
            jnp.sum(squares[degree * degree : (degree + 1) ** 2], axis=0)
            for degree in range(MAX_DEGREE + 1)
        ]
    )


def normalize(node_feats, norm_gain, totals):
    levels = MAX_DEGREE + 1
    degree_of = np.repeat(np.arange(levels), 2 * np.arange(levels) + 1)
    entry_counts = (2 * np.arange(levels) + 1) * CHANNELS
    inverse = 1.0 / jnp.sqrt(totals / jnp.asarray(entry_counts, jnp.float32)[:, None] + EPSILON)
    gain_rows = norm_gain[degree_of]
    scale_rows = inverse[degree_of]
    return (node_feats.astype(jnp.float32) * gain_rows[:, :, None] * scale_rows[:, None, :]).astype(
        jnp.bfloat16
    )


def normalize_rows(values, gain_full, totals):
    levels = MAX_DEGREE + 1
    degree_of = np.repeat(np.arange(levels), 2 * np.arange(levels) + 1)
    entry_counts = (2 * np.arange(levels) + 1) * CHANNELS
    inverse = 1.0 / jnp.sqrt(totals / jnp.asarray(entry_counts, jnp.float32)[:, None] + EPSILON)
    gain_rows = gain_full[degree_of]
    scale_rows = inverse[degree_of]
    return (values * gain_rows[:, :, None] * scale_rows[:, None, :]).astype(jnp.bfloat16)


def rotate(source, wig_rows):
    pieces = [None] * ROTATED
    for degree in range(MAX_DEGREE + 1):
        reach_order = min(degree, MAX_ORDER)
        span_cols = 2 * degree + 1
        first_row = wigner_start(degree)
        for position in range(2 * reach_order + 1):
            total = None
            for column in range(span_cols):
                term = wig_rows[first_row + position * span_cols + column][None, :] * source[degree * degree + column]
                total = term if total is None else total + term
            pieces[order_index(degree, position - reach_order)] = total
    return jnp.stack(pieces).astype(jnp.bfloat16)


def unrotate(gated, wig_rows):
    pieces = []
    for degree in range(MAX_DEGREE + 1):
        reach_order = min(degree, MAX_ORDER)
        span_cols = 2 * degree + 1
        first_row = wigner_start(degree)
        for column in range(span_cols):
            total = None
            for position in range(2 * reach_order + 1):
                term = wig_rows[first_row + position * span_cols + column][None, :] * gated[
                    order_index(degree, position - reach_order)
                ]
                total = term if total is None else total + term
            pieces.append(total)
    return jnp.stack(pieces)


def radial_weights(lengths, kind_ids, radial_in, species_table, radial_out):
    basis_count = radial_in.shape[0]
    spacing = CUTOFF / (basis_count - 1)
    centers = jnp.arange(basis_count, dtype=jnp.float32) * spacing
    basis_rows = jnp.exp(
        -0.5 * jnp.square((lengths[None, :] - centers[:, None]) / (2.0 * spacing))
    ).astype(jnp.bfloat16)
    onehot = (
        kind_ids[None, :] == jnp.arange(species_table.shape[0], dtype=jnp.int32)[:, None]
    ).astype(jnp.bfloat16)
    hidden = jax.nn.silu(left_dot(radial_in, basis_rows) + left_dot(species_table, onehot)).astype(
        jnp.bfloat16
    )
    return left_dot(radial_out, hidden)


def convolve(rotated, radial, order_zero, order_one, order_two):
    levels = MAX_DEGREE + 1
    channel_count = rotated.shape[1]
    num_edges = rotated.shape[2]
    lowest = (
        rotated[:levels].astype(jnp.float32).reshape(levels * channel_count, num_edges) * radial
    ).astype(jnp.bfloat16)
    outputs = [left_dot(order_zero, lowest).reshape(levels, channel_count, num_edges)]
    first_row = levels
    for harmonic, weight in ((1, order_one), (2, order_two)):
        span_rows = levels - harmonic
        plus_rows = rotated[first_row : first_row + span_rows].reshape(
            span_rows * channel_count, num_edges
        )
        minus_rows = rotated[first_row + span_rows : first_row + 2 * span_rows].reshape(
            span_rows * channel_count, num_edges
        )
        joined = jnp.concatenate([plus_rows, minus_rows], axis=1)
        real_part = left_dot(weight[0], joined)
        cross_part = left_dot(weight[1], joined)
        outputs.append(
            (real_part[:, :num_edges] - cross_part[:, num_edges:]).reshape(
                span_rows, channel_count, num_edges
            )
        )
        outputs.append(
            (cross_part[:, :num_edges] + real_part[:, num_edges:]).reshape(
                span_rows, channel_count, num_edges
            )
        )
        first_row = first_row + 2 * span_rows
    mixed = jnp.concatenate(outputs, axis=0)
    scalar = mixed[0]
    return jnp.concatenate(
        [jax.nn.silu(scalar)[None], mixed[1:] * jax.nn.sigmoid(scalar)[None]], axis=0
    ).astype(jnp.bfloat16)


def conv_kernel(
    src_ref, wig_ref, length_ref, kind_ref, basis_in_ref, kind_table_ref, radial_out_ref,
    zero_hbm, one_hbm, two_hbm, onehot_ref, out_ref, zero_ref, one_ref, two_ref, copy_sems,
):
    loads = [
        pltpu.make_async_copy(zero_hbm, zero_ref, copy_sems.at[0]),
        pltpu.make_async_copy(one_hbm, one_ref, copy_sems.at[1]),
        pltpu.make_async_copy(two_hbm, two_ref, copy_sems.at[2]),
    ]
    for load in loads:
        load.start()
    levels = MAX_DEGREE + 1
    channel_count = CHANNELS
    num_edges = onehot_ref.shape[0]
    basis_count = basis_in_ref.shape[1]
    wig = wig_ref[...].astype(jnp.float32)
    owners = src_ref.shape[0]
    span_chan = CHANNELS // owners
    turned = [src_ref[r].astype(jnp.float32).T for r in range(owners)]
    base = COEFFS * span_chan
    half = num_edges
    pick = (
        lax.broadcasted_iota(jnp.int32, (half, span_chan), 0) % span_chan
        == lax.broadcasted_iota(jnp.int32, (half, span_chan), 1)
    ) & (lax.broadcasted_iota(jnp.int32, (half, span_chan), 0) < 3 * span_chan)
    pick = pick.astype(jnp.float32)
    gain_at = base + levels * 2 * span_chan
    gain = jnp.concatenate(
        [
            jnp.dot(block[gain_at : gain_at + span_chan], pick, preferred_element_type=jnp.float32)
            for block in turned
        ],
        axis=0,
    )
    projection = []
    for degree in range(levels):
        start = base + degree * 2 * span_chan
        projection.append(
            jnp.concatenate(
                [
                    jnp.concatenate(
                        [block[start : start + span_chan], block[start + span_chan : start + 2 * span_chan]],
                        axis=1,
                    )
                    for block in turned
                ],
                axis=0,
            ).astype(jnp.bfloat16)
        )

    rows = [
        jnp.concatenate([block[j * span_chan : (j + 1) * span_chan] for block in turned], axis=0)
        for j in range(COEFFS)
    ]
    normed = [None] * len(rows)
    for degree in range(levels):
        span = range(degree * degree, (degree + 1) ** 2)
        total = None
        for j in span:
            part = jnp.sum(rows[j] * rows[j], axis=0, keepdims=True)
            total = part if total is None else total + part
        inverse = 1.0 / jnp.sqrt(total / float((2 * degree + 1) * CHANNELS) + EPSILON)
        scale = gain[:, degree : degree + 1]
        for j in span:
            normed[j] = (rows[j] * scale * inverse).astype(jnp.bfloat16).astype(jnp.float32)

    rotated = [None] * ROTATED
    for degree in range(levels):
        reach_order = min(degree, MAX_ORDER)
        span_cols = 2 * degree + 1
        first_row = wigner_start(degree)
        for position in range(2 * reach_order + 1):
            total = None
            for column in range(span_cols):
                row = first_row + position * span_cols + column
                term = wig[row : row + 1, :] * normed[degree * degree + column]
                total = term if total is None else total + term
            rotated[order_index(degree, position - reach_order)] = total.astype(jnp.bfloat16)

    spacing = CUTOFF / (basis_count - 1)
    centers = lax.broadcasted_iota(jnp.int32, (basis_count, num_edges), 0).astype(jnp.float32) * spacing
    basis_rows = jnp.exp(
        -0.5 * jnp.square((length_ref[...] - centers) / (2.0 * spacing))
    ).astype(jnp.bfloat16)
    hidden = jnp.dot(basis_in_ref[...], basis_rows, preferred_element_type=jnp.float32) + jnp.dot(
        kind_table_ref[...], kind_ref[...], preferred_element_type=jnp.float32
    )
    hidden = (hidden * jax.nn.sigmoid(hidden)).astype(jnp.bfloat16)
    radial = jnp.dot(radial_out_ref[...], hidden, preferred_element_type=jnp.float32)

    lowest = jnp.concatenate(
        [
            (rotated[degree].astype(jnp.float32) * radial[degree * channel_count : (degree + 1) * channel_count]).astype(
                jnp.bfloat16
            )
            for degree in range(levels)
        ],
        axis=0,
    )
    loads[0].wait()
    mixed0 = jnp.dot(zero_ref[...], lowest, preferred_element_type=jnp.float32)
    mixed = [mixed0[degree * channel_count : (degree + 1) * channel_count] for degree in range(levels)]
    first_row = levels
    for harmonic, weight_ref, load in ((1, one_ref, loads[1]), (2, two_ref, loads[2])):
        load.wait()
        span_rows = levels - harmonic
        plus_rows = jnp.concatenate(rotated[first_row : first_row + span_rows], axis=0)
        minus_rows = jnp.concatenate(rotated[first_row + span_rows : first_row + 2 * span_rows], axis=0)
        joined = jnp.concatenate([plus_rows, minus_rows], axis=1)
        real_part = jnp.dot(weight_ref[0], joined, preferred_element_type=jnp.float32)
        cross_part = jnp.dot(weight_ref[1], joined, preferred_element_type=jnp.float32)
        new_plus = real_part[:, :num_edges] - cross_part[:, num_edges:]
        new_minus = cross_part[:, :num_edges] + real_part[:, num_edges:]
        mixed += [new_plus[k * channel_count : (k + 1) * channel_count] for k in range(span_rows)]
        mixed += [new_minus[k * channel_count : (k + 1) * channel_count] for k in range(span_rows)]
        first_row = first_row + 2 * span_rows

    scalar = mixed[0]
    gate = jax.nn.sigmoid(scalar)
    gated = [(scalar * gate).astype(jnp.bfloat16).astype(jnp.float32)] + [
        (piece * gate).astype(jnp.bfloat16).astype(jnp.float32) for piece in mixed[1:]
    ]

    messages = []
    for degree in range(levels):
        reach_order = min(degree, MAX_ORDER)
        span_cols = 2 * degree + 1
        first_row = wigner_start(degree)
        for column in range(span_cols):
            total = None
            for position in range(2 * reach_order + 1):
                row = first_row + position * span_cols + column
                term = wig[row : row + 1, :] * gated[order_index(degree, position - reach_order)]
                total = term if total is None else total + term
            messages.append(total)
    stacked = jnp.concatenate(messages, axis=0)
    upper_part = stacked.astype(jnp.bfloat16)
    lower_part = (stacked - upper_part.astype(jnp.float32)).astype(jnp.bfloat16)
    onehot = onehot_ref[...]
    summed = jnp.dot(upper_part, onehot, preferred_element_type=jnp.float32) + jnp.dot(
        lower_part, onehot, preferred_element_type=jnp.float32
    )
    half = span_chan // 2
    pieces = [[] for _ in range(owners)]
    for degree in range(levels):
        weight = projection[degree]
        for j in range(degree * degree, (degree + 1) ** 2):
            piece = summed[j * channel_count : (j + 1) * channel_count]
            high = piece.astype(jnp.bfloat16)
            low = (piece - high.astype(jnp.float32)).astype(jnp.bfloat16)
            both = jnp.dot(weight, jnp.concatenate([high, low], axis=1), preferred_element_type=jnp.float32)
            result = both[:, :num_edges] + both[:, num_edges:]
            for r in range(owners):
                block = result[r * span_chan : (r + 1) * span_chan]
                pieces[r].append(jnp.concatenate([block[:half], block[half:]], axis=1))
    fill = out_ref.shape[1] - COEFFS * half
    for r in range(owners):
        tail = [jnp.zeros((fill, out_ref.shape[2]), jnp.float32)] if fill else []
        out_ref[r] = jnp.concatenate(pieces[r] + tail, axis=0).astype(out_ref.dtype)


def edge_operands(wig_mine, lengths, kind_onehot, radial_in, species_table, radial_out,
                  order_zero, order_one, order_two, onehot):
    return (
        wig_mine,
        lengths[None, :],
        kind_onehot,
        radial_in.T,
        species_table.T,
        radial_out.T,
        order_zero.T,
        jnp.transpose(order_one, (0, 2, 1)),
        jnp.transpose(order_two, (0, 2, 1)),
        onehot,
    )


def convolve_edges(source, side):
    coeffs, channel_count = COEFFS, CHANNELS
    onehot = side[-1]
    num_edges, atom_count = onehot.shape
    owners = source.shape[0]
    out_rows = coeffs * (channel_count // owners) // 2
    operands = (source,) + tuple(side)
    radial_in, radial_out = side[3], side[5]
    order_zero, order_one, order_two = side[6], side[7], side[8]
    flops = 2 * num_edges * (order_zero.size + 2 * order_one.size + 2 * order_two.size + radial_out.size + radial_in.size)
    return pl.pallas_call(
        conv_kernel,
        out_shape=jax.ShapeDtypeStruct((owners, out_rows, 2 * atom_count), jnp.bfloat16),
        in_specs=[pl.BlockSpec(memory_space=pltpu.VMEM)] * 7
        + [pl.BlockSpec(memory_space=pl.ANY)] * 3
        + [pl.BlockSpec(memory_space=pltpu.VMEM)],
        out_specs=pl.BlockSpec(memory_space=pltpu.VMEM),
        scratch_shapes=[
            pltpu.VMEM(order_zero.shape, order_zero.dtype),
            pltpu.VMEM(order_one.shape, order_one.dtype),
            pltpu.VMEM(order_two.shape, order_two.dtype),
            pltpu.SemaphoreType.DMA((3,)),
        ],
        cost_estimate=pl.CostEstimate(
            flops=flops,
            transcendentals=num_edges * (radial_in.shape[1] + 2 * channel_count),
            bytes_accessed=sum(int(x.size) * x.dtype.itemsize for x in operands) + owners * out_rows * atom_count * 4,
        ),
    )(*operands)


def gather_kernel(index_ref, local_ref, arrived_ref, extra_ref, *refs):
    out_ref = refs[-1]
    owners, per_owner, row_width = out_ref.shape
    row_used = local_ref.shape[1]
    table = jnp.concatenate([local_ref[...], arrived_ref[...]], axis=0)
    hot = (
        index_ref[...] == lax.broadcasted_iota(jnp.int32, (index_ref.shape[0], table.shape[0]), 1)
    ).astype(jnp.bfloat16)
    picked = jnp.dot(hot, table, preferred_element_type=jnp.float32).astype(out_ref.dtype)
    extra = extra_ref[...]
    for q in range(owners):
        out_ref[q, :, 0:row_used] = picked[q * per_owner : (q + 1) * per_owner]
        out_ref[q, :, row_used:row_width] = extra


def gather_rows(edge_source, node_rows, arrived, extra, owners, row_width, side):
    per_owner = edge_source.shape[0] // owners
    operands = (edge_source[:, None], node_rows, arrived, extra)
    return pl.pallas_call(
        gather_kernel,
        out_shape=jax.ShapeDtypeStruct((owners, per_owner, row_width), jnp.bfloat16),
        in_specs=[pl.BlockSpec(memory_space=pltpu.VMEM)] * len(operands)
        + [pl.BlockSpec(memory_space=pl.ANY)] * len(side),
        out_specs=pl.BlockSpec(memory_space=pltpu.VMEM),
        cost_estimate=pl.CostEstimate(
            flops=2 * edge_source.shape[0] * (node_rows.shape[0] + arrived.shape[0]) * node_rows.shape[1],
            transcendentals=0,
            bytes_accessed=sum(int(x.size) * x.dtype.itemsize for x in operands)
            + owners * per_owner * row_width * 2,
        ),
    )(*operands, *side)


def split_dot(values, weight):
    upper_part = values.astype(jnp.bfloat16)
    lower_part = (values - upper_part.astype(jnp.float32)).astype(jnp.bfloat16)
    return jnp.dot(upper_part, weight, preferred_element_type=jnp.float32) + jnp.dot(
        lower_part, weight, preferred_element_type=jnp.float32
    )


def body(
    node_feats,
    norm_gain,
    species,
    send_list,
    edge_source,
    edge_target,
    edge_count,
    edge_length,
    wigner,
    radial_in,
    species_table,
    radial_out,
    order_zero,
    order_one,
    order_two,
    project_weight,
):
    levels = MAX_DEGREE + 1
    owners = lax.axis_size("irreps")
    quarter = lax.axis_index("irreps")
    coeffs, span_chan, atom_count = node_feats.shape
    per_owner = edge_source.shape[0] // owners
    first_edge = quarter * per_owner

    row_used = coeffs * span_chan
    row_width = 128 * pl.cdiv(row_used, 128)
    node_rows = node_feats.reshape(row_used, atom_count).T
    send_hot = (send_list[:, None] == jnp.arange(atom_count, dtype=jnp.int32)[None, :]).astype(jnp.bfloat16)
    outgoing_rows = lax.dot_general(
        send_hot, node_feats.reshape(row_used, atom_count), (((1,), (1,)), ((), ())),
        preferred_element_type=jnp.float32,
    ).astype(jnp.bfloat16)
    arrived = lax.all_to_all(outgoing_rows, "graph", 0, 0, tiled=True)

    gain_high = lax.reduce_precision(norm_gain, exponent_bits=8, mantissa_bits=7)
    gain_rest = norm_gain - gain_high
    gain_mid = lax.reduce_precision(gain_rest, exponent_bits=8, mantissa_bits=7)
    gain_low = gain_rest - gain_mid
    gain_block = jnp.transpose(jnp.stack([gain_high, gain_mid, gain_low]), (2, 0, 1))
    gain_block = jnp.pad(gain_block, ((0, 0), (0, 0), (0, 1))).reshape(span_chan, 3 * (levels + 1))
    gain_block = jnp.pad(gain_block, ((0, 0), (0, per_owner - gain_block.shape[1]))).astype(jnp.bfloat16)
    pair_order = np.concatenate([np.arange(0, span_chan, 2), np.arange(1, span_chan, 2)])
    weight_block = jnp.transpose(
        project_weight[:, :, pair_order].reshape(levels, CHANNELS // per_owner, per_owner, span_chan), (0, 1, 3, 2)
    ).reshape(-1, per_owner)
    extra = jnp.concatenate([weight_block, gain_block], axis=0).T

    wig_mine = lax.dynamic_slice_in_dim(wigner, first_edge, per_owner, 1)
    targets_mine = lax.dynamic_slice_in_dim(edge_target, first_edge, per_owner)
    lengths_mine = lax.dynamic_slice_in_dim(edge_length, first_edge, per_owner)
    kinds = species[targets_mine]
    kind_onehot = (
        kinds[None, :] == jnp.arange(species_table.shape[0], dtype=jnp.int32)[:, None]
    ).astype(jnp.bfloat16)
    edge_weight = jnp.where(
        first_edge + jnp.arange(per_owner, dtype=jnp.int32) < edge_count[0], 0.25, 0.0
    ).astype(jnp.float32)
    onehot = jnp.where(
        targets_mine[:, None] == jnp.arange(atom_count, dtype=jnp.int32)[None, :],
        edge_weight[:, None],
        0.0,
    ).astype(jnp.bfloat16)
    side = edge_operands(
        wig_mine, lengths_mine, kind_onehot, radial_in, species_table, radial_out,
        order_zero, order_one, order_two, onehot,
    )
    outgoing = gather_rows(edge_source, node_rows, arrived, extra, owners, row_width, side)
    source = lax.all_to_all(outgoing, "irreps", 0, 0, tiled=True)
    projected = convolve_edges(source, side)
    returned = lax.all_to_all(projected, "irreps", 0, 0, tiled=True)
    total = jnp.sum(returned.astype(jnp.float32), axis=0)[: coeffs * span_chan // 2]
    total = total.reshape(coeffs, span_chan // 2, 2, atom_count).reshape(coeffs, span_chan, atom_count)
    return (node_feats.astype(jnp.float32) + total).astype(jnp.bfloat16)


def solution(mesh):
    return jax.shard_map(
        body,
        mesh=mesh,
        in_specs=(
            P(None, "irreps", "graph"),
            P(None, "irreps"),
            P("graph"),
            P("graph"),
            P("graph"),
            P("graph"),
            P("graph"),
            P("graph"),
            P(None, "graph"),
            P(),
            P(),
            P(),
            P(),
            P(),
            P(),
            P(None, None, "irreps"),
        ),
        out_specs=P(None, "irreps", "graph"),
        check_vma=False,
    )
```
